32 devices in a mesh: groups: 2 (over y), tm: 4 (over z), mp: 2 (over x), section: 2 (over core).
Axes of the slice: x: 2, y: 2, z: 4, core: 2. Of those that a mesh axis runs over, the one named last changes fastest.
Arguments:
- series: bfloat16 [4, 64, 16384], P('groups', None, 'tm'), parts along dimension 0, may hold values from -80 to 80
- lengths: int32 [4], P('groups'), parts along dimension 0, may hold values from 2048 to 16384, as said below
- patch_weight: bfloat16 [4096, 1280], P(None, ('mp', 'section')), may hold values from -0.09375 to 0.09375
- norm_gain: bfloat16 [2, 1280], P('section'), may hold values from 0.099609375 to 1.8984375
- query_weight: bfloat16 [2, 1280, 1280], P('section', None, 'mp'), may hold values from -4 to 4
- key_weight: bfloat16 [2, 1280, 320], P('section', None, 'mp'), may hold values from -4 to 4
- value_weight: bfloat16 [2, 1280, 320], P('section', None, 'mp'), may hold values from -0.15625 to 0.15625
- out_weight: bfloat16 [2, 1280, 1280], P('section', 'mp'), may hold values from -0.625 to 0.625
Outputs:
- key_cache: bfloat16 [2, 4, 4, 80, 512], P('section', 'groups', 'mp', None, 'tm'), parts along dimension 1
- value_cache: bfloat16 [2, 4, 4, 80, 512], P('section', 'groups', 'mp', None, 'tm'), parts along dimension 1
- hidden: bfloat16 [4, 512, 1280], P(('groups', 'section'), 'tm', 'mp'), parts along dimension 0
The draws below stay inside these ranges and needn't reach their ends.
There are 2 independent parts, one for each index of `groups`. The reference program is written for one: setup_inputs(seed, part) draws one part's arguments, and reference() takes and returns one part's arrays. A program takes and returns all parts, laid end to end along the dimension named above; an argument that names none is the same for every part. Nothing has to cross between parts.
Inputs may be any that keep to these rules, and one draw needn't show every extreme that they name: `lengths`: a multiple of 32; the last sequence of a part has its whole history of 16384 steps.
All inputs are finite; a program needn't handle non-finite values.
Results may differ from the reference program's by a relative error of at most 0.02.
Values may be sent and summed in bfloat16 or wider, within the bound.
No kernel may reach another device: no remote copies, remote signals or barrier semaphores. Data moves between devices by JAX's collectives and lax.ppermute only.
A program may use at most 64 MiB of HBM per device.

```python
import math
import jax
import jax.numpy as jnp
from jax import lax

CH = 64
STRIDE = 32
KERNEL = 64
D = 1280
HEADS = 16
KV_HEADS = 4
HD = 80
SEQS = 2
LAYERS = 2
NTOK = 512
STEPS = 16384


def draw_series(key, part):
    first_key, second_key, third_key = jax.random.split(key, 3)
    ramp = 1.0 + 2.0 * jnp.arange(STEPS, dtype=jnp.float32) / STEPS
    spread = jnp.exp(jax.random.uniform(second_key, (SEQS, CH, 1), minval=math.log(0.3), maxval=math.log(4.0)))
    levels = jax.random.uniform(first_key, (SEQS, CH, 1), minval=-2.0, maxval=2.0)
    noise = jnp.clip(jax.random.normal(third_key, (SEQS, CH, STEPS)), -6.0, 6.0)
    return (levels + spread * ramp[None, None, :] * noise).astype(jnp.bfloat16)


def draw_lengths(key, part):
    strides = jax.random.randint(key, (SEQS,), NTOK // 8, NTOK + 1)
    strides = strides.at[SEQS - 1].set(NTOK)
    return (strides * STRIDE).astype(jnp.int32)


def draw_key_weight(key, part):
    noise = jnp.clip(jax.random.normal(jax.random.fold_in(key, 11), (LAYERS, D, KV_HEADS * HD)), -6.0, 6.0) * D ** (-0.5)
    return noise.astype(jnp.bfloat16)


def draw_query_weight(key, part):
    noise = jnp.clip(jax.random.normal(jax.random.fold_in(key, 13), (LAYERS, D, HEADS * HD)), -6.0, 6.0) * D ** (-0.5)
    return noise.astype(jnp.bfloat16)


def shard_levels(own_key, dims, cuts, smallest, top_value):
    def one(dim, blocks):
        steps = jax.random.uniform(jax.random.fold_in(jax.random.fold_in(own_key, 6), dim), (blocks,), jnp.float32, smallest / len(cuts), top_value / len(cuts))
        return jnp.repeat(jnp.exp(steps), dims[dim] // blocks).reshape((-1,) + (1,) * (len(dims) - dim - 1))

    loudness = one(*cuts[0])
    for cut in cuts[1:]:
        loudness = loudness * one(*cut)
    return loudness


def bell_draw(stream_key, shape, scale, most, cuts=(), held_as=jnp.bfloat16):
    loudness = shard_levels(stream_key, shape, cuts, -0.22, 0.18) if cuts else 1.0
    result = jax.random.normal(stream_key, shape, jnp.float32) * scale * loudness
    return jnp.minimum(jnp.maximum(result, -most), most).astype(held_as)


def setup_inputs(seed: int = 0, part: int = 0) -> dict:
    splits = jax.random.split(jax.random.key(seed), 9)
    own_keys = jax.random.split(jax.random.fold_in(splits[8], part), 9)
    series = draw_series(jax.random.fold_in(jax.random.fold_in(splits[8], part), 71), part)
    lengths = draw_lengths(jax.random.fold_in(jax.random.fold_in(splits[8], part), 71), part)
    patch_weight = bell_draw(splits[2], (CH * KERNEL, D), (CH * KERNEL) ** -0.5, 0.09375, ((1, 4),))
    norm_gain = jnp.clip(1.0 + 0.18 * jax.random.normal(splits[3], (LAYERS, D), jnp.float32), 0.099609375, 1.8984375).astype(jnp.bfloat16)
    query_weight = draw_query_weight(jax.random.fold_in(splits[8], 71), part)
    key_weight = draw_key_weight(jax.random.fold_in(splits[8], 71), part)
    value_weight = bell_draw(splits[6], (LAYERS, D, KV_HEADS * HD), D ** -0.5, 0.15625, ((0, 2), (2, 2)))
    out_weight = bell_draw(splits[7], (LAYERS, HEADS * HD, D), HD ** -0.5, 0.625, ((0, 2), (1, 2)))
    return {"series": series, "lengths": lengths, "patch_weight": patch_weight, "norm_gain": norm_gain, "query_weight": query_weight, "key_weight": key_weight, "value_weight": value_weight, "out_weight": out_weight}


def attention_rows(query_block, key_mat, value_mat, allowed):
    scores = jnp.einsum('gbe,en->gbn', query_block, key_mat)
    scores = jnp.where(allowed[None], scores, -jnp.inf)
    row_max = lax.optimization_barrier(jnp.max(scores, -1, keepdims=True))
    exp_scores = jnp.exp(scores - row_max)
    denominator = lax.optimization_barrier(jnp.sum(exp_scores, -1, keepdims=True))
    rounded = lax.optimization_barrier(exp_scores.astype(jnp.bfloat16))
    attn_weights = rounded.astype(jnp.float32)
    return (jnp.einsum('gbn,en->gbe', attn_weights, value_mat) / denominator).astype(jnp.bfloat16)

def layer_pass(hidden_in, lengths, gain, query_w, key_w, value_w, out_w):
    seq_count, tok_count, feature_count = hidden_in.shape
    hidden32 = hidden_in.astype(jnp.float32)
    scaled = hidden32 * lax.rsqrt(lax.optimization_barrier(jnp.mean(hidden32 * hidden32, -1, keepdims=True)) + 1e-06)
    layer_input = (scaled * gain.astype(jnp.float32)).astype(jnp.bfloat16)
    flat_rows = layer_input.reshape(seq_count * tok_count, feature_count)
    queries = (jnp.dot(flat_rows, query_w, preferred_element_type=jnp.float32) * HD ** (-0.5)).astype(jnp.bfloat16)
    keys_flat = jnp.dot(flat_rows, key_w, preferred_element_type=jnp.float32).astype(jnp.bfloat16)
    values_flat = jnp.dot(flat_rows, value_w, preferred_element_type=jnp.float32).astype(jnp.bfloat16)
    key_t = keys_flat.reshape(seq_count, tok_count, KV_HEADS, HD).transpose(0, 2, 3, 1)
    value_t = values_flat.reshape(seq_count, tok_count, KV_HEADS, HD).transpose(0, 2, 3, 1)
    group_size = HEADS // KV_HEADS
    block_rows = min(512, tok_count)
    block_count = tok_count // block_rows
    queries = queries.reshape(seq_count, tok_count, KV_HEADS, group_size, HD)
    positions = jnp.arange(tok_count)
    attended_list = []
    for seq_index in range(seq_count):
        first_valid = tok_count - lengths[seq_index] // STRIDE
        query_seq = queries[seq_index].astype(jnp.float32).reshape(block_count, block_rows, KV_HEADS, group_size, HD)
        query_seq = query_seq.transpose(2, 0, 3, 1, 4)
        key_seq = key_t[seq_index].astype(jnp.float32)
        value_seq = value_t[seq_index].astype(jnp.float32)

        def one_head(operands):
            query_head, key_mat, value_mat = operands

            def one_block(block_operands):
                query_block, start = block_operands
                rows = start + positions[:block_rows]
                allowed = (positions[None, :] <= rows[:, None]) & ((positions[None, :] >= first_valid) | (positions[None, :] == rows[:, None]))
                return attention_rows(query_block, key_mat, value_mat, allowed)
            starts = positions[:block_count] * block_rows
            return lax.map(one_block, (query_head, starts))
        out_seq = lax.map(one_head, (query_seq, key_seq, value_seq))
        attended_list.append(out_seq.transpose(1, 3, 0, 2, 4).reshape(tok_count, HEADS * HD))
    attended = jnp.stack(attended_list).reshape(seq_count * tok_count, HEADS * HD)
    update = jnp.dot(attended, out_w, preferred_element_type=jnp.float32).reshape(seq_count, tok_count, feature_count)
    return ((hidden32 + update).astype(jnp.bfloat16), key_t, value_t)

def reference(series, lengths, patch_weight, norm_gain, query_weight, key_weight, value_weight, out_weight):
    seq_count, channels, step_count = series.shape
    positions = jnp.arange(step_count)
    valid = (positions[None, :] >= (step_count - lengths)[:, None]).astype(jnp.float32)
    masked = series.astype(jnp.float32) * valid[:, None, :]
    history = lengths.astype(jnp.float32)[:, None]
    channel_mean = lax.optimization_barrier(jnp.sum(masked, -1)) / history
    centered = (masked - channel_mean[..., None]) * valid[:, None, :]
    variance = lax.optimization_barrier(jnp.sum(centered * centered, -1)) / history
    normed = (centered * lax.rsqrt(variance + 1e-05)[..., None]).astype(jnp.bfloat16)
    normed = lax.optimization_barrier(normed)
    blocks = normed.astype(jnp.float32).reshape(seq_count, channels, step_count // STRIDE, STRIDE)
    halves = patch_weight.astype(jnp.float32).reshape(channels, 2, STRIDE, D)
    right_terms = jnp.einsum('scjr,crd->sjd', blocks, halves[:, 1])
    left_all = jnp.einsum('scjr,crd->sjd', blocks, halves[:, 0])
    left_terms = jnp.concatenate([jnp.zeros_like(left_all[:, :1]), left_all[:, :-1]], 1)
    hidden_rows = (left_terms + right_terms).astype(jnp.bfloat16)
    key_list = []
    value_list = []
    for layer_index in range(LAYERS):
        hidden_rows, key_t, value_t = layer_pass(hidden_rows, lengths, norm_gain[layer_index], query_weight[layer_index], key_weight[layer_index], value_weight[layer_index], out_weight[layer_index])
        key_list.append(key_t)
        value_list.append(value_t)
    return (jnp.stack(key_list), jnp.stack(value_list), hidden_rows)
```

```python
import jax
import jax.numpy as jnp
from jax import lax
from jax.sharding import PartitionSpec as P

STRIDE = 32
HD = 80
SMALL_GROUP = 4


def shift_from(value, axis, size, by, cyclic):
    pairs = [(i, (i + by) % size) for i in range(size) if cyclic or i + by < size]
    return lax.ppermute(value, axis, pairs)


def gather_ordered(value, axis, size, me):
    if size > SMALL_GROUP:
        return lax.all_gather(value, axis, axis=0)
    received = [value] + [shift_from(value, axis, size, by, True) for by in range(1, size)]
    stack = jnp.stack(received, 0)
    order = (me - jnp.arange(size, dtype=jnp.int32)) % size
    return jnp.take(stack, order, axis=0)


def gather_causal(value, axis, size, me, width):
    if size > SMALL_GROUP:
        gathered = lax.all_gather(value, axis, axis=value.ndim - 1, tiled=True)
        return gathered, jnp.arange(size * width, dtype=jnp.int32)
    pieces = []
    positions = []
    local = jnp.arange(width, dtype=jnp.int32)
    for by in range(size - 1, 0, -1):
        pieces.append(shift_from(value, axis, size, by, False))
        positions.append((me - by) * width + local)
    pieces.append(value)
    positions.append(me * width + local)
    return jnp.concatenate(pieces, -1), jnp.concatenate(positions, 0)


def absorb_block(running, key_block, value_block, key_pos, query_rows, query_pos, first_valid):
    run_max, run_sum, accumulated = running
    allowed = (key_pos[None, None, :] <= query_pos[None, :, None]) & (
        (key_pos[None, None, :] >= first_valid[:, None, None])
        | (key_pos[None, None, :] == query_pos[None, :, None])
    )
    scores = jnp.einsum(
        "btkgh,bkhn->bkgtn", query_rows, key_block, preferred_element_type=jnp.float32
    )
    scores = jnp.where(allowed[:, None, None], scores, -jnp.inf)
    new_max = jnp.maximum(run_max, jnp.max(scores, -1))
    rescale = jnp.exp(run_max - new_max)
    exp_scores = jnp.exp(scores - new_max[..., None])
    new_sum = run_sum * rescale + jnp.sum(exp_scores, -1)
    contribution = jnp.einsum(
        "bkgtn,bkhn->bkgth",
        exp_scores.astype(jnp.bfloat16),
        value_block,
        preferred_element_type=jnp.float32,
    )
    return (new_max, new_sum, accumulated * rescale[..., None] + contribution)


def attend_layer(hidden_in, seq_lens, gain, query_w, key_w, value_w, out_w, sizes):
    tm_n, tm_at, total_tokens = sizes
    batch_count, tok_count, feature_count = hidden_in.shape
    hidden32 = hidden_in.astype(jnp.float32)
    gain32 = gain.astype(jnp.float32)
    scaled = hidden32 * lax.rsqrt(jnp.mean(hidden32 * hidden32, -1, keepdims=True) + 1e-06)
    layer_input = (scaled * gain32).astype(jnp.bfloat16)
    queries = (
        jnp.einsum("btd,de->bte", layer_input, query_w, preferred_element_type=jnp.float32)
        * HD ** (-0.5)
    ).astype(jnp.bfloat16)
    key_t = jnp.einsum(
        "btd,de->bet", layer_input, key_w, preferred_element_type=jnp.float32
    ).astype(jnp.bfloat16)
    value_t = jnp.einsum(
        "btd,de->bet", layer_input, value_w, preferred_element_type=jnp.float32
    ).astype(jnp.bfloat16)
    kv_local = key_w.shape[1] // HD
    group_size = query_w.shape[1] // key_w.shape[1]
    key_t = key_t.reshape(batch_count, kv_local, HD, tok_count)
    value_t = value_t.reshape(batch_count, kv_local, HD, tok_count)
    query_rows = queries.reshape(batch_count, tok_count, kv_local, group_size, HD)
    query_pos = tm_at * tok_count + jnp.arange(tok_count, dtype=jnp.int32)
    first_valid = total_tokens - seq_lens // STRIDE
    both, key_pos = gather_causal(jnp.stack([key_t, value_t], 0), "tm", tm_n, tm_at, tok_count)
    key_count = both.shape[-1]
    block_width = 1024 if key_count % 1024 == 0 else key_count
    rounds = key_count // block_width
    blocks = jnp.moveaxis(
        both.reshape(2, batch_count, kv_local, HD, rounds, block_width), 4, 0
    )
    pos_blocks = key_pos.reshape(rounds, block_width)
    start_state = (
        jnp.full((batch_count, kv_local, group_size, tok_count), -1e30, jnp.float32),
        jnp.zeros((batch_count, kv_local, group_size, tok_count), jnp.float32),
        jnp.zeros((batch_count, kv_local, group_size, tok_count, HD), jnp.float32),
    )
    if rounds == 1:
        result = absorb_block(
            start_state, blocks[0, 0], blocks[0, 1], pos_blocks[0], query_rows, query_pos,
            first_valid,
        )
    else:

        def scan_step(state, block_item):
            kv_block, pos_block = block_item
            return (
                absorb_block(
                    state, kv_block[0], kv_block[1], pos_block, query_rows, query_pos,
                    first_valid,
                ),
                None,
            )

        result, _ = lax.scan(scan_step, start_state, (blocks, pos_blocks))
    run_max, run_sum, accumulated = result
    attended = (accumulated / run_sum[..., None]).astype(jnp.bfloat16)
    attended = attended.transpose(0, 3, 1, 2, 4).reshape(
        batch_count, tok_count, kv_local * group_size * HD
    )
    partial_value = jnp.einsum("bte,ed->btd", attended, out_w, preferred_element_type=jnp.float32)
    return partial_value.astype(jnp.bfloat16), key_t, value_t


def per_device(
    series, lengths, patch_weight, norm_gain, query_weight, key_weight, value_weight, out_weight,
    *, tm_n, mp_n, sec_n
):
    seq_count, channels, steps_dev = series.shape
    tok_count = steps_dev // STRIDE
    tm_at = lax.axis_index("tm")
    mp_at = lax.axis_index("mp")
    sec_at = lax.axis_index("section")
    feat_axes = ("mp", "section")
    feat_n = mp_n * sec_n
    feat_at = mp_at * sec_n + sec_at
    total_steps = steps_dev * tm_n
    total_tokens = tok_count * tm_n

    prior_raw = shift_from(series[:, :, steps_dev - STRIDE :], "tm", tm_n, 1, False)

    first_step = total_steps - lengths
    step_pos = tm_at * steps_dev + jnp.arange(steps_dev, dtype=jnp.int32)
    valid = (step_pos[None, :] >= first_step[:, None]).astype(jnp.float32)
    values = series.astype(jnp.float32)
    masked = values * valid[:, None, :]
    local_sum = jnp.sum(masked, -1)
    shard_lo = jnp.arange(tm_n, dtype=jnp.int32) * steps_dev
    counts = jnp.clip(
        shard_lo[None, :] + steps_dev - jnp.maximum(shard_lo[None, :], first_step[:, None]),
        0,
        steps_dev,
    ).astype(jnp.float32)
    my_count = jnp.sum(valid, -1)
    local_mean = local_sum / jnp.maximum(my_count, 1.0)[:, None]
    local_dev = (values - local_mean[..., None]) * valid[:, None, :]
    local_m2 = jnp.sum(local_dev * local_dev, -1)
    stats = gather_ordered(jnp.stack([local_sum, local_m2], 0), "tm", tm_n, tm_at)
    history = lengths.astype(jnp.float32)[:, None]
    shard_sums = stats[:, 0]
    shard_m2 = stats[:, 1]
    channel_mean = jnp.sum(shard_sums, 0) / history
    shard_counts = jnp.moveaxis(counts, 1, 0)[:, :, None]
    shard_means = shard_sums / jnp.maximum(shard_counts, 1.0)
    gap = shard_means - channel_mean[None]
    spread_total = jnp.sum(shard_m2 + shard_counts * gap * gap, 0)
    variance = spread_total / history
    inv_std = lax.rsqrt(variance + 1e-05)[..., None]

    centered = (masked - channel_mean[..., None]) * valid[:, None, :]
    normed = (centered * inv_std).astype(jnp.bfloat16)
    prior_pos = tm_at * steps_dev - STRIDE + jnp.arange(STRIDE, dtype=jnp.int32)
    prior_valid = ((prior_pos[None, :] >= first_step[:, None]) & (prior_pos[None, :] >= 0)).astype(
        jnp.float32
    )[:, None, :]
    prior_normed = (
        (prior_raw.astype(jnp.float32) * prior_valid - channel_mean[..., None])
        * prior_valid
        * inv_std
    ).astype(jnp.bfloat16)

    blocks = normed.reshape(seq_count, channels, tok_count, STRIDE)
    column_count = patch_weight.shape[1]
    halves = patch_weight.reshape(channels, 2, STRIDE, column_count)
    right_terms = jnp.einsum(
        "scjr,crd->sjd", blocks, halves[:, 1], preferred_element_type=jnp.float32
    )
    left_all = jnp.einsum("scjr,crd->sjd", blocks, halves[:, 0], preferred_element_type=jnp.float32)
    edge_term = jnp.einsum(
        "scr,crd->sd", prior_normed, halves[:, 0], preferred_element_type=jnp.float32
    )
    left_terms = jnp.concatenate([edge_term[:, None, :], left_all[:, : tok_count - 1, :]], 1)
    tokens = (left_terms + right_terms).astype(jnp.bfloat16)

    pieces = gather_ordered(tokens, feat_axes, feat_n, feat_at)
    hidden0 = jnp.moveaxis(pieces, 0, 2).reshape(seq_count, tok_count, feat_n * column_count)
    feature_count = hidden0.shape[2]
    head_cols = feature_count // mp_n
    sizes = (tm_n, tm_at, total_tokens)

    partial0, key0, value0 = attend_layer(
        hidden0, lengths, norm_gain[0], query_weight[0], key_weight[0], value_weight[0],
        out_weight[0], sizes,
    )
    arrivals = []
    for by in range(mp_n):
        pairs = [(m * sec_n, ((m + by) % mp_n) * sec_n + 1) for m in range(mp_n)]
        arrivals.append(lax.ppermute(partial0, feat_axes, pairs))
    if mp_n > 1:
        order = (mp_at - jnp.arange(mp_n, dtype=jnp.int32)) % mp_n
        arrivals = jnp.take(jnp.stack(arrivals, 0), order, axis=0)
        head_sum = jnp.sum(arrivals.astype(jnp.float32), 0)
    else:
        head_sum = arrivals[0].astype(jnp.float32)
    hidden1 = (hidden0.astype(jnp.float32) + head_sum).astype(jnp.bfloat16)

    partial1, key1, value1 = attend_layer(
        hidden1, lengths, norm_gain[0], query_weight[0], key_weight[0], value_weight[0],
        out_weight[0], sizes,
    )
    is_first = sec_at == 0
    key_store = jnp.where(is_first, key0, key1)[None]
    value_store = jnp.where(is_first, value0, value1)[None]

    per_section = seq_count // sec_n
    low_rows = partial1[:per_section]
    high_rows = partial1[per_section:]
    low_hidden = hidden1[:per_section]
    to_low = []
    to_high = []
    for by in range(mp_n):
        target_mp = (mp_at + by) % mp_n
        cols = lax.dynamic_slice_in_dim(low_rows, target_mp * head_cols, head_cols, 2)
        if by == 0:
            cols = jnp.stack(
                [lax.dynamic_slice_in_dim(low_hidden, target_mp * head_cols, head_cols, 2), cols], 0
            )
        pairs = [(m * sec_n + 1, ((m + by) % mp_n) * sec_n) for m in range(mp_n)]
        to_low.append(lax.ppermute(cols, feat_axes, pairs))
        if by > 0:
            cols_high = lax.dynamic_slice_in_dim(high_rows, target_mp * head_cols, head_cols, 2)
            pairs = [(m * sec_n + 1, ((m + by) % mp_n) * sec_n + 1) for m in range(mp_n)]
            to_high.append(lax.ppermute(cols_high, feat_axes, pairs))
    low_total = to_low[0][0].astype(jnp.float32) + (
        to_low[0][1].astype(jnp.float32)
        + sum(piece.astype(jnp.float32) for piece in to_low[1:])
    )
    own_high = lax.dynamic_slice_in_dim(high_rows, mp_at * head_cols, head_cols, 2)
    own_hidden = lax.dynamic_slice_in_dim(hidden1[per_section:], mp_at * head_cols, head_cols, 2)
    high_total = own_hidden.astype(jnp.float32) + (
        own_high.astype(jnp.float32) + sum(piece.astype(jnp.float32) for piece in to_high)
    )
    final_cols = jnp.where(is_first, low_total, high_total).astype(jnp.bfloat16)
    return (key_store, value_store, final_cols)


def solution(mesh):
    sizes = dict(tm_n=mesh.shape["tm"], mp_n=mesh.shape["mp"], sec_n=mesh.shape["section"])
    in_specs = (
        P("groups", None, "tm"),
        P("groups"),
        P(None, ("mp", "section")),
        P("section", None),
        P("section", None, "mp"),
        P("section", None, "mp"),
        P("section", None, "mp"),
        P("section", "mp", None),
    )
    out_specs = (
        P("section", "groups", "mp", None, "tm"),
        P("section", "groups", "mp", None, "tm"),
        P(("groups", "section"), "tm", "mp"),
    )

    def body(*args):
        return per_device(*args, **sizes)

    return jax.shard_map(body, mesh=mesh, in_specs=in_specs, out_specs=out_specs, check_vma=False)
```

```python
import jax
import jax.numpy as jnp
from jax import lax
from jax.sharding import PartitionSpec as P

STRIDE = 32
HD = 80
SMALL_GROUP = 4


def shift_from(value, axis, size, by, cyclic):
    pairs = [(i, (i + by) % size) for i in range(size) if cyclic or i + by < size]
    return lax.ppermute(value, axis, pairs)


def gather_ordered(value, axis, size, me):
    if size > SMALL_GROUP:
        return lax.all_gather(value, axis, axis=0)
    received = [value] + [shift_from(value, axis, size, by, True) for by in range(1, size)]
    stack = jnp.stack(received, 0)
    order = (me - jnp.arange(size, dtype=jnp.int32)) % size
    return jnp.take(stack, order, axis=0)


def gather_causal(value, tm_n, sec_n, tm_at, phase, width):
    if tm_n > SMALL_GROUP:
        gathered = lax.all_gather(value, "tm", axis=value.ndim - 1, tiled=True)
        return gathered, jnp.arange(tm_n * width, dtype=jnp.int32)
    pieces = []
    positions = []
    local = jnp.arange(width, dtype=jnp.int32)
    for by in range(tm_n - 1, 0, -1):
        pairs = [(t * sec_n + phase, (t + by) * sec_n + phase) for t in range(tm_n - by)]
        pieces.append(lax.ppermute(value, ("tm", "section"), pairs))
        positions.append((tm_at - by) * width + local)
    pieces.append(value)
    positions.append(tm_at * width + local)
    return jnp.concatenate(pieces, -1), jnp.concatenate(positions, 0)


def absorb_block(running, key_block, value_block, key_pos, query_rows, query_pos, first_valid):
    run_max, run_sum, accumulated = running
    allowed = (key_pos[None, None, :] <= query_pos[None, :, None]) & (
        (key_pos[None, None, :] >= first_valid[:, None, None])
        | (key_pos[None, None, :] == query_pos[None, :, None])
    )
    scores = jnp.einsum(
        "btkgh,bkhn->bkgtn", query_rows, key_block, preferred_element_type=jnp.float32
    )
    scores = jnp.where(allowed[:, None, None], scores, -jnp.inf)
    new_max = jnp.maximum(run_max, jnp.max(scores, -1))
    rescale = jnp.exp(run_max - new_max)
    exp_scores = jnp.exp(scores - new_max[..., None])
    new_sum = run_sum * rescale + jnp.sum(exp_scores, -1)
    contribution = jnp.einsum(
        "bkgtn,bkhn->bkgth",
        exp_scores.astype(jnp.bfloat16),
        value_block,
        preferred_element_type=jnp.float32,
    )
    return (new_max, new_sum, accumulated * rescale[..., None] + contribution)


def attend_layer(hidden_in, seq_lens, gain, query_w, key_w, value_w, out_w, sizes, phase):
    tm_n, sec_n, tm_at, total_tokens = sizes
    batch_count, tok_count, feature_count = hidden_in.shape
    hidden32 = hidden_in.astype(jnp.float32)
    gain32 = gain.astype(jnp.float32)
    scaled = hidden32 * lax.rsqrt(jnp.mean(hidden32 * hidden32, -1, keepdims=True) + 1e-06)
    layer_input = (scaled * gain32).astype(jnp.bfloat16)
    queries = (
        jnp.einsum("btd,de->bte", layer_input, query_w, preferred_element_type=jnp.float32)
        * HD ** (-0.5)
    ).astype(jnp.bfloat16)
    key_t = jnp.einsum(
        "btd,de->bet", layer_input, key_w, preferred_element_type=jnp.float32
    ).astype(jnp.bfloat16)
    value_t = jnp.einsum(
        "btd,de->bet", layer_input, value_w, preferred_element_type=jnp.float32
    ).astype(jnp.bfloat16)
    kv_local = key_w.shape[1] // HD
    group_size = query_w.shape[1] // key_w.shape[1]
    key_t = key_t.reshape(batch_count, kv_local, HD, tok_count)
    value_t = value_t.reshape(batch_count, kv_local, HD, tok_count)
    query_rows = queries.reshape(batch_count, tok_count, kv_local, group_size, HD)
    query_pos = tm_at * tok_count + jnp.arange(tok_count, dtype=jnp.int32)
    first_valid = total_tokens - seq_lens // STRIDE
    both, key_pos = gather_causal(
        jnp.stack([key_t, value_t], 0), tm_n, sec_n, tm_at, phase, tok_count
    )
    key_count = both.shape[-1]
    block_width = 1024 if key_count % 1024 == 0 else key_count
    rounds = key_count // block_width
    blocks = jnp.moveaxis(
        both.reshape(2, batch_count, kv_local, HD, rounds, block_width), 4, 0
    )
    pos_blocks = key_pos.reshape(rounds, block_width)
    start_state = (
        jnp.full((batch_count, kv_local, group_size, tok_count), -1e30, jnp.float32),
        jnp.zeros((batch_count, kv_local, group_size, tok_count), jnp.float32),
        jnp.zeros((batch_count, kv_local, group_size, tok_count, HD), jnp.float32),
    )
    if rounds == 1:
        result = absorb_block(
            start_state, blocks[0, 0], blocks[0, 1], pos_blocks[0], query_rows, query_pos,
            first_valid,
        )
    else:

        def scan_step(state, block_item):
            kv_block, pos_block = block_item
            return (
                absorb_block(
                    state, kv_block[0], kv_block[1], pos_block, query_rows, query_pos,
                    first_valid,
                ),
                None,
            )

        result, _ = lax.scan(scan_step, start_state, (blocks, pos_blocks))
    run_max, run_sum, accumulated = result
    attended = (accumulated / run_sum[..., None]).astype(jnp.bfloat16)
    attended = attended.transpose(0, 3, 1, 2, 4).reshape(
        batch_count, tok_count, kv_local * group_size * HD
    )
    partial_value = jnp.einsum("bte,ed->btd", attended, out_w, preferred_element_type=jnp.float32)
    return partial_value.astype(jnp.bfloat16), key_t, value_t


def per_device(
    series, lengths, patch_weight, norm_gain, query_weight, key_weight, value_weight, out_weight,
    *, tm_n, mp_n, sec_n
):
    seq_count, channels, steps_dev = series.shape
    tok_count = steps_dev // STRIDE
    tm_at = lax.axis_index("tm")
    mp_at = lax.axis_index("mp")
    sec_at = lax.axis_index("section")
    feat_axes = ("mp", "section")
    feat_n = mp_n * sec_n
    feat_at = mp_at * sec_n + sec_at
    total_steps = steps_dev * tm_n
    total_tokens = tok_count * tm_n

    prior_raw = shift_from(series[:, :, steps_dev - STRIDE :], "tm", tm_n, 1, False)

    first_step = total_steps - lengths
    step_pos = tm_at * steps_dev + jnp.arange(steps_dev, dtype=jnp.int32)
    valid = (step_pos[None, :] >= first_step[:, None]).astype(jnp.float32)
    values = series.astype(jnp.float32)
    masked = values * valid[:, None, :]
    local_sum = jnp.sum(masked, -1)
    shard_lo = jnp.arange(tm_n, dtype=jnp.int32) * steps_dev
    counts = jnp.clip(
        shard_lo[None, :] + steps_dev - jnp.maximum(shard_lo[None, :], first_step[:, None]),
        0,
        steps_dev,
    ).astype(jnp.float32)
    my_count = jnp.sum(valid, -1)
    local_mean = local_sum / jnp.maximum(my_count, 1.0)[:, None]
    local_dev = (values - local_mean[..., None]) * valid[:, None, :]
    local_m2 = jnp.sum(local_dev * local_dev, -1)
    stats = gather_ordered(jnp.stack([local_sum, local_m2], 0), "tm", tm_n, tm_at)
    history = lengths.astype(jnp.float32)[:, None]
    shard_sums = stats[:, 0]
    shard_m2 = stats[:, 1]
    channel_mean = jnp.sum(shard_sums, 0) / history
    shard_counts = jnp.moveaxis(counts, 1, 0)[:, :, None]
    shard_means = shard_sums / jnp.maximum(shard_counts, 1.0)
    gap = shard_means - channel_mean[None]
    spread_total = jnp.sum(shard_m2 + shard_counts * gap * gap, 0)
    variance = spread_total / history
    inv_std = lax.rsqrt(variance + 1e-05)[..., None]

    padded = jnp.concatenate([prior_raw, series], -1).astype(jnp.float32)
    padded_pos = tm_at * steps_dev - STRIDE + jnp.arange(steps_dev + STRIDE, dtype=jnp.int32)
    padded_valid = (
        (padded_pos[None, :] >= first_step[:, None]) & (padded_pos[None, :] >= 0)
    ).astype(jnp.float32)[:, None, :]
    normed = (
        (padded * padded_valid - channel_mean[..., None]) * padded_valid * inv_std
    ).astype(jnp.bfloat16)
    left = normed[:, :, :steps_dev].reshape(seq_count, channels, tok_count, STRIDE)
    right = normed[:, :, STRIDE:].reshape(seq_count, channels, tok_count, STRIDE)
    window = jnp.concatenate([left, right], -1).transpose(0, 2, 1, 3)
    window = window.reshape(seq_count, tok_count, channels * 2 * STRIDE)
    tokens = jnp.einsum(
        "sjk,kd->sjd", window, patch_weight, preferred_element_type=jnp.float32
    ).astype(jnp.bfloat16)
    column_count = patch_weight.shape[1]
    hidden0 = lax.all_gather(tokens, feat_axes, axis=2, tiled=True)
    feature_count = hidden0.shape[2]
    head_cols = feature_count // mp_n
    sizes = (tm_n, sec_n, tm_at, total_tokens)

    partial0, key0, value0 = attend_layer(
        hidden0, lengths, norm_gain[0], query_weight[0], key_weight[0], value_weight[0],
        out_weight[0], sizes, 0,
    )
    arrivals = []
    for by in range(mp_n):
        pairs = [(m * sec_n, ((m + by) % mp_n) * sec_n + 1) for m in range(mp_n)]
        arrivals.append(lax.ppermute(partial0, feat_axes, pairs))
    if mp_n == 2:
        head_sum = arrivals[0].astype(jnp.float32) + arrivals[1].astype(jnp.float32)
    elif mp_n > 2:
        order = (mp_at - jnp.arange(mp_n, dtype=jnp.int32)) % mp_n
        arrivals = jnp.take(jnp.stack(arrivals, 0), order, axis=0)
        head_sum = jnp.sum(arrivals.astype(jnp.float32), 0)
    else:
        head_sum = arrivals[0].astype(jnp.float32)
    hidden1 = (hidden0.astype(jnp.float32) + head_sum).astype(jnp.bfloat16)

    partial1, key1, value1 = attend_layer(
        hidden1, lengths, norm_gain[0], query_weight[0], key_weight[0], value_weight[0],
        out_weight[0], sizes, 1,
    )
    is_first = sec_at == 0
    key_store = jnp.where(is_first, key0, key1)[None]
    value_store = jnp.where(is_first, value0, value1)[None]

    per_section = seq_count // sec_n
    low_rows = partial1[:per_section]
    high_rows = partial1[per_section:]
    low_hidden = hidden1[:per_section]
    to_low = []
    to_high = []
    for by in range(mp_n):
        target_mp = (mp_at + by) % mp_n
        cols = lax.dynamic_slice_in_dim(low_rows, target_mp * head_cols, head_cols, 2)
        if by == 0:
            cols = jnp.stack(
                [lax.dynamic_slice_in_dim(low_hidden, target_mp * head_cols, head_cols, 2), cols], 0
            )
        pairs = [(m * sec_n + 1, ((m + by) % mp_n) * sec_n) for m in range(mp_n)]
        to_low.append(lax.ppermute(cols, feat_axes, pairs))
        if by > 0:
            cols_high = lax.dynamic_slice_in_dim(high_rows, target_mp * head_cols, head_cols, 2)
            pairs = [(m * sec_n + 1, ((m + by) % mp_n) * sec_n + 1) for m in range(mp_n)]
            to_high.append(lax.ppermute(cols_high, feat_axes, pairs))
    low_total = to_low[0][0].astype(jnp.float32) + (
        to_low[0][1].astype(jnp.float32)
        + sum(piece.astype(jnp.float32) for piece in to_low[1:])
    )
    own_high = lax.dynamic_slice_in_dim(high_rows, mp_at * head_cols, head_cols, 2)
    own_hidden = lax.dynamic_slice_in_dim(hidden1[per_section:], mp_at * head_cols, head_cols, 2)
    high_total = own_hidden.astype(jnp.float32) + (
        own_high.astype(jnp.float32) + sum(piece.astype(jnp.float32) for piece in to_high)
    )
    final_cols = jnp.where(is_first, low_total, high_total).astype(jnp.bfloat16)
    return (key_store, value_store, final_cols)


def solution(mesh):
    sizes = dict(tm_n=mesh.shape["tm"], mp_n=mesh.shape["mp"], sec_n=mesh.shape["section"])
    in_specs = (
        P("groups", None, "tm"),
        P("groups"),
        P(None, ("mp", "section")),
        P("section", None),
        P("section", None, "mp"),
        P("section", None, "mp"),
        P("section", None, "mp"),
        P("section", "mp", None),
    )
    out_specs = (
        P("section", "groups", "mp", None, "tm"),
        P("section", "groups", "mp", None, "tm"),
        P(("groups", "section"), "tm", "mp"),
    )

    def body(*args):
        return per_device(*args, **sizes)

    return jax.shard_map(body, mesh=mesh, in_specs=in_specs, out_specs=out_specs, check_vma=False)
```

```python
import jax
import jax.numpy as jnp
from jax import lax
from jax.sharding import PartitionSpec as P

STRIDE = 32
HD = 80
SMALL_GROUP = 4


def shift_from(value, axis, size, by, cyclic):
    pairs = [(i, (i + by) % size) for i in range(size) if cyclic or i + by < size]
    return lax.ppermute(value, axis, pairs)


def gather_ordered(value, axis, size, me):
    if size > SMALL_GROUP:
        return lax.all_gather(value, axis, axis=0)
    received = [value] + [shift_from(value, axis, size, by, True) for by in range(1, size)]
    stack = jnp.stack(received, 0)
    order = (me - jnp.arange(size, dtype=jnp.int32)) % size
    return jnp.take(stack, order, axis=0)


def gather_causal(value, tm_n, sec_n, tm_at, phase, width):
    if tm_n > SMALL_GROUP:
        gathered = lax.all_gather(value, "tm", axis=value.ndim - 1, tiled=True)
        return gathered, jnp.arange(tm_n * width, dtype=jnp.int32)
    pieces = []
    positions = []
    local = jnp.arange(width, dtype=jnp.int32)
    for by in range(tm_n - 1, 0, -1):
        pairs = [(t * sec_n + phase, (t + by) * sec_n + phase) for t in range(tm_n - by)]
        pieces.append(lax.ppermute(value, ("tm", "section"), pairs))
        positions.append((tm_at - by) * width + local)
    pieces.append(value)
    positions.append(tm_at * width + local)
    return jnp.concatenate(pieces, -1), jnp.concatenate(positions, 0)


def absorb_block(running, key_block, value_block, key_pos, query_rows, query_pos, first_valid):
    run_max, run_sum, accumulated = running
    allowed = (key_pos[None, None, :] <= query_pos[None, :, None]) & (
        (key_pos[None, None, :] >= first_valid[:, None, None])
        | (key_pos[None, None, :] == query_pos[None, :, None])
    )
    scores = jnp.einsum(
        "btkgh,bkhn->bkgtn", query_rows, key_block, preferred_element_type=jnp.float32
    )
    scores = jnp.where(allowed[:, None, None], scores, -jnp.inf)
    new_max = jnp.maximum(run_max, jnp.max(scores, -1))
    rescale = jnp.exp(run_max - new_max)
    exp_scores = jnp.exp(scores - new_max[..., None])
    new_sum = run_sum * rescale + jnp.sum(exp_scores, -1)
    contribution = jnp.einsum(
        "bkgtn,bkhn->bkgth",
        exp_scores.astype(jnp.bfloat16),
        value_block,
        preferred_element_type=jnp.float32,
    )
    return (new_max, new_sum, accumulated * rescale[..., None] + contribution)


def attend_layer(hidden_in, seq_lens, gain, query_w, key_w, value_w, out_w, sizes, phase):
    tm_n, sec_n, tm_at, total_tokens = sizes
    batch_count, tok_count, feature_count = hidden_in.shape
    hidden32 = hidden_in.astype(jnp.float32)
    gain32 = gain.astype(jnp.float32)
    scaled = hidden32 * lax.rsqrt(jnp.mean(hidden32 * hidden32, -1, keepdims=True) + 1e-06)
    layer_input = (scaled * gain32).astype(jnp.bfloat16)
    queries = (
        jnp.einsum("btd,de->bte", layer_input, query_w, preferred_element_type=jnp.float32)
        * HD ** (-0.5)
    ).astype(jnp.bfloat16)
    key_t = jnp.einsum(
        "btd,de->bet", layer_input, key_w, preferred_element_type=jnp.float32
    ).astype(jnp.bfloat16)
    value_t = jnp.einsum(
        "btd,de->bet", layer_input, value_w, preferred_element_type=jnp.float32
    ).astype(jnp.bfloat16)
    kv_local = key_w.shape[1] // HD
    group_size = query_w.shape[1] // key_w.shape[1]
    key_t = key_t.reshape(batch_count, kv_local, HD, tok_count)
    value_t = value_t.reshape(batch_count, kv_local, HD, tok_count)
    query_rows = queries.reshape(batch_count, tok_count, kv_local, group_size, HD)
    query_pos = tm_at * tok_count + jnp.arange(tok_count, dtype=jnp.int32)
    first_valid = total_tokens - seq_lens // STRIDE
    both, key_pos = gather_causal(
        jnp.stack([key_t, value_t], 0), tm_n, sec_n, tm_at, phase, tok_count
    )
    key_count = both.shape[-1]
    block_width = 1024 if key_count % 1024 == 0 else key_count
    rounds = key_count // block_width
    blocks = jnp.moveaxis(
        both.reshape(2, batch_count, kv_local, HD, rounds, block_width), 4, 0
    )
    pos_blocks = key_pos.reshape(rounds, block_width)
    start_state = (
        jnp.full((batch_count, kv_local, group_size, tok_count), -1e30, jnp.float32),
        jnp.zeros((batch_count, kv_local, group_size, tok_count), jnp.float32),
        jnp.zeros((batch_count, kv_local, group_size, tok_count, HD), jnp.float32),
    )
    if rounds == 1:
        result = absorb_block(
            start_state, blocks[0, 0], blocks[0, 1], pos_blocks[0], query_rows, query_pos,
            first_valid,
        )
    else:

        def scan_step(state, block_item):
            kv_block, pos_block = block_item
            return (
                absorb_block(
                    state, kv_block[0], kv_block[1], pos_block, query_rows, query_pos,
                    first_valid,
                ),
                None,
            )

        result, _ = lax.scan(scan_step, start_state, (blocks, pos_blocks))
    run_max, run_sum, accumulated = result
    attended = (accumulated / run_sum[..., None]).astype(jnp.bfloat16)
    attended = attended.transpose(0, 3, 1, 2, 4).reshape(
        batch_count, tok_count, kv_local * group_size * HD
    )
    partial_value = jnp.einsum("bte,ed->btd", attended, out_w, preferred_element_type=jnp.float32)
    return partial_value.astype(jnp.bfloat16), key_t, value_t


def per_device(
    series, lengths, patch_weight, norm_gain, query_weight, key_weight, value_weight, out_weight,
    *, tm_n, mp_n, sec_n
):
    seq_count, channels, steps_dev = series.shape
    tok_count = steps_dev // STRIDE
    tm_at = lax.axis_index("tm")
    mp_at = lax.axis_index("mp")
    sec_at = lax.axis_index("section")
    feat_axes = ("mp", "section")
    feat_n = mp_n * sec_n
    feat_at = mp_at * sec_n + sec_at
    total_steps = steps_dev * tm_n
    total_tokens = tok_count * tm_n

    first_step = total_steps - lengths
    step_pos = tm_at * steps_dev + jnp.arange(steps_dev, dtype=jnp.int32)
    valid = (step_pos[None, :] >= first_step[:, None]).astype(jnp.float32)
    values = series.astype(jnp.float32)
    masked = values * valid[:, None, :]
    local_sum = jnp.sum(masked, -1)
    shard_lo = jnp.arange(tm_n, dtype=jnp.int32) * steps_dev
    counts = jnp.clip(
        shard_lo[None, :] + steps_dev - jnp.maximum(shard_lo[None, :], first_step[:, None]),
        0,
        steps_dev,
    ).astype(jnp.float32)
    my_count = jnp.sum(valid, -1)
    local_mean = local_sum / jnp.maximum(my_count, 1.0)[:, None]
    local_dev = (values - local_mean[..., None]) * valid[:, None, :]
    local_m2 = jnp.sum(local_dev * local_dev, -1)
    tail = series[:, :, steps_dev - STRIDE :]
    if tm_n > SMALL_GROUP:
        stats = lax.all_gather(jnp.stack([local_sum, local_m2], -1), "tm", axis=0)
        prior_raw = shift_from(tail, "tm", tm_n, 1, False).astype(jnp.float32)
    else:
        payload = jnp.concatenate(
            [jnp.stack([local_sum, local_m2], -1), tail.astype(jnp.float32)], -1
        )
        received = [payload] + [shift_from(payload, "tm", tm_n, by, True) for by in range(1, tm_n)]
        prior_raw = received[1][..., 2:] if tm_n > 1 else jnp.zeros_like(payload[..., 2:])
        order = (tm_at - jnp.arange(tm_n, dtype=jnp.int32)) % tm_n
        stats = jnp.take(jnp.stack([piece[..., :2] for piece in received], 0), order, axis=0)
    history = lengths.astype(jnp.float32)[:, None]
    shard_sums = stats[..., 0]
    shard_m2 = stats[..., 1]
    channel_mean = jnp.sum(shard_sums, 0) / history
    shard_counts = jnp.moveaxis(counts, 1, 0)[:, :, None]
    shard_means = shard_sums / jnp.maximum(shard_counts, 1.0)
    gap = shard_means - channel_mean[None]
    spread_total = jnp.sum(shard_m2 + shard_counts * gap * gap, 0)
    variance = spread_total / history
    inv_std = lax.rsqrt(variance + 1e-05)[..., None]

    padded = jnp.concatenate([prior_raw, series.astype(jnp.float32)], -1)
    padded_pos = tm_at * steps_dev - STRIDE + jnp.arange(steps_dev + STRIDE, dtype=jnp.int32)
    padded_valid = (
        (padded_pos[None, :] >= first_step[:, None]) & (padded_pos[None, :] >= 0)
    ).astype(jnp.float32)[:, None, :]
    normed = (
        (padded * padded_valid - channel_mean[..., None]) * padded_valid * inv_std
    ).astype(jnp.bfloat16)
    blocks = jnp.swapaxes(normed.reshape(seq_count, channels, tok_count + 1, STRIDE), 2, 3)
    window = jnp.concatenate([blocks[..., :tok_count], blocks[..., 1:]], 2)
    window = window.reshape(seq_count, channels * 2 * STRIDE, tok_count)
    tokens = jnp.einsum(
        "kd,skj->sjd", patch_weight, window, preferred_element_type=jnp.float32
    ).astype(jnp.bfloat16)
    column_count = patch_weight.shape[1]
    hidden0 = lax.all_gather(tokens, feat_axes, axis=2, tiled=True)
    feature_count = hidden0.shape[2]
    head_cols = feature_count // mp_n
    sizes = (tm_n, sec_n, tm_at, total_tokens)

    partial0, key0, value0 = attend_layer(
        hidden0, lengths, norm_gain[0], query_weight[0], key_weight[0], value_weight[0],
        out_weight[0], sizes, 0,
    )
    arrivals = []
    for by in range(mp_n):
        pairs = [(m * sec_n, ((m + by) % mp_n) * sec_n + 1) for m in range(mp_n)]
        arrivals.append(lax.ppermute(partial0, feat_axes, pairs))
    if mp_n == 2:
        head_sum = arrivals[0].astype(jnp.float32) + arrivals[1].astype(jnp.float32)
    elif mp_n > 2:
        order = (mp_at - jnp.arange(mp_n, dtype=jnp.int32)) % mp_n
        arrivals = jnp.take(jnp.stack(arrivals, 0), order, axis=0)
        head_sum = jnp.sum(arrivals.astype(jnp.float32), 0)
    else:
        head_sum = arrivals[0].astype(jnp.float32)
    hidden1 = (hidden0.astype(jnp.float32) + head_sum).astype(jnp.bfloat16)

    partial1, key1, value1 = attend_layer(
        hidden1, lengths, norm_gain[0], query_weight[0], key_weight[0], value_weight[0],
        out_weight[0], sizes, 1,
    )
    is_first = sec_at == 0
    key_store = jnp.where(is_first, key0, key1)[None]
    value_store = jnp.where(is_first, value0, value1)[None]

    per_section = seq_count // sec_n
    low_rows = partial1[:per_section]
    high_rows = partial1[per_section:]
    low_hidden = hidden1[:per_section]
    to_low = []
    to_high = []
    for by in range(mp_n):
        target_mp = (mp_at + by) % mp_n
        cols = lax.dynamic_slice_in_dim(low_rows, target_mp * head_cols, head_cols, 2)
        if by == 0:
            cols = jnp.stack(
                [lax.dynamic_slice_in_dim(low_hidden, target_mp * head_cols, head_cols, 2), cols], 0
            )
        pairs = [(m * sec_n + 1, ((m + by) % mp_n) * sec_n) for m in range(mp_n)]
        to_low.append(lax.ppermute(cols, feat_axes, pairs))
        if by > 0:
            cols_high = lax.dynamic_slice_in_dim(high_rows, target_mp * head_cols, head_cols, 2)
            pairs = [(m * sec_n + 1, ((m + by) % mp_n) * sec_n + 1) for m in range(mp_n)]
            to_high.append(lax.ppermute(cols_high, feat_axes, pairs))
    low_total = to_low[0][0].astype(jnp.float32) + (
        to_low[0][1].astype(jnp.float32)
        + sum(piece.astype(jnp.float32) for piece in to_low[1:])
    )
    own_high = lax.dynamic_slice_in_dim(high_rows, mp_at * head_cols, head_cols, 2)
    own_hidden = lax.dynamic_slice_in_dim(hidden1[per_section:], mp_at * head_cols, head_cols, 2)
    high_total = own_hidden.astype(jnp.float32) + (
        own_high.astype(jnp.float32) + sum(piece.astype(jnp.float32) for piece in to_high)
    )
    final_cols = jnp.where(is_first, low_total, high_total).astype(jnp.bfloat16)
    return (key_store, value_store, final_cols)


def solution(mesh):
    sizes = dict(tm_n=mesh.shape["tm"], mp_n=mesh.shape["mp"], sec_n=mesh.shape["section"])
    in_specs = (
        P("groups", None, "tm"),
        P("groups"),
        P(None, ("mp", "section")),
        P("section", None),
        P("section", None, "mp"),
        P("section", None, "mp"),
        P("section", None, "mp"),
        P("section", "mp", None),
    )
    out_specs = (
        P("section", "groups", "mp", None, "tm"),
        P("section", "groups", "mp", None, "tm"),
        P(("groups", "section"), "tm", "mp"),
    )

    def body(*args):
        return per_device(*args, **sizes)

    return jax.shard_map(body, mesh=mesh, in_specs=in_specs, out_specs=out_specs, check_vma=False)
```

```python
import jax
import jax.numpy as jnp
from jax import lax
from jax.sharding import PartitionSpec as P

STRIDE = 32
HD = 80
SMALL_GROUP = 4


def shift_from(value, axis, size, by, cyclic):
    pairs = [(i, (i + by) % size) for i in range(size) if cyclic or i + by < size]
    return lax.ppermute(value, axis, pairs)


def gather_ordered(value, axis, size, me):
    if size > SMALL_GROUP:
        return lax.all_gather(value, axis, axis=0)
    received = [value] + [shift_from(value, axis, size, by, True) for by in range(1, size)]
    stack = jnp.stack(received, 0)
    order = (me - jnp.arange(size, dtype=jnp.int32)) % size
    return jnp.take(stack, order, axis=0)


def gather_causal(value, tm_n, sec_n, tm_at, phase, width):
    if tm_n > SMALL_GROUP:
        gathered = lax.all_gather(value, "tm", axis=value.ndim - 1, tiled=True)
        return gathered, jnp.arange(tm_n * width, dtype=jnp.int32)
    pieces = []
    positions = []
    local = jnp.arange(width, dtype=jnp.int32)
    for by in range(tm_n - 1, 0, -1):
        pairs = [(t * sec_n + phase, (t + by) * sec_n + phase) for t in range(tm_n - by)]
        pieces.append(lax.ppermute(value, ("tm", "section"), pairs))
        positions.append((tm_at - by) * width + local)
    pieces.append(value)
    positions.append(tm_at * width + local)
    return jnp.concatenate(pieces, -1), jnp.concatenate(positions, 0)


def absorb_block(running, key_block, value_block, key_pos, query_rows, query_pos, first_valid):
    run_max, run_sum, accumulated = running
    allowed = (key_pos[None, None, :] <= query_pos[None, :, None]) & (
        (key_pos[None, None, :] >= first_valid[:, None, None])
        | (key_pos[None, None, :] == query_pos[None, :, None])
    )
    scores = jnp.einsum(
        "btkgh,bkhn->bkgtn", query_rows, key_block, preferred_element_type=jnp.float32
    )
    scores = jnp.where(allowed[:, None, None], scores, -jnp.inf)
    new_max = jnp.maximum(run_max, jnp.max(scores, -1))
    rescale = jnp.exp(run_max - new_max)
    exp_scores = jnp.exp(scores - new_max[..., None])
    new_sum = run_sum * rescale + jnp.sum(exp_scores, -1)
    contribution = jnp.einsum(
        "bkgtn,bkhn->bkgth",
        exp_scores.astype(jnp.bfloat16),
        value_block,
        preferred_element_type=jnp.float32,
    )
    return (new_max, new_sum, accumulated * rescale[..., None] + contribution)


def attend_layer(hidden_in, seq_lens, gain, query_w, key_w, value_w, out_w, sizes, phase):
    tm_n, sec_n, tm_at, total_tokens = sizes
    batch_count, tok_count, feature_count = hidden_in.shape
    hidden32 = hidden_in.astype(jnp.float32)
    gain32 = gain.astype(jnp.float32)
    scaled = hidden32 * lax.rsqrt(jnp.mean(hidden32 * hidden32, -1, keepdims=True) + 1e-06)
    layer_input = (scaled * gain32).astype(jnp.bfloat16)
    queries = (
        jnp.einsum("btd,de->bte", layer_input, query_w, preferred_element_type=jnp.float32)
        * HD ** (-0.5)
    ).astype(jnp.bfloat16)
    key_t = jnp.einsum(
        "btd,de->bet", layer_input, key_w, preferred_element_type=jnp.float32
    ).astype(jnp.bfloat16)
    value_t = jnp.einsum(
        "btd,de->bet", layer_input, value_w, preferred_element_type=jnp.float32
    ).astype(jnp.bfloat16)
    kv_local = key_w.shape[1] // HD
    group_size = query_w.shape[1] // key_w.shape[1]
    key_t = key_t.reshape(batch_count, kv_local, HD, tok_count)
    value_t = value_t.reshape(batch_count, kv_local, HD, tok_count)
    query_rows = queries.reshape(batch_count, tok_count, kv_local, group_size, HD)
    query_pos = tm_at * tok_count + jnp.arange(tok_count, dtype=jnp.int32)
    first_valid = total_tokens - seq_lens // STRIDE
    both, key_pos = gather_causal(
        jnp.stack([key_t, value_t], 0), tm_n, sec_n, tm_at, phase, tok_count
    )
    key_count = both.shape[-1]
    block_width = 1024 if key_count % 1024 == 0 else key_count
    rounds = key_count // block_width
    blocks = jnp.moveaxis(
        both.reshape(2, batch_count, kv_local, HD, rounds, block_width), 4, 0
    )
    pos_blocks = key_pos.reshape(rounds, block_width)
    start_state = (
        jnp.full((batch_count, kv_local, group_size, tok_count), -1e30, jnp.float32),
        jnp.zeros((batch_count, kv_local, group_size, tok_count), jnp.float32),
        jnp.zeros((batch_count, kv_local, group_size, tok_count, HD), jnp.float32),
    )
    if rounds == 1:
        result = absorb_block(
            start_state, blocks[0, 0], blocks[0, 1], pos_blocks[0], query_rows, query_pos,
            first_valid,
        )
    else:

        def scan_step(state, block_item):
            kv_block, pos_block = block_item
            return (
                absorb_block(
                    state, kv_block[0], kv_block[1], pos_block, query_rows, query_pos,
                    first_valid,
                ),
                None,
            )

        result, _ = lax.scan(scan_step, start_state, (blocks, pos_blocks))
    run_max, run_sum, accumulated = result
    attended = (accumulated / run_sum[..., None]).astype(jnp.bfloat16)
    attended = attended.transpose(0, 3, 1, 2, 4).reshape(
        batch_count, tok_count, kv_local * group_size * HD
    )
    partial_value = jnp.einsum("bte,ed->btd", attended, out_w, preferred_element_type=jnp.float32)
    return partial_value.astype(jnp.bfloat16), key_t, value_t


def per_device(
    series, lengths, patch_weight, norm_gain, query_weight, key_weight, value_weight, out_weight,
    *, tm_n, mp_n, sec_n
):
    seq_count, channels, steps_dev = series.shape
    tok_count = steps_dev // STRIDE
    tm_at = lax.axis_index("tm")
    mp_at = lax.axis_index("mp")
    sec_at = lax.axis_index("section")
    feat_axes = ("mp", "section")
    feat_n = mp_n * sec_n
    feat_at = mp_at * sec_n + sec_at
    total_steps = steps_dev * tm_n
    total_tokens = tok_count * tm_n

    first_step = total_steps - lengths
    step_pos = tm_at * steps_dev + jnp.arange(steps_dev, dtype=jnp.int32)
    valid = (step_pos[None, :] >= first_step[:, None]).astype(jnp.float32)
    values = series.astype(jnp.float32)
    masked = values * valid[:, None, :]
    local_sum = jnp.sum(masked, -1)
    shard_lo = jnp.arange(tm_n, dtype=jnp.int32) * steps_dev
    counts = jnp.clip(
        shard_lo[None, :] + steps_dev - jnp.maximum(shard_lo[None, :], first_step[:, None]),
        0,
        steps_dev,
    ).astype(jnp.float32)
    my_count = jnp.sum(valid, -1)
    local_mean = local_sum / jnp.maximum(my_count, 1.0)[:, None]
    local_dev = (values - local_mean[..., None]) * valid[:, None, :]
    local_m2 = jnp.sum(local_dev * local_dev, -1)
    tail = series[:, :, steps_dev - STRIDE :]
    if tm_n > SMALL_GROUP:
        stats = lax.all_gather(jnp.stack([local_sum, local_m2], -1), "tm", axis=0)
        prior_raw = shift_from(tail, "tm", tm_n, 1, False).astype(jnp.float32)
    else:
        payload = jnp.concatenate(
            [jnp.stack([local_sum, local_m2], -1), tail.astype(jnp.float32)], -1
        )
        received = [payload] + [shift_from(payload, "tm", tm_n, by, True) for by in range(1, tm_n)]
        prior_raw = received[1][..., 2:] if tm_n > 1 else jnp.zeros_like(payload[..., 2:])
        order = (tm_at - jnp.arange(tm_n, dtype=jnp.int32)) % tm_n
        stats = jnp.take(jnp.stack([piece[..., :2] for piece in received], 0), order, axis=0)
    history = lengths.astype(jnp.float32)[:, None]
    shard_sums = stats[..., 0]
    shard_m2 = stats[..., 1]
    channel_mean = jnp.sum(shard_sums, 0) / history
    shard_counts = jnp.moveaxis(counts, 1, 0)[:, :, None]
    shard_means = shard_sums / jnp.maximum(shard_counts, 1.0)
    gap = shard_means - channel_mean[None]
    spread_total = jnp.sum(shard_m2 + shard_counts * gap * gap, 0)
    variance = spread_total / history
    inv_std = lax.rsqrt(variance + 1e-05)[..., None]

    padded = jnp.concatenate([prior_raw, series.astype(jnp.float32)], -1)
    padded_pos = tm_at * steps_dev - STRIDE + jnp.arange(steps_dev + STRIDE, dtype=jnp.int32)
    padded_valid = (
        (padded_pos[None, :] >= first_step[:, None]) & (padded_pos[None, :] >= 0)
    ).astype(jnp.float32)[:, None, :]
    normed = (
        (padded * padded_valid - channel_mean[..., None]) * padded_valid * inv_std
    ).astype(jnp.bfloat16)
    kernel = patch_weight.reshape(channels, 2 * STRIDE, patch_weight.shape[1])
    tokens = lax.conv_general_dilated(
        normed,
        kernel,
        window_strides=(STRIDE,),
        padding="VALID",
        dimension_numbers=("NCW", "IWO", "NWC"),
        preferred_element_type=jnp.float32,
    ).astype(jnp.bfloat16)
    column_count = patch_weight.shape[1]
    hidden0 = lax.all_gather(tokens, feat_axes, axis=2, tiled=True)
    feature_count = hidden0.shape[2]
    head_cols = feature_count // mp_n
    sizes = (tm_n, sec_n, tm_at, total_tokens)

    partial0, key0, value0 = attend_layer(
        hidden0, lengths, norm_gain[0], query_weight[0], key_weight[0], value_weight[0],
        out_weight[0], sizes, 0,
    )
    arrivals = []
    for by in range(mp_n):
        pairs = [(m * sec_n, ((m + by) % mp_n) * sec_n + 1) for m in range(mp_n)]
        arrivals.append(lax.ppermute(partial0, feat_axes, pairs))
    if mp_n == 2:
        head_sum = arrivals[0].astype(jnp.float32) + arrivals[1].astype(jnp.float32)
    elif mp_n > 2:
        order = (mp_at - jnp.arange(mp_n, dtype=jnp.int32)) % mp_n
        arrivals = jnp.take(jnp.stack(arrivals, 0), order, axis=0)
        head_sum = jnp.sum(arrivals.astype(jnp.float32), 0)
    else:
        head_sum = arrivals[0].astype(jnp.float32)
    hidden1 = (hidden0.astype(jnp.float32) + head_sum).astype(jnp.bfloat16)

    partial1, key1, value1 = attend_layer(
        hidden1, lengths, norm_gain[0], query_weight[0], key_weight[0], value_weight[0],
        out_weight[0], sizes, 1,
    )
    is_first = sec_at == 0
    key_store = jnp.where(is_first, key0, key1)[None]
    value_store = jnp.where(is_first, value0, value1)[None]

    per_section = seq_count // sec_n
    low_rows = partial1[:per_section]
    high_rows = partial1[per_section:]
    low_hidden = hidden1[:per_section]
    to_low = []
    to_high = []
    for by in range(mp_n):
        target_mp = (mp_at + by) % mp_n
        cols = lax.dynamic_slice_in_dim(low_rows, target_mp * head_cols, head_cols, 2)
        if by == 0:
            cols = jnp.stack(
                [lax.dynamic_slice_in_dim(low_hidden, target_mp * head_cols, head_cols, 2), cols], 0
            )
        pairs = [(m * sec_n + 1, ((m + by) % mp_n) * sec_n) for m in range(mp_n)]
        to_low.append(lax.ppermute(cols, feat_axes, pairs))
        if by > 0:
            cols_high = lax.dynamic_slice_in_dim(high_rows, target_mp * head_cols, head_cols, 2)
            pairs = [(m * sec_n + 1, ((m + by) % mp_n) * sec_n + 1) for m in range(mp_n)]
            to_high.append(lax.ppermute(cols_high, feat_axes, pairs))
    low_total = to_low[0][0].astype(jnp.float32) + (
        to_low[0][1].astype(jnp.float32)
        + sum(piece.astype(jnp.float32) for piece in to_low[1:])
    )
    own_high = lax.dynamic_slice_in_dim(high_rows, mp_at * head_cols, head_cols, 2)
    own_hidden = lax.dynamic_slice_in_dim(hidden1[per_section:], mp_at * head_cols, head_cols, 2)
    high_total = own_hidden.astype(jnp.float32) + (
        own_high.astype(jnp.float32) + sum(piece.astype(jnp.float32) for piece in to_high)
    )
    final_cols = jnp.where(is_first, low_total, high_total).astype(jnp.bfloat16)
    return (key_store, value_store, final_cols)


def solution(mesh):
    sizes = dict(tm_n=mesh.shape["tm"], mp_n=mesh.shape["mp"], sec_n=mesh.shape["section"])
    in_specs = (
        P("groups", None, "tm"),
        P("groups"),
        P(None, ("mp", "section")),
        P("section", None),
        P("section", None, "mp"),
        P("section", None, "mp"),
        P("section", None, "mp"),
        P("section", "mp", None),
    )
    out_specs = (
        P("section", "groups", "mp", None, "tm"),
        P("section", "groups", "mp", None, "tm"),
        P(("groups", "section"), "tm", "mp"),
    )

    def body(*args):
        return per_device(*args, **sizes)

    return jax.shard_map(body, mesh=mesh, in_specs=in_specs, out_specs=out_specs, check_vma=False)
```

```python
import jax
import jax.numpy as jnp
from jax import lax
from jax.sharding import PartitionSpec as P

STRIDE = 32
HD = 80
SMALL_GROUP = 4


def shift_from(value, axis, size, by, cyclic):
    pairs = [(i, (i + by) % size) for i in range(size) if cyclic or i + by < size]
    return lax.ppermute(value, axis, pairs)


def gather_ordered(value, axis, size, me):
    if size > SMALL_GROUP:
        return lax.all_gather(value, axis, axis=0)
    received = [value] + [shift_from(value, axis, size, by, True) for by in range(1, size)]
    stack = jnp.stack(received, 0)
    order = (me - jnp.arange(size, dtype=jnp.int32)) % size
    return jnp.take(stack, order, axis=0)


def gather_causal(value, tm_n, sec_n, tm_at, phase, width):
    if tm_n > SMALL_GROUP:
        gathered = lax.all_gather(value, "tm", axis=value.ndim - 1, tiled=True)
        return gathered, jnp.arange(tm_n * width, dtype=jnp.int32)
    pieces = []
    positions = []
    local = jnp.arange(width, dtype=jnp.int32)
    for by in range(tm_n - 1, 0, -1):
        pairs = [(t * sec_n + phase, (t + by) * sec_n + phase) for t in range(tm_n - by)]
        pieces.append(lax.ppermute(value, ("tm", "section"), pairs))
        positions.append((tm_at - by) * width + local)
    pieces.append(value)
    positions.append(tm_at * width + local)
    return jnp.concatenate(pieces, -1), jnp.concatenate(positions, 0)


def absorb_block(running, key_block, value_block, key_pos, query_rows, query_pos, first_valid):
    run_max, run_sum, accumulated = running
    allowed = (key_pos[None, None, :] <= query_pos[None, :, None]) & (
        (key_pos[None, None, :] >= first_valid[:, None, None])
        | (key_pos[None, None, :] == query_pos[None, :, None])
    )
    scores = jnp.einsum(
        "btkgh,bkhn->bkgtn", query_rows, key_block, preferred_element_type=jnp.float32
    )
    scores = jnp.where(allowed[:, None, None], scores, -jnp.inf)
    new_max = jnp.maximum(run_max, jnp.max(scores, -1))
    rescale = jnp.exp(run_max - new_max)
    exp_scores = jnp.exp(scores - new_max[..., None])
    new_sum = run_sum * rescale + jnp.sum(exp_scores, -1)
    contribution = jnp.einsum(
        "bkgtn,bkhn->bkgth",
        exp_scores.astype(jnp.bfloat16),
        value_block,
        preferred_element_type=jnp.float32,
    )
    return (new_max, new_sum, accumulated * rescale[..., None] + contribution)


def attend_layer(hidden_in, seq_lens, gain, query_w, key_w, value_w, out_w, sizes, phase):
    tm_n, sec_n, tm_at, total_tokens = sizes
    batch_count, tok_count, feature_count = hidden_in.shape
    hidden32 = hidden_in.astype(jnp.float32)
    gain32 = gain.astype(jnp.float32)
    scaled = hidden32 * lax.rsqrt(jnp.mean(hidden32 * hidden32, -1, keepdims=True) + 1e-06)
    layer_input = (scaled * gain32).astype(jnp.bfloat16)
    queries = (
        jnp.einsum("btd,de->bte", layer_input, query_w, preferred_element_type=jnp.float32)
        * HD ** (-0.5)
    ).astype(jnp.bfloat16)
    key_t = jnp.einsum(
        "btd,de->bet", layer_input, key_w, preferred_element_type=jnp.float32
    ).astype(jnp.bfloat16)
    value_t = jnp.einsum(
        "btd,de->bet", layer_input, value_w, preferred_element_type=jnp.float32
    ).astype(jnp.bfloat16)
    kv_local = key_w.shape[1] // HD
    group_size = query_w.shape[1] // key_w.shape[1]
    key_t = key_t.reshape(batch_count, kv_local, HD, tok_count)
    value_t = value_t.reshape(batch_count, kv_local, HD, tok_count)
    query_rows = queries.reshape(batch_count, tok_count, kv_local, group_size, HD)
    query_pos = tm_at * tok_count + jnp.arange(tok_count, dtype=jnp.int32)
    first_valid = total_tokens - seq_lens // STRIDE
    both, key_pos = gather_causal(
        jnp.stack([key_t, value_t], 0), tm_n, sec_n, tm_at, phase, tok_count
    )
    key_count = both.shape[-1]
    block_width = 1024 if key_count % 1024 == 0 else key_count
    rounds = key_count // block_width
    blocks = jnp.moveaxis(
        both.reshape(2, batch_count, kv_local, HD, rounds, block_width), 4, 0
    )
    pos_blocks = key_pos.reshape(rounds, block_width)
    start_state = (
        jnp.full((batch_count, kv_local, group_size, tok_count), -1e30, jnp.float32),
        jnp.zeros((batch_count, kv_local, group_size, tok_count), jnp.float32),
        jnp.zeros((batch_count, kv_local, group_size, tok_count, HD), jnp.float32),
    )
    if rounds == 1:
        result = absorb_block(
            start_state, blocks[0, 0], blocks[0, 1], pos_blocks[0], query_rows, query_pos,
            first_valid,
        )
    else:

        def scan_step(state, block_item):
            kv_block, pos_block = block_item
            return (
                absorb_block(
                    state, kv_block[0], kv_block[1], pos_block, query_rows, query_pos,
                    first_valid,
                ),
                None,
            )

        result, _ = lax.scan(scan_step, start_state, (blocks, pos_blocks))
    run_max, run_sum, accumulated = result
    attended = (accumulated / run_sum[..., None]).astype(jnp.bfloat16)
    attended = attended.transpose(0, 3, 1, 2, 4).reshape(
        batch_count, tok_count, kv_local * group_size * HD
    )
    if out_w is None:
        return attended, key_t, value_t
    partial_value = jnp.einsum("bte,ed->btd", attended, out_w, preferred_element_type=jnp.float32)
    return partial_value.astype(jnp.bfloat16), key_t, value_t


def per_device(
    series, lengths, patch_weight, norm_gain, query_weight, key_weight, value_weight, out_weight,
    *, tm_n, mp_n, sec_n
):
    seq_count, channels, steps_dev = series.shape
    tok_count = steps_dev // STRIDE
    tm_at = lax.axis_index("tm")
    mp_at = lax.axis_index("mp")
    sec_at = lax.axis_index("section")
    feat_axes = ("mp", "section")
    feat_n = mp_n * sec_n
    to_second = [
        [(m * sec_n, ((m + by) % mp_n) * sec_n + 1) for m in range(mp_n)] for by in range(mp_n)
    ]
    moved_rows = [lax.ppermute(out_weight[0], feat_axes, pairs) for pairs in to_second]
    total_steps = steps_dev * tm_n
    total_tokens = tok_count * tm_n

    first_step = total_steps - lengths
    step_pos = tm_at * steps_dev + jnp.arange(steps_dev, dtype=jnp.int32)
    valid = (step_pos[None, :] >= first_step[:, None]).astype(jnp.float32)
    values = series.astype(jnp.float32)
    masked = values * valid[:, None, :]
    local_sum = jnp.sum(masked, -1)
    shard_lo = jnp.arange(tm_n, dtype=jnp.int32) * steps_dev
    counts = jnp.clip(
        shard_lo[None, :] + steps_dev - jnp.maximum(shard_lo[None, :], first_step[:, None]),
        0,
        steps_dev,
    ).astype(jnp.float32)
    my_count = jnp.sum(valid, -1)
    local_mean = local_sum / jnp.maximum(my_count, 1.0)[:, None]
    local_dev = (values - local_mean[..., None]) * valid[:, None, :]
    local_m2 = jnp.sum(local_dev * local_dev, -1)
    tail = series[:, :, steps_dev - STRIDE :]
    if tm_n > SMALL_GROUP:
        stats = lax.all_gather(jnp.stack([local_sum, local_m2], -1), "tm", axis=0)
        prior_raw = shift_from(tail, "tm", tm_n, 1, False).astype(jnp.float32)
    else:
        payload = jnp.concatenate(
            [jnp.stack([local_sum, local_m2], -1), tail.astype(jnp.float32)], -1
        )
        received = [payload] + [shift_from(payload, "tm", tm_n, by, True) for by in range(1, tm_n)]
        prior_raw = received[1][..., 2:] if tm_n > 1 else jnp.zeros_like(payload[..., 2:])
        order = (tm_at - jnp.arange(tm_n, dtype=jnp.int32)) % tm_n
        stats = jnp.take(jnp.stack([piece[..., :2] for piece in received], 0), order, axis=0)
    history = lengths.astype(jnp.float32)[:, None]
    shard_sums = stats[..., 0]
    shard_m2 = stats[..., 1]
    channel_mean = jnp.sum(shard_sums, 0) / history
    shard_counts = jnp.moveaxis(counts, 1, 0)[:, :, None]
    shard_means = shard_sums / jnp.maximum(shard_counts, 1.0)
    gap = shard_means - channel_mean[None]
    spread_total = jnp.sum(shard_m2 + shard_counts * gap * gap, 0)
    variance = spread_total / history
    inv_std = lax.rsqrt(variance + 1e-05)[..., None]

    padded = jnp.concatenate([prior_raw, series.astype(jnp.float32)], -1)
    padded_pos = tm_at * steps_dev - STRIDE + jnp.arange(steps_dev + STRIDE, dtype=jnp.int32)
    padded_valid = (
        (padded_pos[None, :] >= first_step[:, None]) & (padded_pos[None, :] >= 0)
    ).astype(jnp.float32)[:, None, :]
    normed = (
        (padded * padded_valid - channel_mean[..., None]) * padded_valid * inv_std
    ).astype(jnp.bfloat16)
    kernel = patch_weight.reshape(channels, 2 * STRIDE, patch_weight.shape[1])
    tokens = lax.conv_general_dilated(
        normed,
        kernel,
        window_strides=(STRIDE,),
        padding="VALID",
        dimension_numbers=("NCW", "IWO", "NWC"),
        preferred_element_type=jnp.float32,
    ).astype(jnp.bfloat16)
    column_count = patch_weight.shape[1]
    hidden0 = lax.all_gather(tokens, feat_axes, axis=2, tiled=True)
    feature_count = hidden0.shape[2]
    head_cols = feature_count // mp_n
    sizes = (tm_n, sec_n, tm_at, total_tokens)

    attended0, key0, value0 = attend_layer(
        hidden0, lengths, norm_gain[0], query_weight[0], key_weight[0], value_weight[0],
        None, sizes, 0,
    )
    head_sum = None
    for pairs, rows in zip(to_second, moved_rows):
        arrived = lax.ppermute(attended0, feat_axes, pairs)
        term = jnp.einsum("bte,ed->btd", arrived, rows, preferred_element_type=jnp.float32)
        head_sum = term if head_sum is None else head_sum + term
    hidden1 = (hidden0.astype(jnp.float32) + head_sum).astype(jnp.bfloat16)

    partial1, key1, value1 = attend_layer(
        hidden1, lengths, norm_gain[0], query_weight[0], key_weight[0], value_weight[0],
        out_weight[0], sizes, 1,
    )
    is_first = sec_at == 0
    key_store = jnp.where(is_first, key0, key1)[None]
    value_store = jnp.where(is_first, value0, value1)[None]

    per_section = seq_count // sec_n
    low_rows = partial1[:per_section]
    high_rows = partial1[per_section:]
    low_hidden = hidden1[:per_section]
    to_low = []
    to_high = []
    for by in range(mp_n):
        target_mp = (mp_at + by) % mp_n
        cols = lax.dynamic_slice_in_dim(low_rows, target_mp * head_cols, head_cols, 2)
        if by == 0:
            cols = jnp.stack(
                [lax.dynamic_slice_in_dim(low_hidden, target_mp * head_cols, head_cols, 2), cols], 0
            )
        pairs = [(m * sec_n + 1, ((m + by) % mp_n) * sec_n) for m in range(mp_n)]
        to_low.append(lax.ppermute(cols, feat_axes, pairs))
        if by > 0:
            cols_high = lax.dynamic_slice_in_dim(high_rows, target_mp * head_cols, head_cols, 2)
            pairs = [(m * sec_n + 1, ((m + by) % mp_n) * sec_n + 1) for m in range(mp_n)]
            to_high.append(lax.ppermute(cols_high, feat_axes, pairs))
    low_total = to_low[0][0].astype(jnp.float32) + (
        to_low[0][1].astype(jnp.float32)
        + sum(piece.astype(jnp.float32) for piece in to_low[1:])
    )
    own_high = lax.dynamic_slice_in_dim(high_rows, mp_at * head_cols, head_cols, 2)
    own_hidden = lax.dynamic_slice_in_dim(hidden1[per_section:], mp_at * head_cols, head_cols, 2)
    high_total = own_hidden.astype(jnp.float32) + (
        own_high.astype(jnp.float32) + sum(piece.astype(jnp.float32) for piece in to_high)
    )
    final_cols = jnp.where(is_first, low_total, high_total).astype(jnp.bfloat16)
    return (key_store, value_store, final_cols)


def solution(mesh):
    sizes = dict(tm_n=mesh.shape["tm"], mp_n=mesh.shape["mp"], sec_n=mesh.shape["section"])
    in_specs = (
        P("groups", None, "tm"),
        P("groups"),
        P(None, ("mp", "section")),
        P("section", None),
        P("section", None, "mp"),
        P("section", None, "mp"),
        P("section", None, "mp"),
        P("section", "mp", None),
    )
    out_specs = (
        P("section", "groups", "mp", None, "tm"),
        P("section", "groups", "mp", None, "tm"),
        P(("groups", "section"), "tm", "mp"),
    )

    def body(*args):
        return per_device(*args, **sizes)

    return jax.shard_map(body, mesh=mesh, in_specs=in_specs, out_specs=out_specs, check_vma=False)
```

```python
import jax
import jax.numpy as jnp
from jax import lax
from jax.sharding import PartitionSpec as P

STRIDE = 32
HD = 80
SMALL_GROUP = 4


def shift_from(value, axis, size, by, cyclic):
    pairs = [(i, (i + by) % size) for i in range(size) if cyclic or i + by < size]
    return lax.ppermute(value, axis, pairs)


def gather_ordered(value, axis, size, me):
    if size > SMALL_GROUP:
        return lax.all_gather(value, axis, axis=0)
    received = [value] + [shift_from(value, axis, size, by, True) for by in range(1, size)]
    stack = jnp.stack(received, 0)
    order = (me - jnp.arange(size, dtype=jnp.int32)) % size
    return jnp.take(stack, order, axis=0)


def gather_causal(value, tm_n, sec_n, tm_at, phase, width):
    if tm_n > SMALL_GROUP:
        gathered = lax.all_gather(value, "tm", axis=value.ndim - 1, tiled=True)
        return gathered, jnp.arange(tm_n * width, dtype=jnp.int32)
    pieces = []
    positions = []
    local = jnp.arange(width, dtype=jnp.int32)
    for by in range(tm_n - 1, 0, -1):
        pairs = [(t * sec_n + phase, (t + by) * sec_n + phase) for t in range(tm_n - by)]
        pieces.append(lax.ppermute(value, ("tm", "section"), pairs))
        positions.append((tm_at - by) * width + local)
    pieces.append(value)
    positions.append(tm_at * width + local)
    return jnp.concatenate(pieces, -1), jnp.concatenate(positions, 0)


def absorb_block(running, key_block, value_block, key_pos, query_rows, query_pos, first_valid):
    run_max, run_sum, accumulated = running
    allowed = (key_pos[None, None, :] <= query_pos[None, :, None]) & (
        (key_pos[None, None, :] >= first_valid[:, None, None])
        | (key_pos[None, None, :] == query_pos[None, :, None])
    )
    scores = jnp.einsum(
        "btkgh,bkhn->bkgtn", query_rows, key_block, preferred_element_type=jnp.float32
    )
    scores = jnp.where(allowed[:, None, None], scores, -jnp.inf)
    new_max = jnp.maximum(run_max, jnp.max(scores, -1))
    rescale = jnp.exp(run_max - new_max)
    exp_scores = jnp.exp(scores - new_max[..., None])
    new_sum = run_sum * rescale + jnp.sum(exp_scores, -1)
    contribution = jnp.einsum(
        "bkgtn,bkhn->bkgth",
        exp_scores.astype(jnp.bfloat16),
        value_block,
        preferred_element_type=jnp.float32,
    )
    return (new_max, new_sum, accumulated * rescale[..., None] + contribution)


def attend_layer(hidden_in, seq_lens, gain, query_w, key_w, value_w, out_w, sizes, phase):
    tm_n, sec_n, tm_at, total_tokens = sizes
    batch_count, tok_count, feature_count = hidden_in.shape
    hidden32 = hidden_in.astype(jnp.float32)
    gain32 = gain.astype(jnp.float32)
    scaled = hidden32 * lax.rsqrt(jnp.mean(hidden32 * hidden32, -1, keepdims=True) + 1e-06)
    layer_input = (scaled * gain32).astype(jnp.bfloat16)
    queries = (
        jnp.einsum("btd,de->bte", layer_input, query_w, preferred_element_type=jnp.float32)
        * HD ** (-0.5)
    ).astype(jnp.bfloat16)
    key_t = jnp.einsum(
        "btd,de->bet", layer_input, key_w, preferred_element_type=jnp.float32
    ).astype(jnp.bfloat16)
    value_t = jnp.einsum(
        "btd,de->bet", layer_input, value_w, preferred_element_type=jnp.float32
    ).astype(jnp.bfloat16)
    kv_local = key_w.shape[1] // HD
    group_size = query_w.shape[1] // key_w.shape[1]
    key_t = key_t.reshape(batch_count, kv_local, HD, tok_count)
    value_t = value_t.reshape(batch_count, kv_local, HD, tok_count)
    query_rows = queries.reshape(batch_count, tok_count, kv_local, group_size, HD)
    query_pos = tm_at * tok_count + jnp.arange(tok_count, dtype=jnp.int32)
    first_valid = total_tokens - seq_lens // STRIDE
    both, key_pos = gather_causal(
        jnp.stack([key_t, value_t], 0), tm_n, sec_n, tm_at, phase, tok_count
    )
    key_count = both.shape[-1]
    block_width = 1024 if key_count % 1024 == 0 else key_count
    rounds = key_count // block_width
    blocks = jnp.moveaxis(
        both.reshape(2, batch_count, kv_local, HD, rounds, block_width), 4, 0
    )
    pos_blocks = key_pos.reshape(rounds, block_width)
    start_state = (
        jnp.full((batch_count, kv_local, group_size, tok_count), -1e30, jnp.float32),
        jnp.zeros((batch_count, kv_local, group_size, tok_count), jnp.float32),
        jnp.zeros((batch_count, kv_local, group_size, tok_count, HD), jnp.float32),
    )
    if rounds == 1:
        result = absorb_block(
            start_state, blocks[0, 0], blocks[0, 1], pos_blocks[0], query_rows, query_pos,
            first_valid,
        )
    else:

        def scan_step(state, block_item):
            kv_block, pos_block = block_item
            return (
                absorb_block(
                    state, kv_block[0], kv_block[1], pos_block, query_rows, query_pos,
                    first_valid,
                ),
                None,
            )

        result, _ = lax.scan(scan_step, start_state, (blocks, pos_blocks))
    run_max, run_sum, accumulated = result
    attended = (accumulated / run_sum[..., None]).astype(jnp.bfloat16)
    attended = attended.transpose(0, 3, 1, 2, 4).reshape(
        batch_count, tok_count, kv_local * group_size * HD
    )
    if out_w is None:
        return attended, key_t, value_t
    partial_value = jnp.einsum("bte,ed->btd", attended, out_w, preferred_element_type=jnp.float32)
    return partial_value.astype(jnp.bfloat16), key_t, value_t


def per_device(
    series, lengths, patch_weight, norm_gain, query_weight, key_weight, value_weight, out_weight,
    *, tm_n, mp_n, sec_n
):
    seq_count, channels, steps_dev = series.shape
    tok_count = steps_dev // STRIDE
    tm_at = lax.axis_index("tm")
    mp_at = lax.axis_index("mp")
    sec_at = lax.axis_index("section")
    feat_axes = ("mp", "section")
    feat_n = mp_n * sec_n
    to_second = [
        [(m * sec_n, ((m + by) % mp_n) * sec_n + 1) for m in range(mp_n)] for by in range(mp_n)
    ]
    moved_rows = [lax.ppermute(out_weight[0], feat_axes, pairs) for pairs in to_second]
    total_steps = steps_dev * tm_n
    total_tokens = tok_count * tm_n

    first_step = total_steps - lengths
    step_pos = tm_at * steps_dev + jnp.arange(steps_dev, dtype=jnp.int32)
    valid = (step_pos[None, :] >= first_step[:, None]).astype(jnp.float32)
    values = series.astype(jnp.float32)
    masked = values * valid[:, None, :]
    local_sum = jnp.sum(masked, -1)
    shard_lo = jnp.arange(tm_n, dtype=jnp.int32) * steps_dev
    counts = jnp.clip(
        shard_lo[None, :] + steps_dev - jnp.maximum(shard_lo[None, :], first_step[:, None]),
        0,
        steps_dev,
    ).astype(jnp.float32)
    my_count = jnp.sum(valid, -1)
    local_mean = local_sum / jnp.maximum(my_count, 1.0)[:, None]
    local_dev = (values - local_mean[..., None]) * valid[:, None, :]
    local_m2 = jnp.sum(local_dev * local_dev, -1)
    tail = series[:, :, steps_dev - STRIDE :]
    if tm_n > SMALL_GROUP:
        stats = lax.all_gather(jnp.stack([local_sum, local_m2], -1), "tm", axis=0)
        prior_raw = shift_from(tail, "tm", tm_n, 1, False).astype(jnp.float32)
    else:
        payload = jnp.concatenate(
            [jnp.stack([local_sum, local_m2], -1), tail.astype(jnp.float32)], -1
        )
        received = [payload] + [shift_from(payload, "tm", tm_n, by, True) for by in range(1, tm_n)]
        prior_raw = received[1][..., 2:] if tm_n > 1 else jnp.zeros_like(payload[..., 2:])
        order = (tm_at - jnp.arange(tm_n, dtype=jnp.int32)) % tm_n
        stats = jnp.take(jnp.stack([piece[..., :2] for piece in received], 0), order, axis=0)
    history = lengths.astype(jnp.float32)[:, None]
    shard_sums = stats[..., 0]
    shard_m2 = stats[..., 1]
    channel_mean = jnp.sum(shard_sums, 0) / history
    shard_counts = jnp.moveaxis(counts, 1, 0)[:, :, None]
    shard_means = shard_sums / jnp.maximum(shard_counts, 1.0)
    gap = shard_means - channel_mean[None]
    spread_total = jnp.sum(shard_m2 + shard_counts * gap * gap, 0)
    variance = spread_total / history
    inv_std = lax.rsqrt(variance + 1e-05)[..., None]

    raw_blocks = jnp.swapaxes(series.reshape(seq_count, channels, tok_count, STRIDE), 2, 3)
    block_pos = (
        tm_at * steps_dev
        + jnp.arange(tok_count, dtype=jnp.int32)[None, :] * STRIDE
        + jnp.arange(STRIDE, dtype=jnp.int32)[:, None]
    )
    block_valid = (block_pos[None] >= first_step[:, None, None]).astype(jnp.float32)[:, None]
    normed = (
        (raw_blocks.astype(jnp.float32) * block_valid - channel_mean[..., None, None])
        * block_valid
        * inv_std[..., None]
    ).astype(jnp.bfloat16)
    prior_pos = tm_at * steps_dev - STRIDE + jnp.arange(STRIDE, dtype=jnp.int32)
    prior_valid = ((prior_pos[None, :] >= first_step[:, None]) & (prior_pos[None, :] >= 0)).astype(
        jnp.float32
    )[:, None, :]
    prior_normed = (
        (prior_raw * prior_valid - channel_mean[..., None]) * prior_valid * inv_std
    ).astype(jnp.bfloat16)
    column_count = patch_weight.shape[1]
    halves = patch_weight.T.reshape(column_count, channels, 2, STRIDE)
    flat = normed.reshape(seq_count, channels * STRIDE, tok_count)
    left_w = halves[:, :, 0].reshape(column_count, channels * STRIDE)
    right_w = halves[:, :, 1].reshape(column_count, channels * STRIDE)
    right_terms = jnp.einsum("dk,skj->sdj", right_w, flat, preferred_element_type=jnp.float32)
    left_all = jnp.einsum("dk,skj->sdj", left_w, flat, preferred_element_type=jnp.float32)
    edge_term = jnp.einsum(
        "dk,sk->sd", left_w, prior_normed.reshape(seq_count, channels * STRIDE),
        preferred_element_type=jnp.float32,
    )
    left_terms = jnp.concatenate([edge_term[:, :, None], left_all[:, :, : tok_count - 1]], 2)
    tokens = jnp.swapaxes((left_terms + right_terms).astype(jnp.bfloat16), 1, 2)
    hidden0 = lax.all_gather(tokens, feat_axes, axis=2, tiled=True)
    feature_count = hidden0.shape[2]
    head_cols = feature_count // mp_n
    sizes = (tm_n, sec_n, tm_at, total_tokens)

    attended0, key0, value0 = attend_layer(
        hidden0, lengths, norm_gain[0], query_weight[0], key_weight[0], value_weight[0],
        None, sizes, 0,
    )
    head_sum = None
    for pairs, rows in zip(to_second, moved_rows):
        arrived = lax.ppermute(attended0, feat_axes, pairs)
        term = jnp.einsum("bte,ed->btd", arrived, rows, preferred_element_type=jnp.float32)
        head_sum = term if head_sum is None else head_sum + term
    hidden1 = (hidden0.astype(jnp.float32) + head_sum).astype(jnp.bfloat16)

    partial1, key1, value1 = attend_layer(
        hidden1, lengths, norm_gain[0], query_weight[0], key_weight[0], value_weight[0],
        out_weight[0], sizes, 1,
    )
    is_first = sec_at == 0
    key_store = jnp.where(is_first, key0, key1)[None]
    value_store = jnp.where(is_first, value0, value1)[None]

    per_section = seq_count // sec_n
    low_rows = partial1[:per_section]
    high_rows = partial1[per_section:]
    low_hidden = hidden1[:per_section]
    to_low = []
    to_high = []
    for by in range(mp_n):
        target_mp = (mp_at + by) % mp_n
        cols = lax.dynamic_slice_in_dim(low_rows, target_mp * head_cols, head_cols, 2)
        if by == 0:
            cols = jnp.stack(
                [lax.dynamic_slice_in_dim(low_hidden, target_mp * head_cols, head_cols, 2), cols], 0
            )
        pairs = [(m * sec_n + 1, ((m + by) % mp_n) * sec_n) for m in range(mp_n)]
        to_low.append(lax.ppermute(cols, feat_axes, pairs))
        if by > 0:
            cols_high = lax.dynamic_slice_in_dim(high_rows, target_mp * head_cols, head_cols, 2)
            pairs = [(m * sec_n + 1, ((m + by) % mp_n) * sec_n + 1) for m in range(mp_n)]
            to_high.append(lax.ppermute(cols_high, feat_axes, pairs))
    low_total = to_low[0][0].astype(jnp.float32) + (
        to_low[0][1].astype(jnp.float32)
        + sum(piece.astype(jnp.float32) for piece in to_low[1:])
    )
    own_high = lax.dynamic_slice_in_dim(high_rows, mp_at * head_cols, head_cols, 2)
    own_hidden = lax.dynamic_slice_in_dim(hidden1[per_section:], mp_at * head_cols, head_cols, 2)
    high_total = own_hidden.astype(jnp.float32) + (
        own_high.astype(jnp.float32) + sum(piece.astype(jnp.float32) for piece in to_high)
    )
    final_cols = jnp.where(is_first, low_total, high_total).astype(jnp.bfloat16)
    return (key_store, value_store, final_cols)


def solution(mesh):
    sizes = dict(tm_n=mesh.shape["tm"], mp_n=mesh.shape["mp"], sec_n=mesh.shape["section"])
    in_specs = (
        P("groups", None, "tm"),
        P("groups"),
        P(None, ("mp", "section")),
        P("section", None),
        P("section", None, "mp"),
        P("section", None, "mp"),
        P("section", None, "mp"),
        P("section", "mp", None),
    )
    out_specs = (
        P("section", "groups", "mp", None, "tm"),
        P("section", "groups", "mp", None, "tm"),
        P(("groups", "section"), "tm", "mp"),
    )

    def body(*args):
        return per_device(*args, **sizes)

    return jax.shard_map(body, mesh=mesh, in_specs=in_specs, out_specs=out_specs, check_vma=False)
```

```python
import jax
import jax.numpy as jnp
from jax import lax
from jax.sharding import PartitionSpec as P

STRIDE = 32
HD = 80
SMALL_GROUP = 4


def shift_from(value, axis, size, by, cyclic):
    pairs = [(i, (i + by) % size) for i in range(size) if cyclic or i + by < size]
    return lax.ppermute(value, axis, pairs)


def gather_ordered(value, axis, size, me):
    if size > SMALL_GROUP:
        return lax.all_gather(value, axis, axis=0)
    received = [value] + [shift_from(value, axis, size, by, True) for by in range(1, size)]
    stack = jnp.stack(received, 0)
    order = (me - jnp.arange(size, dtype=jnp.int32)) % size
    return jnp.take(stack, order, axis=0)


def gather_causal(value, tm_n, sec_n, tm_at, phase, width):
    if tm_n > SMALL_GROUP:
        gathered = lax.all_gather(value, "tm", axis=value.ndim - 1, tiled=True)
        return gathered, jnp.arange(tm_n * width, dtype=jnp.int32)
    pieces = []
    positions = []
    local = jnp.arange(width, dtype=jnp.int32)
    for by in range(tm_n - 1, 0, -1):
        pairs = [(t * sec_n + phase, (t + by) * sec_n + phase) for t in range(tm_n - by)]
        pieces.append(lax.ppermute(value, ("tm", "section"), pairs))
        positions.append((tm_at - by) * width + local)
    pieces.append(value)
    positions.append(tm_at * width + local)
    return jnp.concatenate(pieces, -1), jnp.concatenate(positions, 0)


def absorb_block(running, key_block, value_block, key_pos, query_rows, query_pos, first_valid):
    run_max, run_sum, accumulated = running
    allowed = (key_pos[None, None, :] <= query_pos[None, :, None]) & (
        (key_pos[None, None, :] >= first_valid[:, None, None])
        | (key_pos[None, None, :] == query_pos[None, :, None])
    )
    scores = jnp.einsum(
        "btkgh,bkhn->bkgtn", query_rows, key_block, preferred_element_type=jnp.float32
    )
    scores = jnp.where(allowed[:, None, None], scores, -jnp.inf)
    new_max = jnp.maximum(run_max, jnp.max(scores, -1))
    rescale = jnp.exp(run_max - new_max)
    exp_scores = jnp.exp(scores - new_max[..., None])
    new_sum = run_sum * rescale + jnp.sum(exp_scores, -1)
    contribution = jnp.einsum(
        "bkgtn,bkhn->bkgth",
        exp_scores.astype(jnp.bfloat16),
        value_block,
        preferred_element_type=jnp.float32,
    )
    return (new_max, new_sum, accumulated * rescale[..., None] + contribution)


def attend_layer(hidden_in, seq_lens, gain, query_w, key_w, value_w, out_w, sizes, phase):
    tm_n, sec_n, tm_at, total_tokens = sizes
    batch_count, tok_count, feature_count = hidden_in.shape
    hidden32 = hidden_in.astype(jnp.float32)
    gain32 = gain.astype(jnp.float32)
    scaled = hidden32 * lax.rsqrt(jnp.mean(hidden32 * hidden32, -1, keepdims=True) + 1e-06)
    layer_input = (scaled * gain32).astype(jnp.bfloat16)
    queries = (
        jnp.einsum("btd,de->bte", layer_input, query_w, preferred_element_type=jnp.float32)
        * HD ** (-0.5)
    ).astype(jnp.bfloat16)
    key_t = jnp.einsum(
        "btd,de->bet", layer_input, key_w, preferred_element_type=jnp.float32
    ).astype(jnp.bfloat16)
    value_t = jnp.einsum(
        "btd,de->bet", layer_input, value_w, preferred_element_type=jnp.float32
    ).astype(jnp.bfloat16)
    kv_local = key_w.shape[1] // HD
    group_size = query_w.shape[1] // key_w.shape[1]
    key_t = key_t.reshape(batch_count, kv_local, HD, tok_count)
    value_t = value_t.reshape(batch_count, kv_local, HD, tok_count)
    query_rows = queries.reshape(batch_count, tok_count, kv_local, group_size, HD)
    query_pos = tm_at * tok_count + jnp.arange(tok_count, dtype=jnp.int32)
    first_valid = total_tokens - seq_lens // STRIDE
    both, key_pos = gather_causal(
        jnp.stack([key_t, value_t], 0), tm_n, sec_n, tm_at, phase, tok_count
    )
    key_count = both.shape[-1]
    block_width = 1024 if key_count % 1024 == 0 else key_count
    rounds = key_count // block_width
    blocks = jnp.moveaxis(
        both.reshape(2, batch_count, kv_local, HD, rounds, block_width), 4, 0
    )
    pos_blocks = key_pos.reshape(rounds, block_width)
    start_state = (
        jnp.full((batch_count, kv_local, group_size, tok_count), -1e30, jnp.float32),
        jnp.zeros((batch_count, kv_local, group_size, tok_count), jnp.float32),
        jnp.zeros((batch_count, kv_local, group_size, tok_count, HD), jnp.float32),
    )
    if rounds == 1:
        result = absorb_block(
            start_state, blocks[0, 0], blocks[0, 1], pos_blocks[0], query_rows, query_pos,
            first_valid,
        )
    else:

        def scan_step(state, block_item):
            kv_block, pos_block = block_item
            return (
                absorb_block(
                    state, kv_block[0], kv_block[1], pos_block, query_rows, query_pos,
                    first_valid,
                ),
                None,
            )

        result, _ = lax.scan(scan_step, start_state, (blocks, pos_blocks))
    run_max, run_sum, accumulated = result
    attended = (accumulated / run_sum[..., None]).astype(jnp.bfloat16)
    attended = attended.transpose(0, 3, 1, 2, 4).reshape(
        batch_count, tok_count, kv_local * group_size * HD
    )
    if out_w is None:
        return attended, key_t, value_t
    partial_value = jnp.einsum("bte,ed->btd", attended, out_w, preferred_element_type=jnp.float32)
    return partial_value.astype(jnp.bfloat16), key_t, value_t


def per_device(
    series, lengths, patch_weight, norm_gain, query_weight, key_weight, value_weight, out_weight,
    *, tm_n, mp_n, sec_n
):
    seq_count, channels, steps_dev = series.shape
    tok_count = steps_dev // STRIDE
    tm_at = lax.axis_index("tm")
    mp_at = lax.axis_index("mp")
    sec_at = lax.axis_index("section")
    feat_axes = ("mp", "section")
    feat_n = mp_n * sec_n
    to_second = [
        [(m * sec_n, ((m + by) % mp_n) * sec_n + 1) for m in range(mp_n)] for by in range(mp_n)
    ]
    moved_rows = [lax.ppermute(out_weight[0], feat_axes, pairs) for pairs in to_second]
    total_steps = steps_dev * tm_n
    total_tokens = tok_count * tm_n

    first_step = total_steps - lengths
    step_pos = tm_at * steps_dev + jnp.arange(steps_dev, dtype=jnp.int32)
    valid = (step_pos[None, :] >= first_step[:, None]).astype(jnp.float32)
    values = series.astype(jnp.float32)
    masked = values * valid[:, None, :]
    local_sum = jnp.sum(masked, -1)
    shard_lo = jnp.arange(tm_n, dtype=jnp.int32) * steps_dev
    counts = jnp.clip(
        shard_lo[None, :] + steps_dev - jnp.maximum(shard_lo[None, :], first_step[:, None]),
        0,
        steps_dev,
    ).astype(jnp.float32)
    my_count = jnp.sum(valid, -1)
    local_mean = local_sum / jnp.maximum(my_count, 1.0)[:, None]
    local_dev = (values - local_mean[..., None]) * valid[:, None, :]
    local_m2 = jnp.sum(local_dev * local_dev, -1)
    tail = series[:, :, steps_dev - STRIDE :]
    payload = jnp.concatenate([jnp.stack([local_sum, local_m2], -1), tail.astype(jnp.float32)], -1)
    gathered = lax.all_gather(payload, "tm", axis=0)
    stats = gathered[..., :2]
    prior_raw = jnp.take(gathered, (tm_at + tm_n - 1) % tm_n, axis=0)[..., 2:]
    history = lengths.astype(jnp.float32)[:, None]
    shard_sums = stats[..., 0]
    shard_m2 = stats[..., 1]
    channel_mean = jnp.sum(shard_sums, 0) / history
    shard_counts = jnp.moveaxis(counts, 1, 0)[:, :, None]
    shard_means = shard_sums / jnp.maximum(shard_counts, 1.0)
    gap = shard_means - channel_mean[None]
    spread_total = jnp.sum(shard_m2 + shard_counts * gap * gap, 0)
    variance = spread_total / history
    inv_std = lax.rsqrt(variance + 1e-05)[..., None]

    padded = jnp.concatenate([prior_raw, series.astype(jnp.float32)], -1)
    padded_pos = tm_at * steps_dev - STRIDE + jnp.arange(steps_dev + STRIDE, dtype=jnp.int32)
    padded_valid = (
        (padded_pos[None, :] >= first_step[:, None]) & (padded_pos[None, :] >= 0)
    ).astype(jnp.float32)[:, None, :]
    normed = (
        (padded * padded_valid - channel_mean[..., None]) * padded_valid * inv_std
    ).astype(jnp.bfloat16)
    kernel = patch_weight.reshape(channels, 2 * STRIDE, patch_weight.shape[1])
    tokens = lax.conv_general_dilated(
        normed,
        kernel,
        window_strides=(STRIDE,),
        padding="VALID",
        dimension_numbers=("NCW", "IWO", "NWC"),
        preferred_element_type=jnp.float32,
    ).astype(jnp.bfloat16)
    column_count = patch_weight.shape[1]
    hidden0 = lax.all_gather(tokens, feat_axes, axis=2, tiled=True)
    feature_count = hidden0.shape[2]
    head_cols = feature_count // mp_n
    sizes = (tm_n, sec_n, tm_at, total_tokens)

    attended0, key0, value0 = attend_layer(
        hidden0, lengths, norm_gain[0], query_weight[0], key_weight[0], value_weight[0],
        None, sizes, 0,
    )
    head_sum = None
    for pairs, rows in zip(to_second, moved_rows):
        arrived = lax.ppermute(attended0, feat_axes, pairs)
        term = jnp.einsum("bte,ed->btd", arrived, rows, preferred_element_type=jnp.float32)
        head_sum = term if head_sum is None else head_sum + term
    hidden1 = (hidden0.astype(jnp.float32) + head_sum).astype(jnp.bfloat16)

    partial1, key1, value1 = attend_layer(
        hidden1, lengths, norm_gain[0], query_weight[0], key_weight[0], value_weight[0],
        out_weight[0], sizes, 1,
    )
    is_first = sec_at == 0
    key_store = jnp.where(is_first, key0, key1)[None]
    value_store = jnp.where(is_first, value0, value1)[None]

    per_section = seq_count // sec_n
    low_rows = partial1[:per_section]
    high_rows = partial1[per_section:]
    low_hidden = hidden1[:per_section]
    to_low = []
    to_high = []
    for by in range(mp_n):
        target_mp = (mp_at + by) % mp_n
        cols = lax.dynamic_slice_in_dim(low_rows, target_mp * head_cols, head_cols, 2)
        if by == 0:
            cols = jnp.stack(
                [lax.dynamic_slice_in_dim(low_hidden, target_mp * head_cols, head_cols, 2), cols], 0
            )
        pairs = [(m * sec_n + 1, ((m + by) % mp_n) * sec_n) for m in range(mp_n)]
        to_low.append(lax.ppermute(cols, feat_axes, pairs))
        if by > 0:
            cols_high = lax.dynamic_slice_in_dim(high_rows, target_mp * head_cols, head_cols, 2)
            pairs = [(m * sec_n + 1, ((m + by) % mp_n) * sec_n + 1) for m in range(mp_n)]
            to_high.append(lax.ppermute(cols_high, feat_axes, pairs))
    low_total = to_low[0][0].astype(jnp.float32) + (
        to_low[0][1].astype(jnp.float32)
        + sum(piece.astype(jnp.float32) for piece in to_low[1:])
    )
    own_high = lax.dynamic_slice_in_dim(high_rows, mp_at * head_cols, head_cols, 2)
    own_hidden = lax.dynamic_slice_in_dim(hidden1[per_section:], mp_at * head_cols, head_cols, 2)
    high_total = own_hidden.astype(jnp.float32) + (
        own_high.astype(jnp.float32) + sum(piece.astype(jnp.float32) for piece in to_high)
    )
    final_cols = jnp.where(is_first, low_total, high_total).astype(jnp.bfloat16)
    return (key_store, value_store, final_cols)


def solution(mesh):
    sizes = dict(tm_n=mesh.shape["tm"], mp_n=mesh.shape["mp"], sec_n=mesh.shape["section"])
    in_specs = (
        P("groups", None, "tm"),
        P("groups"),
        P(None, ("mp", "section")),
        P("section", None),
        P("section", None, "mp"),
        P("section", None, "mp"),
        P("section", None, "mp"),
        P("section", "mp", None),
    )
    out_specs = (
        P("section", "groups", "mp", None, "tm"),
        P("section", "groups", "mp", None, "tm"),
        P(("groups", "section"), "tm", "mp"),
    )

    def body(*args):
        return per_device(*args, **sizes)

    return jax.shard_map(body, mesh=mesh, in_specs=in_specs, out_specs=out_specs, check_vma=False)
```

```python
import jax
import jax.numpy as jnp
from jax import lax
from jax.sharding import PartitionSpec as P

STRIDE = 32
HD = 80
SMALL_GROUP = 4


def shift_from(value, axis, size, by, cyclic):
    pairs = [(i, (i + by) % size) for i in range(size) if cyclic or i + by < size]
    return lax.ppermute(value, axis, pairs)


def gather_ordered(value, axis, size, me):
    if size > SMALL_GROUP:
        return lax.all_gather(value, axis, axis=0)
    received = [value] + [shift_from(value, axis, size, by, True) for by in range(1, size)]
    stack = jnp.stack(received, 0)
    order = (me - jnp.arange(size, dtype=jnp.int32)) % size
    return jnp.take(stack, order, axis=0)


def gather_causal(value, tm_n, sec_n, tm_at, phase, width):
    if tm_n > SMALL_GROUP:
        gathered = lax.all_gather(value, "tm", axis=value.ndim - 1, tiled=True)
        return gathered, jnp.arange(tm_n * width, dtype=jnp.int32)
    pieces = []
    positions = []
    local = jnp.arange(width, dtype=jnp.int32)
    for by in range(tm_n - 1, 0, -1):
        pairs = [(t * sec_n + phase, (t + by) * sec_n + phase) for t in range(tm_n - by)]
        pieces.append(lax.ppermute(value, ("tm", "section"), pairs))
        positions.append((tm_at - by) * width + local)
    pieces.append(value)
    positions.append(tm_at * width + local)
    return jnp.concatenate(pieces, -1), jnp.concatenate(positions, 0)


def absorb_block(running, key_block, value_block, key_pos, query_rows, query_pos, first_valid):
    run_max, run_sum, accumulated = running
    allowed = (key_pos[None, None, :] <= query_pos[None, :, None]) & (
        (key_pos[None, None, :] >= first_valid[:, None, None])
        | (key_pos[None, None, :] == query_pos[None, :, None])
    )
    scores = jnp.einsum(
        "btkgh,bkhn->bkgtn", query_rows, key_block, preferred_element_type=jnp.float32
    )
    scores = jnp.where(allowed[:, None, None], scores, -jnp.inf)
    new_max = jnp.maximum(run_max, jnp.max(scores, -1))
    rescale = jnp.exp(run_max - new_max)
    exp_scores = jnp.exp(scores - new_max[..., None])
    new_sum = run_sum * rescale + jnp.sum(exp_scores, -1)
    contribution = jnp.einsum(
        "bkgtn,bkhn->bkgth",
        exp_scores.astype(jnp.bfloat16),
        value_block,
        preferred_element_type=jnp.float32,
    )
    return (new_max, new_sum, accumulated * rescale[..., None] + contribution)


def attend_layer(hidden_in, seq_lens, gain, query_w, key_w, value_w, out_w, sizes, phase):
    tm_n, sec_n, tm_at, total_tokens = sizes
    batch_count, tok_count, feature_count = hidden_in.shape
    hidden32 = hidden_in.astype(jnp.float32)
    gain32 = gain.astype(jnp.float32)
    scaled = hidden32 * lax.rsqrt(jnp.mean(hidden32 * hidden32, -1, keepdims=True) + 1e-06)
    layer_input = (scaled * gain32).astype(jnp.bfloat16)
    queries = (
        jnp.einsum("btd,de->bte", layer_input, query_w, preferred_element_type=jnp.float32)
        * HD ** (-0.5)
    ).astype(jnp.bfloat16)
    key_t = jnp.einsum(
        "btd,de->bet", layer_input, key_w, preferred_element_type=jnp.float32
    ).astype(jnp.bfloat16)
    value_t = jnp.einsum(
        "btd,de->bet", layer_input, value_w, preferred_element_type=jnp.float32
    ).astype(jnp.bfloat16)
    kv_local = key_w.shape[1] // HD
    group_size = query_w.shape[1] // key_w.shape[1]
    key_t = key_t.reshape(batch_count, kv_local, HD, tok_count)
    value_t = value_t.reshape(batch_count, kv_local, HD, tok_count)
    query_rows = queries.reshape(batch_count, tok_count, kv_local, group_size, HD)
    query_pos = tm_at * tok_count + jnp.arange(tok_count, dtype=jnp.int32)
    first_valid = total_tokens - seq_lens // STRIDE
    both, key_pos = gather_causal(
        jnp.stack([key_t, value_t], 0), tm_n, sec_n, tm_at, phase, tok_count
    )
    key_count = both.shape[-1]
    block_width = 1024 if key_count % 1024 == 0 else key_count
    rounds = key_count // block_width
    blocks = jnp.moveaxis(
        both.reshape(2, batch_count, kv_local, HD, rounds, block_width), 4, 0
    )
    pos_blocks = key_pos.reshape(rounds, block_width)
    start_state = (
        jnp.full((batch_count, kv_local, group_size, tok_count), -1e30, jnp.float32),
        jnp.zeros((batch_count, kv_local, group_size, tok_count), jnp.float32),
        jnp.zeros((batch_count, kv_local, group_size, tok_count, HD), jnp.float32),
    )
    if rounds == 1:
        result = absorb_block(
            start_state, blocks[0, 0], blocks[0, 1], pos_blocks[0], query_rows, query_pos,
            first_valid,
        )
    else:

        def scan_step(state, block_item):
            kv_block, pos_block = block_item
            return (
                absorb_block(
                    state, kv_block[0], kv_block[1], pos_block, query_rows, query_pos,
                    first_valid,
                ),
                None,
            )

        result, _ = lax.scan(scan_step, start_state, (blocks, pos_blocks))
    run_max, run_sum, accumulated = result
    attended = (accumulated / run_sum[..., None]).astype(jnp.bfloat16)
    attended = attended.transpose(0, 3, 1, 2, 4).reshape(
        batch_count, tok_count, kv_local * group_size * HD
    )
    if out_w is None:
        return attended, key_t, value_t
    partial_value = jnp.einsum("bte,ed->btd", attended, out_w, preferred_element_type=jnp.float32)
    return partial_value.astype(jnp.bfloat16), key_t, value_t


def per_device(
    series, lengths, patch_weight, norm_gain, query_weight, key_weight, value_weight, out_weight,
    *, tm_n, mp_n, sec_n
):
    seq_count, channels, steps_dev = series.shape
    tok_count = steps_dev // STRIDE
    tm_at = lax.axis_index("tm")
    mp_at = lax.axis_index("mp")
    sec_at = lax.axis_index("section")
    feat_axes = ("mp", "section")
    feat_n = mp_n * sec_n
    to_second = [
        [(m * sec_n, ((m + by) % mp_n) * sec_n + 1) for m in range(mp_n)] for by in range(mp_n)
    ]
    moved_rows = [lax.ppermute(out_weight[0], feat_axes, pairs) for pairs in to_second]
    total_steps = steps_dev * tm_n
    total_tokens = tok_count * tm_n

    first_step = total_steps - lengths
    step_pos = tm_at * steps_dev + jnp.arange(steps_dev, dtype=jnp.int32)
    valid = (step_pos[None, :] >= first_step[:, None]).astype(jnp.float32)
    values = series.astype(jnp.float32)
    masked = values * valid[:, None, :]
    local_sum = jnp.sum(masked, -1)
    shard_lo = jnp.arange(tm_n, dtype=jnp.int32) * steps_dev
    counts = jnp.clip(
        shard_lo[None, :] + steps_dev - jnp.maximum(shard_lo[None, :], first_step[:, None]),
        0,
        steps_dev,
    ).astype(jnp.float32)
    my_count = jnp.sum(valid, -1)
    local_mean = local_sum / jnp.maximum(my_count, 1.0)[:, None]
    local_dev = (values - local_mean[..., None]) * valid[:, None, :]
    local_m2 = jnp.sum(local_dev * local_dev, -1)
    tail = series[:, :, steps_dev - STRIDE :]
    if tm_n > SMALL_GROUP:
        stats = lax.all_gather(jnp.stack([local_sum, local_m2], -1), "tm", axis=0)
        prior_raw = shift_from(tail, "tm", tm_n, 1, False).astype(jnp.float32)
    else:
        payload = jnp.concatenate(
            [jnp.stack([local_sum, local_m2], -1), tail.astype(jnp.float32)], -1
        )
        received = [payload] + [shift_from(payload, "tm", tm_n, by, True) for by in range(1, tm_n)]
        prior_raw = received[1][..., 2:] if tm_n > 1 else jnp.zeros_like(payload[..., 2:])
        order = (tm_at - jnp.arange(tm_n, dtype=jnp.int32)) % tm_n
        stats = jnp.take(jnp.stack([piece[..., :2] for piece in received], 0), order, axis=0)
    history = lengths.astype(jnp.float32)[:, None]
    shard_sums = stats[..., 0]
    shard_m2 = stats[..., 1]
    channel_mean = jnp.sum(shard_sums, 0) / history
    shard_counts = jnp.moveaxis(counts, 1, 0)[:, :, None]
    shard_means = shard_sums / jnp.maximum(shard_counts, 1.0)
    gap = shard_means - channel_mean[None]
    spread_total = jnp.sum(shard_m2 + shard_counts * gap * gap, 0)
    variance = spread_total / history
    inv_std = lax.rsqrt(variance + 1e-05)[..., None]

    padded = jnp.concatenate([prior_raw, series.astype(jnp.float32)], -1)
    padded_pos = tm_at * steps_dev - STRIDE + jnp.arange(steps_dev + STRIDE, dtype=jnp.int32)
    padded_valid = (
        (padded_pos[None, :] >= first_step[:, None]) & (padded_pos[None, :] >= 0)
    ).astype(jnp.float32)[:, None, :]
    normed = (
        (padded * padded_valid - channel_mean[..., None]) * padded_valid * inv_std
    ).astype(jnp.bfloat16)
    kernel = patch_weight.reshape(channels, 2 * STRIDE, patch_weight.shape[1])
    chunk_tok = 16 if tok_count % 16 == 0 else tok_count
    chunk_count = tok_count // chunk_tok
    chunks = jnp.stack(
        [
            normed[:, :, q * chunk_tok * STRIDE : (q + 1) * chunk_tok * STRIDE + STRIDE]
            for q in range(chunk_count)
        ],
        1,
    ).reshape(seq_count * chunk_count, channels, chunk_tok * STRIDE + STRIDE)
    tokens = lax.conv_general_dilated(
        chunks,
        kernel,
        window_strides=(STRIDE,),
        padding="VALID",
        dimension_numbers=("NCW", "IWO", "NWC"),
        preferred_element_type=jnp.float32,
    ).astype(jnp.bfloat16)
    tokens = tokens.reshape(seq_count, tok_count, tokens.shape[2])
    column_count = patch_weight.shape[1]
    hidden0 = lax.all_gather(tokens, feat_axes, axis=2, tiled=True)
    feature_count = hidden0.shape[2]
    head_cols = feature_count // mp_n
    sizes = (tm_n, sec_n, tm_at, total_tokens)

    attended0, key0, value0 = attend_layer(
        hidden0, lengths, norm_gain[0], query_weight[0], key_weight[0], value_weight[0],
        None, sizes, 0,
    )
    head_sum = None
    for pairs, rows in zip(to_second, moved_rows):
        arrived = lax.ppermute(attended0, feat_axes, pairs)
        term = jnp.einsum("bte,ed->btd", arrived, rows, preferred_element_type=jnp.float32)
        head_sum = term if head_sum is None else head_sum + term
    hidden1 = (hidden0.astype(jnp.float32) + head_sum).astype(jnp.bfloat16)

    partial1, key1, value1 = attend_layer(
        hidden1, lengths, norm_gain[0], query_weight[0], key_weight[0], value_weight[0],
        out_weight[0], sizes, 1,
    )
    is_first = sec_at == 0
    key_store = jnp.where(is_first, key0, key1)[None]
    value_store = jnp.where(is_first, value0, value1)[None]

    per_section = seq_count // sec_n
    low_rows = partial1[:per_section]
    high_rows = partial1[per_section:]
    low_hidden = hidden1[:per_section]
    to_low = []
    to_high = []
    for by in range(mp_n):
        target_mp = (mp_at + by) % mp_n
        cols = lax.dynamic_slice_in_dim(low_rows, target_mp * head_cols, head_cols, 2)
        if by == 0:
            cols = jnp.stack(
                [lax.dynamic_slice_in_dim(low_hidden, target_mp * head_cols, head_cols, 2), cols], 0
            )
        pairs = [(m * sec_n + 1, ((m + by) % mp_n) * sec_n) for m in range(mp_n)]
        to_low.append(lax.ppermute(cols, feat_axes, pairs))
        if by > 0:
            cols_high = lax.dynamic_slice_in_dim(high_rows, target_mp * head_cols, head_cols, 2)
            pairs = [(m * sec_n + 1, ((m + by) % mp_n) * sec_n + 1) for m in range(mp_n)]
            to_high.append(lax.ppermute(cols_high, feat_axes, pairs))
    low_total = to_low[0][0].astype(jnp.float32) + (
        to_low[0][1].astype(jnp.float32)
        + sum(piece.astype(jnp.float32) for piece in to_low[1:])
    )
    own_high = lax.dynamic_slice_in_dim(high_rows, mp_at * head_cols, head_cols, 2)
    own_hidden = lax.dynamic_slice_in_dim(hidden1[per_section:], mp_at * head_cols, head_cols, 2)
    high_total = own_hidden.astype(jnp.float32) + (
        own_high.astype(jnp.float32) + sum(piece.astype(jnp.float32) for piece in to_high)
    )
    final_cols = jnp.where(is_first, low_total, high_total).astype(jnp.bfloat16)
    return (key_store, value_store, final_cols)


def solution(mesh):
    sizes = dict(tm_n=mesh.shape["tm"], mp_n=mesh.shape["mp"], sec_n=mesh.shape["section"])
    in_specs = (
        P("groups", None, "tm"),
        P("groups"),
        P(None, ("mp", "section")),
        P("section", None),
        P("section", None, "mp"),
        P("section", None, "mp"),
        P("section", None, "mp"),
        P("section", "mp", None),
    )
    out_specs = (
        P("section", "groups", "mp", None, "tm"),
        P("section", "groups", "mp", None, "tm"),
        P(("groups", "section"), "tm", "mp"),
    )

    def body(*args):
        return per_device(*args, **sizes)

    return jax.shard_map(body, mesh=mesh, in_specs=in_specs, out_specs=out_specs, check_vma=False)
```

```python
import jax
import jax.numpy as jnp
from jax import lax
from jax.sharding import PartitionSpec as P

STRIDE = 32
HD = 80
SMALL_GROUP = 4


def shift_from(value, axis, size, by, cyclic):
    pairs = [(i, (i + by) % size) for i in range(size) if cyclic or i + by < size]
    return lax.ppermute(value, axis, pairs)


def gather_ordered(value, axis, size, me):
    if size > SMALL_GROUP:
        return lax.all_gather(value, axis, axis=0)
    received = [value] + [shift_from(value, axis, size, by, True) for by in range(1, size)]
    stack = jnp.stack(received, 0)
    order = (me - jnp.arange(size, dtype=jnp.int32)) % size
    return jnp.take(stack, order, axis=0)


def gather_causal(value, tm_n, sec_n, tm_at, phase, width):
    if tm_n > SMALL_GROUP:
        gathered = lax.all_gather(value, "tm", axis=value.ndim - 1, tiled=True)
        return gathered, jnp.arange(tm_n * width, dtype=jnp.int32)
    pieces = []
    positions = []
    local = jnp.arange(width, dtype=jnp.int32)
    for by in range(tm_n - 1, 0, -1):
        pairs = [(t * sec_n + phase, (t + by) * sec_n + phase) for t in range(tm_n - by)]
        pieces.append(lax.ppermute(value, ("tm", "section"), pairs))
        positions.append((tm_at - by) * width + local)
    pieces.append(value)
    positions.append(tm_at * width + local)
    return jnp.concatenate(pieces, -1), jnp.concatenate(positions, 0)


def absorb_block(running, key_block, value_block, key_pos, query_rows, query_pos, first_valid):
    run_max, run_sum, accumulated = running
    allowed = (key_pos[None, None, :] <= query_pos[None, :, None]) & (
        (key_pos[None, None, :] >= first_valid[:, None, None])
        | (key_pos[None, None, :] == query_pos[None, :, None])
    )
    scores = jnp.einsum(
        "btkgh,bkhn->bkgtn", query_rows, key_block, preferred_element_type=jnp.float32
    )
    scores = jnp.where(allowed[:, None, None], scores, -jnp.inf)
    new_max = jnp.maximum(run_max, jnp.max(scores, -1))
    rescale = jnp.exp(run_max - new_max)
    exp_scores = jnp.exp(scores - new_max[..., None])
    new_sum = run_sum * rescale + jnp.sum(exp_scores, -1)
    contribution = jnp.einsum(
        "bkgtn,bkhn->bkgth",
        exp_scores.astype(jnp.bfloat16),
        value_block,
        preferred_element_type=jnp.float32,
    )
    return (new_max, new_sum, accumulated * rescale[..., None] + contribution)


def attend_layer(hidden_in, seq_lens, gain, query_w, key_w, value_w, out_w, sizes, phase):
    tm_n, sec_n, tm_at, total_tokens = sizes
    batch_count, tok_count, feature_count = hidden_in.shape
    hidden32 = hidden_in.astype(jnp.float32)
    gain32 = gain.astype(jnp.float32)
    scaled = hidden32 * lax.rsqrt(jnp.mean(hidden32 * hidden32, -1, keepdims=True) + 1e-06)
    layer_input = (scaled * gain32).astype(jnp.bfloat16)
    queries = (
        jnp.einsum("btd,de->bte", layer_input, query_w, preferred_element_type=jnp.float32)
        * HD ** (-0.5)
    ).astype(jnp.bfloat16)
    key_t = jnp.einsum(
        "btd,de->bet", layer_input, key_w, preferred_element_type=jnp.float32
    ).astype(jnp.bfloat16)
    value_t = jnp.einsum(
        "btd,de->bet", layer_input, value_w, preferred_element_type=jnp.float32
    ).astype(jnp.bfloat16)
    kv_local = key_w.shape[1] // HD
    group_size = query_w.shape[1] // key_w.shape[1]
    key_t = key_t.reshape(batch_count, kv_local, HD, tok_count)
    value_t = value_t.reshape(batch_count, kv_local, HD, tok_count)
    query_rows = queries.reshape(batch_count, tok_count, kv_local, group_size, HD)
    query_pos = tm_at * tok_count + jnp.arange(tok_count, dtype=jnp.int32)
    first_valid = total_tokens - seq_lens // STRIDE
    both, key_pos = gather_causal(
        jnp.stack([key_t, value_t], 0), tm_n, sec_n, tm_at, phase, tok_count
    )
    key_count = both.shape[-1]
    block_width = 1024 if key_count % 1024 == 0 else key_count
    rounds = key_count // block_width
    blocks = jnp.moveaxis(
        both.reshape(2, batch_count, kv_local, HD, rounds, block_width), 4, 0
    )
    pos_blocks = key_pos.reshape(rounds, block_width)
    start_state = (
        jnp.full((batch_count, kv_local, group_size, tok_count), -1e30, jnp.float32),
        jnp.zeros((batch_count, kv_local, group_size, tok_count), jnp.float32),
        jnp.zeros((batch_count, kv_local, group_size, tok_count, HD), jnp.float32),
    )
    if rounds == 1:
        result = absorb_block(
            start_state, blocks[0, 0], blocks[0, 1], pos_blocks[0], query_rows, query_pos,
            first_valid,
        )
    else:

        def scan_step(state, block_item):
            kv_block, pos_block = block_item
            return (
                absorb_block(
                    state, kv_block[0], kv_block[1], pos_block, query_rows, query_pos,
                    first_valid,
                ),
                None,
            )

        result, _ = lax.scan(scan_step, start_state, (blocks, pos_blocks))
    run_max, run_sum, accumulated = result
    attended = (accumulated / run_sum[..., None]).astype(jnp.bfloat16)
    attended = attended.transpose(0, 3, 1, 2, 4).reshape(
        batch_count, tok_count, kv_local * group_size * HD
    )
    if out_w is None:
        return attended, key_t, value_t
    partial_value = jnp.einsum("bte,ed->btd", attended, out_w, preferred_element_type=jnp.float32)
    return partial_value.astype(jnp.bfloat16), key_t, value_t


def per_device(
    series, lengths, patch_weight, norm_gain, query_weight, key_weight, value_weight, out_weight,
    *, tm_n, mp_n, sec_n
):
    seq_count, channels, steps_dev = series.shape
    tok_count = steps_dev // STRIDE
    tm_at = lax.axis_index("tm")
    mp_at = lax.axis_index("mp")
    sec_at = lax.axis_index("section")
    feat_axes = ("mp", "section")
    feat_n = mp_n * sec_n
    total_steps = steps_dev * tm_n
    total_tokens = tok_count * tm_n

    first_step = total_steps - lengths
    step_pos = tm_at * steps_dev + jnp.arange(steps_dev, dtype=jnp.int32)
    valid = (step_pos[None, :] >= first_step[:, None]).astype(jnp.float32)
    values = series.astype(jnp.float32)
    masked = values * valid[:, None, :]
    local_sum = jnp.sum(masked, -1)
    shard_lo = jnp.arange(tm_n, dtype=jnp.int32) * steps_dev
    counts = jnp.clip(
        shard_lo[None, :] + steps_dev - jnp.maximum(shard_lo[None, :], first_step[:, None]),
        0,
        steps_dev,
    ).astype(jnp.float32)
    my_count = jnp.sum(valid, -1)
    local_mean = local_sum / jnp.maximum(my_count, 1.0)[:, None]
    local_dev = (values - local_mean[..., None]) * valid[:, None, :]
    local_m2 = jnp.sum(local_dev * local_dev, -1)
    tail = series[:, :, steps_dev - STRIDE :]
    if tm_n > SMALL_GROUP:
        stats = lax.all_gather(jnp.stack([local_sum, local_m2], -1), "tm", axis=0)
        prior_raw = shift_from(tail, "tm", tm_n, 1, False).astype(jnp.float32)
    else:
        payload = jnp.concatenate(
            [jnp.stack([local_sum, local_m2], -1), tail.astype(jnp.float32)], -1
        )
        received = [payload] + [shift_from(payload, "tm", tm_n, by, True) for by in range(1, tm_n)]
        prior_raw = received[1][..., 2:] if tm_n > 1 else jnp.zeros_like(payload[..., 2:])
        order = (tm_at - jnp.arange(tm_n, dtype=jnp.int32)) % tm_n
        stats = jnp.take(jnp.stack([piece[..., :2] for piece in received], 0), order, axis=0)
    history = lengths.astype(jnp.float32)[:, None]
    shard_sums = stats[..., 0]
    shard_m2 = stats[..., 1]
    channel_mean = jnp.sum(shard_sums, 0) / history
    shard_counts = jnp.moveaxis(counts, 1, 0)[:, :, None]
    shard_means = shard_sums / jnp.maximum(shard_counts, 1.0)
    gap = shard_means - channel_mean[None]
    spread_total = jnp.sum(shard_m2 + shard_counts * gap * gap, 0)
    variance = spread_total / history
    inv_std = lax.rsqrt(variance + 1e-05)[..., None]

    padded = jnp.concatenate([prior_raw, series.astype(jnp.float32)], -1)
    padded_pos = tm_at * steps_dev - STRIDE + jnp.arange(steps_dev + STRIDE, dtype=jnp.int32)
    padded_valid = (
        (padded_pos[None, :] >= first_step[:, None]) & (padded_pos[None, :] >= 0)
    ).astype(jnp.float32)[:, None, :]
    normed = (
        (padded * padded_valid - channel_mean[..., None]) * padded_valid * inv_std
    ).astype(jnp.bfloat16)
    kernel = patch_weight.reshape(channels, 2 * STRIDE, patch_weight.shape[1])
    chunk_tok = 16 if tok_count % 16 == 0 else tok_count
    chunk_count = tok_count // chunk_tok
    chunks = jnp.stack(
        [
            normed[:, :, q * chunk_tok * STRIDE : (q + 1) * chunk_tok * STRIDE + STRIDE]
            for q in range(chunk_count)
        ],
        1,
    ).reshape(seq_count * chunk_count, channels, chunk_tok * STRIDE + STRIDE)
    tokens = lax.conv_general_dilated(
        chunks,
        kernel,
        window_strides=(STRIDE,),
        padding="VALID",
        dimension_numbers=("NCW", "IWO", "NWC"),
        preferred_element_type=jnp.float32,
    ).astype(jnp.bfloat16)
    tokens = tokens.reshape(seq_count, tok_count, tokens.shape[2])
    column_count = patch_weight.shape[1]
    hidden0 = lax.all_gather(tokens, feat_axes, axis=2, tiled=True)
    feature_count = hidden0.shape[2]
    head_cols = feature_count // mp_n
    sizes = (tm_n, sec_n, tm_at, total_tokens)

    partial0, key0, value0 = attend_layer(
        hidden0, lengths, norm_gain[0], query_weight[0], key_weight[0], value_weight[0],
        out_weight[0], sizes, 0,
    )
    head_sum = None
    for by in range(mp_n):
        pairs = [(m * sec_n, ((m + by) % mp_n) * sec_n + 1) for m in range(mp_n)]
        term = lax.ppermute(partial0, feat_axes, pairs).astype(jnp.float32)
        head_sum = term if head_sum is None else head_sum + term
    hidden1 = (hidden0.astype(jnp.float32) + head_sum).astype(jnp.bfloat16)

    partial1, key1, value1 = attend_layer(
        hidden1, lengths, norm_gain[0], query_weight[0], key_weight[0], value_weight[0],
        out_weight[0], sizes, 1,
    )
    is_first = sec_at == 0
    key_store = jnp.where(is_first, key0, key1)[None]
    value_store = jnp.where(is_first, value0, value1)[None]

    per_section = seq_count // sec_n
    low_rows = partial1[:per_section]
    high_rows = partial1[per_section:]
    low_hidden = hidden1[:per_section]
    to_low = []
    to_high = []
    for by in range(mp_n):
        target_mp = (mp_at + by) % mp_n
        cols = lax.dynamic_slice_in_dim(low_rows, target_mp * head_cols, head_cols, 2)
        if by == 0:
            cols = jnp.stack(
                [lax.dynamic_slice_in_dim(low_hidden, target_mp * head_cols, head_cols, 2), cols], 0
            )
        pairs = [(m * sec_n + 1, ((m + by) % mp_n) * sec_n) for m in range(mp_n)]
        to_low.append(lax.ppermute(cols, feat_axes, pairs))
        if by > 0:
            cols_high = lax.dynamic_slice_in_dim(high_rows, target_mp * head_cols, head_cols, 2)
            pairs = [(m * sec_n + 1, ((m + by) % mp_n) * sec_n + 1) for m in range(mp_n)]
            to_high.append(lax.ppermute(cols_high, feat_axes, pairs))
    low_total = to_low[0][0].astype(jnp.float32) + (
        to_low[0][1].astype(jnp.float32)
        + sum(piece.astype(jnp.float32) for piece in to_low[1:])
    )
    own_high = lax.dynamic_slice_in_dim(high_rows, mp_at * head_cols, head_cols, 2)
    own_hidden = lax.dynamic_slice_in_dim(hidden1[per_section:], mp_at * head_cols, head_cols, 2)
    high_total = own_hidden.astype(jnp.float32) + (
        own_high.astype(jnp.float32) + sum(piece.astype(jnp.float32) for piece in to_high)
    )
    final_cols = jnp.where(is_first, low_total, high_total).astype(jnp.bfloat16)
    return (key_store, value_store, final_cols)


def solution(mesh):
    sizes = dict(tm_n=mesh.shape["tm"], mp_n=mesh.shape["mp"], sec_n=mesh.shape["section"])
    in_specs = (
        P("groups", None, "tm"),
        P("groups"),
        P(None, ("mp", "section")),
        P("section", None),
        P("section", None, "mp"),
        P("section", None, "mp"),
        P("section", None, "mp"),
        P("section", "mp", None),
    )
    out_specs = (
        P("section", "groups", "mp", None, "tm"),
        P("section", "groups", "mp", None, "tm"),
        P(("groups", "section"), "tm", "mp"),
    )

    def body(*args):
        return per_device(*args, **sizes)

    return jax.shard_map(body, mesh=mesh, in_specs=in_specs, out_specs=out_specs, check_vma=False)
```

```python
import jax
import jax.numpy as jnp
from jax import lax
from jax.sharding import PartitionSpec as P

STRIDE = 32
HD = 80
SMALL_GROUP = 4


def shift_from(value, axis, size, by, cyclic):
    pairs = [(i, (i + by) % size) for i in range(size) if cyclic or i + by < size]
    return lax.ppermute(value, axis, pairs)


def gather_ordered(value, axis, size, me):
    if size > SMALL_GROUP:
        return lax.all_gather(value, axis, axis=0)
    received = [value] + [shift_from(value, axis, size, by, True) for by in range(1, size)]
    stack = jnp.stack(received, 0)
    order = (me - jnp.arange(size, dtype=jnp.int32)) % size
    return jnp.take(stack, order, axis=0)


def gather_causal(value, tm_n, sec_n, tm_at, phase, width):
    if tm_n > SMALL_GROUP:
        gathered = lax.all_gather(value, "tm", axis=value.ndim - 1, tiled=True)
        return gathered, jnp.arange(tm_n * width, dtype=jnp.int32)
    pieces = []
    positions = []
    local = jnp.arange(width, dtype=jnp.int32)
    for by in range(tm_n - 1, 0, -1):
        pairs = [(t * sec_n + phase, (t + by) * sec_n + phase) for t in range(tm_n - by)]
        pieces.append(lax.ppermute(value, ("tm", "section"), pairs))
        positions.append((tm_at - by) * width + local)
    pieces.append(value)
    positions.append(tm_at * width + local)
    return jnp.concatenate(pieces, -1), jnp.concatenate(positions, 0)


def absorb_block(running, key_block, value_block, key_pos, query_rows, query_pos, first_valid):
    run_max, run_sum, accumulated = running
    allowed = (key_pos[None, None, :] <= query_pos[None, :, None]) & (
        (key_pos[None, None, :] >= first_valid[:, None, None])
        | (key_pos[None, None, :] == query_pos[None, :, None])
    )
    scores = jnp.einsum(
        "btkgh,bkhn->bkgtn", query_rows, key_block, preferred_element_type=jnp.float32
    )
    scores = jnp.where(allowed[:, None, None], scores, -jnp.inf)
    new_max = jnp.maximum(run_max, jnp.max(scores, -1))
    rescale = jnp.exp(run_max - new_max)
    exp_scores = jnp.exp(scores - new_max[..., None])
    new_sum = run_sum * rescale + jnp.sum(exp_scores, -1)
    contribution = jnp.einsum(
        "bkgtn,bkhn->bkgth",
        exp_scores.astype(jnp.bfloat16),
        value_block,
        preferred_element_type=jnp.float32,
    )
    return (new_max, new_sum, accumulated * rescale[..., None] + contribution)


def attend_layer(hidden_in, seq_lens, gain, query_w, key_w, value_w, out_w, sizes, phase):
    tm_n, sec_n, tm_at, total_tokens = sizes
    batch_count, tok_count, feature_count = hidden_in.shape
    hidden32 = hidden_in.astype(jnp.float32)
    gain32 = gain.astype(jnp.float32)
    scaled = hidden32 * lax.rsqrt(jnp.mean(hidden32 * hidden32, -1, keepdims=True) + 1e-06)
    layer_input = (scaled * gain32).astype(jnp.bfloat16)
    queries = (
        jnp.einsum("btd,de->bte", layer_input, query_w, preferred_element_type=jnp.float32)
        * HD ** (-0.5)
    ).astype(jnp.bfloat16)
    key_t = jnp.einsum(
        "btd,de->bet", layer_input, key_w, preferred_element_type=jnp.float32
    ).astype(jnp.bfloat16)
    value_t = jnp.einsum(
        "btd,de->bet", layer_input, value_w, preferred_element_type=jnp.float32
    ).astype(jnp.bfloat16)
    kv_local = key_w.shape[1] // HD
    group_size = query_w.shape[1] // key_w.shape[1]
    key_t = key_t.reshape(batch_count, kv_local, HD, tok_count)
    value_t = value_t.reshape(batch_count, kv_local, HD, tok_count)
    query_rows = queries.reshape(batch_count, tok_count, kv_local, group_size, HD)
    query_pos = tm_at * tok_count + jnp.arange(tok_count, dtype=jnp.int32)
    first_valid = total_tokens - seq_lens // STRIDE
    both, key_pos = gather_causal(
        jnp.stack([key_t, value_t], 0), tm_n, sec_n, tm_at, phase, tok_count
    )
    key_count = both.shape[-1]
    block_width = 1024 if key_count % 1024 == 0 else key_count
    rounds = key_count // block_width
    blocks = jnp.moveaxis(
        both.reshape(2, batch_count, kv_local, HD, rounds, block_width), 4, 0
    )
    pos_blocks = key_pos.reshape(rounds, block_width)
    start_state = (
        jnp.full((batch_count, kv_local, group_size, tok_count), -1e30, jnp.float32),
        jnp.zeros((batch_count, kv_local, group_size, tok_count), jnp.float32),
        jnp.zeros((batch_count, kv_local, group_size, tok_count, HD), jnp.float32),
    )
    if rounds == 1:
        result = absorb_block(
            start_state, blocks[0, 0], blocks[0, 1], pos_blocks[0], query_rows, query_pos,
            first_valid,
        )
    else:

        def scan_step(state, block_item):
            kv_block, pos_block = block_item
            return (
                absorb_block(
                    state, kv_block[0], kv_block[1], pos_block, query_rows, query_pos,
                    first_valid,
                ),
                None,
            )

        result, _ = lax.scan(scan_step, start_state, (blocks, pos_blocks))
    run_max, run_sum, accumulated = result
    attended = (accumulated / run_sum[..., None]).astype(jnp.bfloat16)
    attended = attended.transpose(0, 3, 1, 2, 4).reshape(
        batch_count, tok_count, kv_local * group_size * HD
    )
    if out_w is None:
        return attended, key_t, value_t
    partial_value = jnp.einsum("bte,ed->btd", attended, out_w, preferred_element_type=jnp.float32)
    return partial_value, key_t, value_t


def per_device(
    series, lengths, patch_weight, norm_gain, query_weight, key_weight, value_weight, out_weight,
    *, tm_n, mp_n, sec_n
):
    seq_count, channels, steps_dev = series.shape
    tok_count = steps_dev // STRIDE
    tm_at = lax.axis_index("tm")
    mp_at = lax.axis_index("mp")
    sec_at = lax.axis_index("section")
    feat_axes = ("mp", "section")
    feat_n = mp_n * sec_n
    total_steps = steps_dev * tm_n
    total_tokens = tok_count * tm_n

    first_step = total_steps - lengths
    step_pos = tm_at * steps_dev + jnp.arange(steps_dev, dtype=jnp.int32)
    valid = (step_pos[None, :] >= first_step[:, None]).astype(jnp.float32)
    values = series.astype(jnp.float32)
    masked = values * valid[:, None, :]
    local_sum = jnp.sum(masked, -1)
    shard_lo = jnp.arange(tm_n, dtype=jnp.int32) * steps_dev
    counts = jnp.clip(
        shard_lo[None, :] + steps_dev - jnp.maximum(shard_lo[None, :], first_step[:, None]),
        0,
        steps_dev,
    ).astype(jnp.float32)
    my_count = jnp.sum(valid, -1)
    local_mean = local_sum / jnp.maximum(my_count, 1.0)[:, None]
    local_dev = (values - local_mean[..., None]) * valid[:, None, :]
    local_m2 = jnp.sum(local_dev * local_dev, -1)
    tail = series[:, :, steps_dev - STRIDE :]
    if tm_n > SMALL_GROUP:
        stats = lax.all_gather(jnp.stack([local_sum, local_m2], -1), "tm", axis=0)
        prior_raw = shift_from(tail, "tm", tm_n, 1, False).astype(jnp.float32)
    else:
        payload = jnp.concatenate(
            [jnp.stack([local_sum, local_m2], -1), tail.astype(jnp.float32)], -1
        )
        received = [payload] + [shift_from(payload, "tm", tm_n, by, True) for by in range(1, tm_n)]
        prior_raw = received[1][..., 2:] if tm_n > 1 else jnp.zeros_like(payload[..., 2:])
        order = (tm_at - jnp.arange(tm_n, dtype=jnp.int32)) % tm_n
        stats = jnp.take(jnp.stack([piece[..., :2] for piece in received], 0), order, axis=0)
    history = lengths.astype(jnp.float32)[:, None]
    shard_sums = stats[..., 0]
    shard_m2 = stats[..., 1]
    channel_mean = jnp.sum(shard_sums, 0) / history
    shard_counts = jnp.moveaxis(counts, 1, 0)[:, :, None]
    shard_means = shard_sums / jnp.maximum(shard_counts, 1.0)
    gap = shard_means - channel_mean[None]
    spread_total = jnp.sum(shard_m2 + shard_counts * gap * gap, 0)
    variance = spread_total / history
    inv_std = lax.rsqrt(variance + 1e-05)[..., None]

    padded = jnp.concatenate([prior_raw, series.astype(jnp.float32)], -1)
    padded_pos = tm_at * steps_dev - STRIDE + jnp.arange(steps_dev + STRIDE, dtype=jnp.int32)
    padded_valid = (
        (padded_pos[None, :] >= first_step[:, None]) & (padded_pos[None, :] >= 0)
    ).astype(jnp.float32)[:, None, :]
    normed = (
        (padded * padded_valid - channel_mean[..., None]) * padded_valid * inv_std
    ).astype(jnp.bfloat16)
    kernel = patch_weight.reshape(channels, 2 * STRIDE, patch_weight.shape[1])
    chunk_tok = 16 if tok_count % 16 == 0 else tok_count
    chunk_count = tok_count // chunk_tok
    chunks = jnp.stack(
        [
            normed[:, :, q * chunk_tok * STRIDE : (q + 1) * chunk_tok * STRIDE + STRIDE]
            for q in range(chunk_count)
        ],
        1,
    ).reshape(seq_count * chunk_count, channels, chunk_tok * STRIDE + STRIDE)
    tokens = lax.conv_general_dilated(
        chunks,
        kernel,
        window_strides=(STRIDE,),
        padding="VALID",
        dimension_numbers=("NCW", "IWO", "NWC"),
        preferred_element_type=jnp.float32,
    ).astype(jnp.bfloat16)
    tokens = tokens.reshape(seq_count, tok_count, tokens.shape[2])
    column_count = patch_weight.shape[1]
    hidden0 = lax.all_gather(tokens, feat_axes, axis=2, tiled=True)
    feature_count = hidden0.shape[2]
    head_cols = feature_count // mp_n
    sizes = (tm_n, sec_n, tm_at, total_tokens)

    partial0, key0, value0 = attend_layer(
        hidden0, lengths, norm_gain[0], query_weight[0], key_weight[0], value_weight[0],
        out_weight[0], sizes, 0,
    )
    head_cols = feature_count // mp_n
    own_cols = mp_at * head_cols
    summed = lax.dynamic_slice_in_dim(partial0, own_cols, head_cols, 2)
    for by in range(1, mp_n):
        target_cols = ((mp_at + by) % mp_n) * head_cols
        piece = lax.dynamic_slice_in_dim(partial0, target_cols, head_cols, 2).astype(jnp.bfloat16)
        pairs = [(m * sec_n, ((m + by) % mp_n) * sec_n) for m in range(mp_n)]
        summed = summed + lax.ppermute(piece, feat_axes, pairs).astype(jnp.float32)
    own_hidden0 = lax.dynamic_slice_in_dim(hidden0, own_cols, head_cols, 2)
    hidden1_cols = (own_hidden0.astype(jnp.float32) + summed).astype(jnp.bfloat16)
    arrivals = []
    for by in range(mp_n):
        pairs = [(m * sec_n, ((m + by) % mp_n) * sec_n + 1) for m in range(mp_n)]
        arrivals.append(lax.ppermute(hidden1_cols, feat_axes, pairs))
    if mp_n == 2:
        hidden1 = jnp.where(
            mp_at == 0,
            jnp.concatenate([arrivals[0], arrivals[1]], 2),
            jnp.concatenate([arrivals[1], arrivals[0]], 2),
        )
    else:
        order = (mp_at - jnp.arange(mp_n, dtype=jnp.int32)) % mp_n
        blocks = jnp.take(jnp.stack(arrivals, 0), order, axis=0)
        hidden1 = jnp.moveaxis(blocks, 0, 2).reshape(hidden0.shape)

    partial1, key1, value1 = attend_layer(
        hidden1, lengths, norm_gain[0], query_weight[0], key_weight[0], value_weight[0],
        out_weight[0], sizes, 1,
    )
    is_first = sec_at == 0
    key_store = jnp.where(is_first, key0, key1)[None]
    value_store = jnp.where(is_first, value0, value1)[None]

    per_section = seq_count // sec_n
    low_rows = partial1[:per_section].astype(jnp.bfloat16)
    high_rows = partial1[per_section:].astype(jnp.bfloat16)
    low_hidden = hidden1[:per_section]
    to_low = []
    to_high = []
    for by in range(mp_n):
        target_mp = (mp_at + by) % mp_n
        cols = lax.dynamic_slice_in_dim(low_rows, target_mp * head_cols, head_cols, 2)
        if by == 0:
            cols = jnp.stack(
                [lax.dynamic_slice_in_dim(low_hidden, target_mp * head_cols, head_cols, 2), cols], 0
            )
        pairs = [(m * sec_n + 1, ((m + by) % mp_n) * sec_n) for m in range(mp_n)]
        to_low.append(lax.ppermute(cols, feat_axes, pairs))
        if by > 0:
            cols_high = lax.dynamic_slice_in_dim(high_rows, target_mp * head_cols, head_cols, 2)
            pairs = [(m * sec_n + 1, ((m + by) % mp_n) * sec_n + 1) for m in range(mp_n)]
            to_high.append(lax.ppermute(cols_high, feat_axes, pairs))
    low_total = to_low[0][0].astype(jnp.float32) + (
        to_low[0][1].astype(jnp.float32)
        + sum(piece.astype(jnp.float32) for piece in to_low[1:])
    )
    own_high = lax.dynamic_slice_in_dim(high_rows, mp_at * head_cols, head_cols, 2)
    own_hidden = lax.dynamic_slice_in_dim(hidden1[per_section:], mp_at * head_cols, head_cols, 2)
    high_total = own_hidden.astype(jnp.float32) + (
        own_high.astype(jnp.float32) + sum(piece.astype(jnp.float32) for piece in to_high)
    )
    final_cols = jnp.where(is_first, low_total, high_total).astype(jnp.bfloat16)
    return (key_store, value_store, final_cols)


def solution(mesh):
    sizes = dict(tm_n=mesh.shape["tm"], mp_n=mesh.shape["mp"], sec_n=mesh.shape["section"])
    in_specs = (
        P("groups", None, "tm"),
        P("groups"),
        P(None, ("mp", "section")),
        P("section", None),
        P("section", None, "mp"),
        P("section", None, "mp"),
        P("section", None, "mp"),
        P("section", "mp", None),
    )
    out_specs = (
        P("section", "groups", "mp", None, "tm"),
        P("section", "groups", "mp", None, "tm"),
        P(("groups", "section"), "tm", "mp"),
    )

    def body(*args):
        return per_device(*args, **sizes)

    return jax.shard_map(body, mesh=mesh, in_specs=in_specs, out_specs=out_specs, check_vma=False)
```

```python
import jax
import jax.numpy as jnp
from jax import lax
from jax.sharding import PartitionSpec as P

STRIDE = 32
HD = 80
SMALL_GROUP = 4


def shift_from(value, axis, size, by, cyclic):
    pairs = [(i, (i + by) % size) for i in range(size) if cyclic or i + by < size]
    return lax.ppermute(value, axis, pairs)


def gather_ordered(value, axis, size, me):
    if size > SMALL_GROUP:
        return lax.all_gather(value, axis, axis=0)
    received = [value] + [shift_from(value, axis, size, by, True) for by in range(1, size)]
    stack = jnp.stack(received, 0)
    order = (me - jnp.arange(size, dtype=jnp.int32)) % size
    return jnp.take(stack, order, axis=0)


def gather_causal(value, tm_n, sec_n, tm_at, phase, width):
    if tm_n > SMALL_GROUP:
        gathered = lax.all_gather(value, "tm", axis=value.ndim - 1, tiled=True)
        return gathered, jnp.arange(tm_n * width, dtype=jnp.int32)
    pieces = []
    positions = []
    local = jnp.arange(width, dtype=jnp.int32)
    for by in range(tm_n - 1, 0, -1):
        pairs = [(t * sec_n + phase, (t + by) * sec_n + phase) for t in range(tm_n - by)]
        pieces.append(lax.ppermute(value, ("tm", "section"), pairs))
        positions.append((tm_at - by) * width + local)
    pieces.append(value)
    positions.append(tm_at * width + local)
    return jnp.concatenate(pieces, -1), jnp.concatenate(positions, 0)


def absorb_block(running, key_block, value_block, key_pos, query_rows, query_pos, first_valid):
    run_max, run_sum, accumulated = running
    allowed = (key_pos[None, None, :] <= query_pos[None, :, None]) & (
        (key_pos[None, None, :] >= first_valid[:, None, None])
        | (key_pos[None, None, :] == query_pos[None, :, None])
    )
    scores = jnp.einsum(
        "btkgh,bkhn->bkgtn", query_rows, key_block, preferred_element_type=jnp.float32
    )
    scores = jnp.where(allowed[:, None, None], scores, -jnp.inf)
    new_max = jnp.maximum(run_max, jnp.max(scores, -1))
    rescale = jnp.exp(run_max - new_max)
    exp_scores = jnp.exp(scores - new_max[..., None])
    new_sum = run_sum * rescale + jnp.sum(exp_scores, -1)
    contribution = jnp.einsum(
        "bkgtn,bkhn->bkgth",
        exp_scores.astype(jnp.bfloat16),
        value_block,
        preferred_element_type=jnp.float32,
    )
    return (new_max, new_sum, accumulated * rescale[..., None] + contribution)


def attend_layer(hidden_in, seq_lens, gain, query_w, key_w, value_w, out_w, sizes, phase):
    tm_n, sec_n, tm_at, total_tokens = sizes
    batch_count, tok_count, feature_count = hidden_in.shape
    hidden32 = hidden_in.astype(jnp.float32)
    gain32 = gain.astype(jnp.float32)
    scaled = hidden32 * lax.rsqrt(jnp.mean(hidden32 * hidden32, -1, keepdims=True) + 1e-06)
    layer_input = (scaled * gain32).astype(jnp.bfloat16)
    queries = (
        jnp.einsum("btd,de->bte", layer_input, query_w, preferred_element_type=jnp.float32)
        * HD ** (-0.5)
    ).astype(jnp.bfloat16)
    key_t = jnp.einsum(
        "btd,de->bet", layer_input, key_w, preferred_element_type=jnp.float32
    ).astype(jnp.bfloat16)
    value_t = jnp.einsum(
        "btd,de->bet", layer_input, value_w, preferred_element_type=jnp.float32
    ).astype(jnp.bfloat16)
    kv_local = key_w.shape[1] // HD
    group_size = query_w.shape[1] // key_w.shape[1]
    key_t = key_t.reshape(batch_count, kv_local, HD, tok_count)
    value_t = value_t.reshape(batch_count, kv_local, HD, tok_count)
    query_rows = queries.reshape(batch_count, tok_count, kv_local, group_size, HD)
    query_pos = tm_at * tok_count + jnp.arange(tok_count, dtype=jnp.int32)
    first_valid = total_tokens - seq_lens // STRIDE
    both, key_pos = gather_causal(
        jnp.stack([key_t, value_t], 0), tm_n, sec_n, tm_at, phase, tok_count
    )
    key_count = both.shape[-1]
    block_width = 1024 if key_count % 1024 == 0 else key_count
    rounds = key_count // block_width
    blocks = jnp.moveaxis(
        both.reshape(2, batch_count, kv_local, HD, rounds, block_width), 4, 0
    )
    pos_blocks = key_pos.reshape(rounds, block_width)
    start_state = (
        jnp.full((batch_count, kv_local, group_size, tok_count), -1e30, jnp.float32),
        jnp.zeros((batch_count, kv_local, group_size, tok_count), jnp.float32),
        jnp.zeros((batch_count, kv_local, group_size, tok_count, HD), jnp.float32),
    )
    if rounds == 1:
        result = absorb_block(
            start_state, blocks[0, 0], blocks[0, 1], pos_blocks[0], query_rows, query_pos,
            first_valid,
        )
    else:

        def scan_step(state, block_item):
            kv_block, pos_block = block_item
            return (
                absorb_block(
                    state, kv_block[0], kv_block[1], pos_block, query_rows, query_pos,
                    first_valid,
                ),
                None,
            )

        result, _ = lax.scan(scan_step, start_state, (blocks, pos_blocks))
    run_max, run_sum, accumulated = result
    attended = (accumulated / run_sum[..., None]).astype(jnp.bfloat16)
    attended = attended.transpose(0, 3, 1, 2, 4).reshape(
        batch_count, tok_count, kv_local * group_size * HD
    )
    if out_w is None:
        return attended, key_t, value_t
    partial_value = jnp.einsum("bte,ed->btd", attended, out_w, preferred_element_type=jnp.float32)
    return partial_value.astype(jnp.bfloat16), key_t, value_t


def per_device(
    series, lengths, patch_weight, norm_gain, query_weight, key_weight, value_weight, out_weight,
    *, tm_n, mp_n, sec_n
):
    seq_count, channels, steps_dev = series.shape
    tok_count = steps_dev // STRIDE
    tm_at = lax.axis_index("tm")
    mp_at = lax.axis_index("mp")
    sec_at = lax.axis_index("section")
    feat_axes = ("mp", "section")
    feat_n = mp_n * sec_n
    total_steps = steps_dev * tm_n
    total_tokens = tok_count * tm_n

    first_step = total_steps - lengths
    step_pos = tm_at * steps_dev + jnp.arange(steps_dev, dtype=jnp.int32)
    valid = (step_pos[None, :] >= first_step[:, None]).astype(jnp.float32)
    values = series.astype(jnp.float32)
    masked = values * valid[:, None, :]
    local_sum = jnp.sum(masked, -1)
    shard_lo = jnp.arange(tm_n, dtype=jnp.int32) * steps_dev
    counts = jnp.clip(
        shard_lo[None, :] + steps_dev - jnp.maximum(shard_lo[None, :], first_step[:, None]),
        0,
        steps_dev,
    ).astype(jnp.float32)
    my_count = jnp.sum(valid, -1)
    local_mean = local_sum / jnp.maximum(my_count, 1.0)[:, None]
    local_dev = (values - local_mean[..., None]) * valid[:, None, :]
    local_m2 = jnp.sum(local_dev * local_dev, -1)
    tail = series[:, :, steps_dev - STRIDE :]
    if tm_n > SMALL_GROUP:
        stats = lax.all_gather(jnp.stack([local_sum, local_m2], -1), "tm", axis=0)
        prior_raw = shift_from(tail, "tm", tm_n, 1, False).astype(jnp.float32)
    else:
        payload = jnp.concatenate(
            [jnp.stack([local_sum, local_m2], -1), tail.astype(jnp.float32)], -1
        )
        received = [payload] + [shift_from(payload, "tm", tm_n, by, True) for by in range(1, tm_n)]
        prior_raw = received[1][..., 2:] if tm_n > 1 else jnp.zeros_like(payload[..., 2:])
        order = (tm_at - jnp.arange(tm_n, dtype=jnp.int32)) % tm_n
        stats = jnp.take(jnp.stack([piece[..., :2] for piece in received], 0), order, axis=0)
    history = lengths.astype(jnp.float32)[:, None]
    shard_sums = stats[..., 0]
    shard_m2 = stats[..., 1]
    channel_mean = jnp.sum(shard_sums, 0) / history
    shard_counts = jnp.moveaxis(counts, 1, 0)[:, :, None]
    shard_means = shard_sums / jnp.maximum(shard_counts, 1.0)
    gap = shard_means - channel_mean[None]
    spread_total = jnp.sum(shard_m2 + shard_counts * gap * gap, 0)
    variance = spread_total / history
    inv_std = lax.rsqrt(variance + 1e-05)[..., None]

    padded = jnp.concatenate([prior_raw, series.astype(jnp.float32)], -1)
    padded_pos = tm_at * steps_dev - STRIDE + jnp.arange(steps_dev + STRIDE, dtype=jnp.int32)
    padded_valid = (
        (padded_pos[None, :] >= first_step[:, None]) & (padded_pos[None, :] >= 0)
    ).astype(jnp.float32)[:, None, :]
    normed = (
        (padded * padded_valid - channel_mean[..., None]) * padded_valid * inv_std
    ).astype(jnp.bfloat16)
    kernel = patch_weight.reshape(channels, 2 * STRIDE, patch_weight.shape[1])
    chunk_tok = 32 if tok_count % 32 == 0 else tok_count
    chunk_count = tok_count // chunk_tok
    chunks = jnp.stack(
        [
            normed[:, :, q * chunk_tok * STRIDE : (q + 1) * chunk_tok * STRIDE + STRIDE]
            for q in range(chunk_count)
        ],
        1,
    ).reshape(seq_count * chunk_count, channels, chunk_tok * STRIDE + STRIDE)
    tokens = lax.conv_general_dilated(
        chunks,
        kernel,
        window_strides=(STRIDE,),
        padding="VALID",
        dimension_numbers=("NCW", "IWO", "NWC"),
        preferred_element_type=jnp.float32,
    ).astype(jnp.bfloat16)
    tokens = tokens.reshape(seq_count, tok_count, tokens.shape[2])
    column_count = patch_weight.shape[1]
    hidden0 = lax.all_gather(tokens, feat_axes, axis=2, tiled=True)
    feature_count = hidden0.shape[2]
    head_cols = feature_count // mp_n
    sizes = (tm_n, sec_n, tm_at, total_tokens)

    partial0, key0, value0 = attend_layer(
        hidden0, lengths, norm_gain[0], query_weight[0], key_weight[0], value_weight[0],
        out_weight[0], sizes, 0,
    )
    head_sum = None
    for by in range(mp_n):
        pairs = [(m * sec_n, ((m + by) % mp_n) * sec_n + 1) for m in range(mp_n)]
        term = lax.ppermute(partial0, feat_axes, pairs).astype(jnp.float32)
        head_sum = term if head_sum is None else head_sum + term
    hidden1 = (hidden0.astype(jnp.float32) + head_sum).astype(jnp.bfloat16)

    partial1, key1, value1 = attend_layer(
        hidden1, lengths, norm_gain[0], query_weight[0], key_weight[0], value_weight[0],
        out_weight[0], sizes, 1,
    )
    is_first = sec_at == 0
    key_store = jnp.where(is_first, key0, key1)[None]
    value_store = jnp.where(is_first, value0, value1)[None]

    per_section = seq_count // sec_n
    low_rows = partial1[:per_section]
    high_rows = partial1[per_section:]
    low_hidden = hidden1[:per_section]
    to_low = []
    to_high = []
    for by in range(mp_n):
        target_mp = (mp_at + by) % mp_n
        cols = lax.dynamic_slice_in_dim(low_rows, target_mp * head_cols, head_cols, 2)
        if by == 0:
            cols = jnp.stack(
                [lax.dynamic_slice_in_dim(low_hidden, target_mp * head_cols, head_cols, 2), cols], 0
            )
        pairs = [(m * sec_n + 1, ((m + by) % mp_n) * sec_n) for m in range(mp_n)]
        to_low.append(lax.ppermute(cols, feat_axes, pairs))
        if by > 0:
            cols_high = lax.dynamic_slice_in_dim(high_rows, target_mp * head_cols, head_cols, 2)
            pairs = [(m * sec_n + 1, ((m + by) % mp_n) * sec_n + 1) for m in range(mp_n)]
            to_high.append(lax.ppermute(cols_high, feat_axes, pairs))
    low_total = to_low[0][0].astype(jnp.float32) + (
        to_low[0][1].astype(jnp.float32)
        + sum(piece.astype(jnp.float32) for piece in to_low[1:])
    )
    own_high = lax.dynamic_slice_in_dim(high_rows, mp_at * head_cols, head_cols, 2)
    own_hidden = lax.dynamic_slice_in_dim(hidden1[per_section:], mp_at * head_cols, head_cols, 2)
    high_total = own_hidden.astype(jnp.float32) + (
        own_high.astype(jnp.float32) + sum(piece.astype(jnp.float32) for piece in to_high)
    )
    final_cols = jnp.where(is_first, low_total, high_total).astype(jnp.bfloat16)
    return (key_store, value_store, final_cols)


def solution(mesh):
    sizes = dict(tm_n=mesh.shape["tm"], mp_n=mesh.shape["mp"], sec_n=mesh.shape["section"])
    in_specs = (
        P("groups", None, "tm"),
        P("groups"),
        P(None, ("mp", "section")),
        P("section", None),
        P("section", None, "mp"),
        P("section", None, "mp"),
        P("section", None, "mp"),
        P("section", "mp", None),
    )
    out_specs = (
        P("section", "groups", "mp", None, "tm"),
        P("section", "groups", "mp", None, "tm"),
        P(("groups", "section"), "tm", "mp"),
    )

    def body(*args):
        return per_device(*args, **sizes)

    return jax.shard_map(body, mesh=mesh, in_specs=in_specs, out_specs=out_specs, check_vma=False)
```

```python
import jax
import jax.numpy as jnp
from jax import lax
from jax.sharding import PartitionSpec as P

STRIDE = 32
HD = 80
SMALL_GROUP = 4


def shift_from(value, axis, size, by, cyclic):
    pairs = [(i, (i + by) % size) for i in range(size) if cyclic or i + by < size]
    return lax.ppermute(value, axis, pairs)


def gather_ordered(value, axis, size, me):
    if size > SMALL_GROUP:
        return lax.all_gather(value, axis, axis=0)
    received = [value] + [shift_from(value, axis, size, by, True) for by in range(1, size)]
    stack = jnp.stack(received, 0)
    order = (me - jnp.arange(size, dtype=jnp.int32)) % size
    return jnp.take(stack, order, axis=0)


def gather_causal(value, tm_n, sec_n, tm_at, phase, width):
    if tm_n > SMALL_GROUP:
        gathered = lax.all_gather(value, "tm", axis=value.ndim - 1, tiled=True)
        return gathered, jnp.arange(tm_n * width, dtype=jnp.int32)
    pieces = []
    positions = []
    local = jnp.arange(width, dtype=jnp.int32)
    for by in range(tm_n - 1, 0, -1):
        pairs = [(t * sec_n + phase, (t + by) * sec_n + phase) for t in range(tm_n - by)]
        pieces.append(lax.ppermute(value, ("tm", "section"), pairs))
        positions.append((tm_at - by) * width + local)
    pieces.append(value)
    positions.append(tm_at * width + local)
    return jnp.concatenate(pieces, -1), jnp.concatenate(positions, 0)


def absorb_block(running, key_block, value_block, key_pos, query_rows, query_pos, first_valid):
    run_max, run_sum, accumulated = running
    allowed = (key_pos[None, None, :] <= query_pos[None, :, None]) & (
        (key_pos[None, None, :] >= first_valid[:, None, None])
        | (key_pos[None, None, :] == query_pos[None, :, None])
    )
    scores = jnp.einsum(
        "btkgh,bkhn->bkgtn", query_rows, key_block, preferred_element_type=jnp.float32
    )
    scores = jnp.where(allowed[:, None, None], scores, -jnp.inf)
    new_max = jnp.maximum(run_max, jnp.max(scores, -1))
    rescale = jnp.exp(run_max - new_max)
    exp_scores = jnp.exp(scores - new_max[..., None])
    new_sum = run_sum * rescale + jnp.sum(exp_scores, -1)
    contribution = jnp.einsum(
        "bkgtn,bkhn->bkgth",
        exp_scores.astype(jnp.bfloat16),
        value_block,
        preferred_element_type=jnp.float32,
    )
    return (new_max, new_sum, accumulated * rescale[..., None] + contribution)


def attend_layer(hidden_in, seq_lens, gain, query_w, key_w, value_w, out_w, sizes, phase):
    tm_n, sec_n, tm_at, total_tokens = sizes
    batch_count, tok_count, feature_count = hidden_in.shape
    hidden32 = hidden_in.astype(jnp.float32)
    gain32 = gain.astype(jnp.float32)
    scaled = hidden32 * lax.rsqrt(jnp.mean(hidden32 * hidden32, -1, keepdims=True) + 1e-06)
    layer_input = (scaled * gain32).astype(jnp.bfloat16)
    queries = (
        jnp.einsum("btd,de->bte", layer_input, query_w, preferred_element_type=jnp.float32)
        * HD ** (-0.5)
    ).astype(jnp.bfloat16)
    key_t = jnp.einsum(
        "btd,de->bet", layer_input, key_w, preferred_element_type=jnp.float32
    ).astype(jnp.bfloat16)
    value_t = jnp.einsum(
        "btd,de->bet", layer_input, value_w, preferred_element_type=jnp.float32
    ).astype(jnp.bfloat16)
    kv_local = key_w.shape[1] // HD
    group_size = query_w.shape[1] // key_w.shape[1]
    key_t = key_t.reshape(batch_count, kv_local, HD, tok_count)
    value_t = value_t.reshape(batch_count, kv_local, HD, tok_count)
    query_rows = queries.reshape(batch_count, tok_count, kv_local, group_size, HD)
    query_pos = tm_at * tok_count + jnp.arange(tok_count, dtype=jnp.int32)
    first_valid = total_tokens - seq_lens // STRIDE
    both, key_pos = gather_causal(
        jnp.stack([key_t, value_t], 0), tm_n, sec_n, tm_at, phase, tok_count
    )
    key_count = both.shape[-1]
    block_width = 1024 if key_count % 1024 == 0 else key_count
    rounds = key_count // block_width
    blocks = jnp.moveaxis(
        both.reshape(2, batch_count, kv_local, HD, rounds, block_width), 4, 0
    )
    pos_blocks = key_pos.reshape(rounds, block_width)
    start_state = (
        jnp.full((batch_count, kv_local, group_size, tok_count), -1e30, jnp.float32),
        jnp.zeros((batch_count, kv_local, group_size, tok_count), jnp.float32),
        jnp.zeros((batch_count, kv_local, group_size, tok_count, HD), jnp.float32),
    )
    if rounds == 1:
        result = absorb_block(
            start_state, blocks[0, 0], blocks[0, 1], pos_blocks[0], query_rows, query_pos,
            first_valid,
        )
    else:

        def scan_step(state, block_item):
            kv_block, pos_block = block_item
            return (
                absorb_block(
                    state, kv_block[0], kv_block[1], pos_block, query_rows, query_pos,
                    first_valid,
                ),
                None,
            )

        result, _ = lax.scan(scan_step, start_state, (blocks, pos_blocks))
    run_max, run_sum, accumulated = result
    attended = (accumulated / run_sum[..., None]).astype(jnp.bfloat16)
    attended = attended.transpose(0, 3, 1, 2, 4).reshape(
        batch_count, tok_count, kv_local * group_size * HD
    )
    if out_w is None:
        return attended, key_t, value_t
    partial_value = jnp.einsum("bte,ed->btd", attended, out_w, preferred_element_type=jnp.float32)
    return partial_value.astype(jnp.bfloat16), key_t, value_t


def per_device(
    series, lengths, patch_weight, norm_gain, query_weight, key_weight, value_weight, out_weight,
    *, tm_n, mp_n, sec_n
):
    seq_count, channels, steps_dev = series.shape
    tok_count = steps_dev // STRIDE
    tm_at = lax.axis_index("tm")
    mp_at = lax.axis_index("mp")
    sec_at = lax.axis_index("section")
    feat_axes = ("mp", "section")
    feat_n = mp_n * sec_n
    total_steps = steps_dev * tm_n
    total_tokens = tok_count * tm_n

    first_step = total_steps - lengths
    step_pos = tm_at * steps_dev + jnp.arange(steps_dev, dtype=jnp.int32)
    valid = (step_pos[None, :] >= first_step[:, None]).astype(jnp.float32)
    values = series.astype(jnp.float32)
    masked = values * valid[:, None, :]
    local_sum = jnp.sum(masked, -1)
    shard_lo = jnp.arange(tm_n, dtype=jnp.int32) * steps_dev
    counts = jnp.clip(
        shard_lo[None, :] + steps_dev - jnp.maximum(shard_lo[None, :], first_step[:, None]),
        0,
        steps_dev,
    ).astype(jnp.float32)
    my_count = jnp.sum(valid, -1)
    local_mean = local_sum / jnp.maximum(my_count, 1.0)[:, None]
    local_dev = (values - local_mean[..., None]) * valid[:, None, :]
    local_m2 = jnp.sum(local_dev * local_dev, -1)
    tail = series[:, :, steps_dev - STRIDE :]
    if tm_n > SMALL_GROUP:
        stats = lax.all_gather(jnp.stack([local_sum, local_m2], -1), "tm", axis=0)
        prior_raw = shift_from(tail, "tm", tm_n, 1, False).astype(jnp.float32)
    else:
        payload = jnp.concatenate(
            [jnp.stack([local_sum, local_m2], -1), tail.astype(jnp.float32)], -1
        )
        received = [payload] + [shift_from(payload, "tm", tm_n, by, True) for by in range(1, tm_n)]
        prior_raw = received[1][..., 2:] if tm_n > 1 else jnp.zeros_like(payload[..., 2:])
        order = (tm_at - jnp.arange(tm_n, dtype=jnp.int32)) % tm_n
        stats = jnp.take(jnp.stack([piece[..., :2] for piece in received], 0), order, axis=0)
    history = lengths.astype(jnp.float32)[:, None]
    shard_sums = stats[..., 0]
    shard_m2 = stats[..., 1]
    channel_mean = jnp.sum(shard_sums, 0) / history
    shard_counts = jnp.moveaxis(counts, 1, 0)[:, :, None]
    shard_means = shard_sums / jnp.maximum(shard_counts, 1.0)
    gap = shard_means - channel_mean[None]
    spread_total = jnp.sum(shard_m2 + shard_counts * gap * gap, 0)
    variance = spread_total / history
    inv_std = lax.rsqrt(variance + 1e-05)[..., None]

    padded = jnp.concatenate([prior_raw, series.astype(jnp.float32)], -1)
    padded_pos = tm_at * steps_dev - STRIDE + jnp.arange(steps_dev + STRIDE, dtype=jnp.int32)
    padded_valid = (
        (padded_pos[None, :] >= first_step[:, None]) & (padded_pos[None, :] >= 0)
    ).astype(jnp.float32)[:, None, :]
    normed = (
        (padded * padded_valid - channel_mean[..., None]) * padded_valid * inv_std
    ).astype(jnp.bfloat16)
    kernel = patch_weight.reshape(channels, 2 * STRIDE, patch_weight.shape[1])
    chunk_tok = 64 if tok_count % 64 == 0 else tok_count
    chunk_count = tok_count // chunk_tok
    chunks = jnp.stack(
        [
            normed[:, :, q * chunk_tok * STRIDE : (q + 1) * chunk_tok * STRIDE + STRIDE]
            for q in range(chunk_count)
        ],
        1,
    ).reshape(seq_count * chunk_count, channels, chunk_tok * STRIDE + STRIDE)
    tokens = lax.conv_general_dilated(
        chunks,
        kernel,
        window_strides=(STRIDE,),
        padding="VALID",
        dimension_numbers=("NCW", "IWO", "NWC"),
        preferred_element_type=jnp.float32,
    ).astype(jnp.bfloat16)
    tokens = tokens.reshape(seq_count, tok_count, tokens.shape[2])
    column_count = patch_weight.shape[1]
    hidden0 = lax.all_gather(tokens, feat_axes, axis=2, tiled=True)
    feature_count = hidden0.shape[2]
    head_cols = feature_count // mp_n
    sizes = (tm_n, sec_n, tm_at, total_tokens)

    partial0, key0, value0 = attend_layer(
        hidden0, lengths, norm_gain[0], query_weight[0], key_weight[0], value_weight[0],
        out_weight[0], sizes, 0,
    )
    head_sum = None
    for by in range(mp_n):
        pairs = [(m * sec_n, ((m + by) % mp_n) * sec_n + 1) for m in range(mp_n)]
        term = lax.ppermute(partial0, feat_axes, pairs).astype(jnp.float32)
        head_sum = term if head_sum is None else head_sum + term
    hidden1 = (hidden0.astype(jnp.float32) + head_sum).astype(jnp.bfloat16)

    partial1, key1, value1 = attend_layer(
        hidden1, lengths, norm_gain[0], query_weight[0], key_weight[0], value_weight[0],
        out_weight[0], sizes, 1,
    )
    is_first = sec_at == 0
    key_store = jnp.where(is_first, key0, key1)[None]
    value_store = jnp.where(is_first, value0, value1)[None]

    per_section = seq_count // sec_n
    low_rows = partial1[:per_section]
    high_rows = partial1[per_section:]
    low_hidden = hidden1[:per_section]
    to_low = []
    to_high = []
    for by in range(mp_n):
        target_mp = (mp_at + by) % mp_n
        cols = lax.dynamic_slice_in_dim(low_rows, target_mp * head_cols, head_cols, 2)
        if by == 0:
            cols = jnp.stack(
                [lax.dynamic_slice_in_dim(low_hidden, target_mp * head_cols, head_cols, 2), cols], 0
            )
        pairs = [(m * sec_n + 1, ((m + by) % mp_n) * sec_n) for m in range(mp_n)]
        to_low.append(lax.ppermute(cols, feat_axes, pairs))
        if by > 0:
            cols_high = lax.dynamic_slice_in_dim(high_rows, target_mp * head_cols, head_cols, 2)
            pairs = [(m * sec_n + 1, ((m + by) % mp_n) * sec_n + 1) for m in range(mp_n)]
            to_high.append(lax.ppermute(cols_high, feat_axes, pairs))
    low_total = to_low[0][0].astype(jnp.float32) + (
        to_low[0][1].astype(jnp.float32)
        + sum(piece.astype(jnp.float32) for piece in to_low[1:])
    )
    own_high = lax.dynamic_slice_in_dim(high_rows, mp_at * head_cols, head_cols, 2)
    own_hidden = lax.dynamic_slice_in_dim(hidden1[per_section:], mp_at * head_cols, head_cols, 2)
    high_total = own_hidden.astype(jnp.float32) + (
        own_high.astype(jnp.float32) + sum(piece.astype(jnp.float32) for piece in to_high)
    )
    final_cols = jnp.where(is_first, low_total, high_total).astype(jnp.bfloat16)
    return (key_store, value_store, final_cols)


def solution(mesh):
    sizes = dict(tm_n=mesh.shape["tm"], mp_n=mesh.shape["mp"], sec_n=mesh.shape["section"])
    in_specs = (
        P("groups", None, "tm"),
        P("groups"),
        P(None, ("mp", "section")),
        P("section", None),
        P("section", None, "mp"),
        P("section", None, "mp"),
        P("section", None, "mp"),
        P("section", "mp", None),
    )
    out_specs = (
        P("section", "groups", "mp", None, "tm"),
        P("section", "groups", "mp", None, "tm"),
        P(("groups", "section"), "tm", "mp"),
    )

    def body(*args):
        return per_device(*args, **sizes)

    return jax.shard_map(body, mesh=mesh, in_specs=in_specs, out_specs=out_specs, check_vma=False)
```

```python
import jax
import jax.numpy as jnp
from jax import lax
from jax.sharding import PartitionSpec as P

STRIDE = 32
HD = 80
SMALL_GROUP = 4


def shift_from(value, axis, size, by, cyclic):
    pairs = [(i, (i + by) % size) for i in range(size) if cyclic or i + by < size]
    return lax.ppermute(value, axis, pairs)


def gather_ordered(value, axis, size, me):
    if size > SMALL_GROUP:
        return lax.all_gather(value, axis, axis=0)
    received = [value] + [shift_from(value, axis, size, by, True) for by in range(1, size)]
    stack = jnp.stack(received, 0)
    order = (me - jnp.arange(size, dtype=jnp.int32)) % size
    return jnp.take(stack, order, axis=0)


def gather_causal(value, tm_n, sec_n, tm_at, phase, width):
    if tm_n > SMALL_GROUP:
        gathered = lax.all_gather(value, "tm", axis=value.ndim - 1, tiled=True)
        return gathered, jnp.arange(tm_n * width, dtype=jnp.int32)
    pieces = []
    positions = []
    local = jnp.arange(width, dtype=jnp.int32)
    for by in range(tm_n - 1, 0, -1):
        pairs = [(t * sec_n + phase, (t + by) * sec_n + phase) for t in range(tm_n - by)]
        pieces.append(lax.ppermute(value, ("tm", "section"), pairs))
        positions.append((tm_at - by) * width + local)
    pieces.append(value)
    positions.append(tm_at * width + local)
    return jnp.concatenate(pieces, -1), jnp.concatenate(positions, 0)


def absorb_block(running, key_block, value_block, key_pos, query_rows, query_pos, first_valid):
    run_max, run_sum, accumulated = running
    allowed = (key_pos[None, None, :] <= query_pos[None, :, None]) & (
        (key_pos[None, None, :] >= first_valid[:, None, None])
        | (key_pos[None, None, :] == query_pos[None, :, None])
    )
    scores = jnp.einsum(
        "btkgh,bkhn->bkgtn", query_rows, key_block, preferred_element_type=jnp.float32
    )
    scores = jnp.where(allowed[:, None, None], scores, -jnp.inf)
    new_max = jnp.maximum(run_max, jnp.max(scores, -1))
    rescale = jnp.exp(run_max - new_max)
    exp_scores = jnp.exp(scores - new_max[..., None])
    new_sum = run_sum * rescale + jnp.sum(exp_scores, -1)
    contribution = jnp.einsum(
        "bkgtn,bkhn->bkgth",
        exp_scores.astype(jnp.bfloat16),
        value_block,
        preferred_element_type=jnp.float32,
    )
    return (new_max, new_sum, accumulated * rescale[..., None] + contribution)


def attend_layer(hidden_in, seq_lens, gain, query_w, key_w, value_w, out_w, sizes, phase):
    tm_n, sec_n, tm_at, total_tokens = sizes
    batch_count, tok_count, feature_count = hidden_in.shape
    hidden32 = hidden_in.astype(jnp.float32)
    gain32 = gain.astype(jnp.float32)
    scaled = hidden32 * lax.rsqrt(jnp.mean(hidden32 * hidden32, -1, keepdims=True) + 1e-06)
    layer_input = (scaled * gain32).astype(jnp.bfloat16)
    queries = (
        jnp.einsum("btd,de->bte", layer_input, query_w, preferred_element_type=jnp.float32)
        * HD ** (-0.5)
    ).astype(jnp.bfloat16)
    key_t = jnp.einsum(
        "btd,de->bet", layer_input, key_w, preferred_element_type=jnp.float32
    ).astype(jnp.bfloat16)
    value_t = jnp.einsum(
        "btd,de->bet", layer_input, value_w, preferred_element_type=jnp.float32
    ).astype(jnp.bfloat16)
    kv_local = key_w.shape[1] // HD
    group_size = query_w.shape[1] // key_w.shape[1]
    key_t = key_t.reshape(batch_count, kv_local, HD, tok_count)
    value_t = value_t.reshape(batch_count, kv_local, HD, tok_count)
    query_rows = queries.reshape(batch_count, tok_count, kv_local, group_size, HD)
    query_pos = tm_at * tok_count + jnp.arange(tok_count, dtype=jnp.int32)
    first_valid = total_tokens - seq_lens // STRIDE
    both, key_pos = gather_causal(
        jnp.stack([key_t, value_t], 0), tm_n, sec_n, tm_at, phase, tok_count
    )
    key_count = both.shape[-1]
    block_width = 1024 if key_count % 1024 == 0 else key_count
    rounds = key_count // block_width
    blocks = jnp.moveaxis(
        both.reshape(2, batch_count, kv_local, HD, rounds, block_width), 4, 0
    )
    pos_blocks = key_pos.reshape(rounds, block_width)
    start_state = (
        jnp.full((batch_count, kv_local, group_size, tok_count), -1e30, jnp.float32),
        jnp.zeros((batch_count, kv_local, group_size, tok_count), jnp.float32),
        jnp.zeros((batch_count, kv_local, group_size, tok_count, HD), jnp.float32),
    )
    if rounds == 1:
        result = absorb_block(
            start_state, blocks[0, 0], blocks[0, 1], pos_blocks[0], query_rows, query_pos,
            first_valid,
        )
    else:

        def scan_step(state, block_item):
            kv_block, pos_block = block_item
            return (
                absorb_block(
                    state, kv_block[0], kv_block[1], pos_block, query_rows, query_pos,
                    first_valid,
                ),
                None,
            )

        result, _ = lax.scan(scan_step, start_state, (blocks, pos_blocks))
    run_max, run_sum, accumulated = result
    attended = (accumulated / run_sum[..., None]).astype(jnp.bfloat16)
    attended = attended.transpose(0, 3, 1, 2, 4).reshape(
        batch_count, tok_count, kv_local * group_size * HD
    )
    if out_w is None:
        return attended, key_t, value_t
    partial_value = jnp.einsum("bte,ed->btd", attended, out_w, preferred_element_type=jnp.float32)
    return partial_value.astype(jnp.bfloat16), key_t, value_t


def per_device(
    series, lengths, patch_weight, norm_gain, query_weight, key_weight, value_weight, out_weight,
    *, tm_n, mp_n, sec_n
):
    seq_count, channels, steps_dev = series.shape
    tok_count = steps_dev // STRIDE
    tm_at = lax.axis_index("tm")
    mp_at = lax.axis_index("mp")
    sec_at = lax.axis_index("section")
    feat_axes = ("mp", "section")
    feat_n = mp_n * sec_n
    total_steps = steps_dev * tm_n
    total_tokens = tok_count * tm_n

    first_step = total_steps - lengths
    step_pos = tm_at * steps_dev + jnp.arange(steps_dev, dtype=jnp.int32)
    valid = (step_pos[None, :] >= first_step[:, None]).astype(jnp.float32)
    values = series.astype(jnp.float32)
    masked = values * valid[:, None, :]
    local_sum = jnp.sum(masked, -1)
    shard_lo = jnp.arange(tm_n, dtype=jnp.int32) * steps_dev
    counts = jnp.clip(
        shard_lo[None, :] + steps_dev - jnp.maximum(shard_lo[None, :], first_step[:, None]),
        0,
        steps_dev,
    ).astype(jnp.float32)
    my_count = jnp.sum(valid, -1)
    local_mean = local_sum / jnp.maximum(my_count, 1.0)[:, None]
    local_dev = (values - local_mean[..., None]) * valid[:, None, :]
    local_m2 = jnp.sum(local_dev * local_dev, -1)
    tail = series[:, :, steps_dev - STRIDE :]
    if tm_n > SMALL_GROUP:
        stats = lax.all_gather(jnp.stack([local_sum, local_m2], -1), "tm", axis=0)
        prior_raw = shift_from(tail, "tm", tm_n, 1, False).astype(jnp.float32)
    else:
        payload = jnp.concatenate(
            [jnp.stack([local_sum, local_m2], -1), tail.astype(jnp.float32)], -1
        )
        received = [payload] + [shift_from(payload, "tm", tm_n, by, True) for by in range(1, tm_n)]
        prior_raw = received[1][..., 2:] if tm_n > 1 else jnp.zeros_like(payload[..., 2:])
        order = (tm_at - jnp.arange(tm_n, dtype=jnp.int32)) % tm_n
        stats = jnp.take(jnp.stack([piece[..., :2] for piece in received], 0), order, axis=0)
    history = lengths.astype(jnp.float32)[:, None]
    shard_sums = stats[..., 0]
    shard_m2 = stats[..., 1]
    channel_mean = jnp.sum(shard_sums, 0) / history
    shard_counts = jnp.moveaxis(counts, 1, 0)[:, :, None]
    shard_means = shard_sums / jnp.maximum(shard_counts, 1.0)
    gap = shard_means - channel_mean[None]
    spread_total = jnp.sum(shard_m2 + shard_counts * gap * gap, 0)
    variance = spread_total / history
    inv_std = lax.rsqrt(variance + 1e-05)[..., None]

    padded = jnp.concatenate([prior_raw, series.astype(jnp.float32)], -1)
    padded_pos = tm_at * steps_dev - STRIDE + jnp.arange(steps_dev + STRIDE, dtype=jnp.int32)
    padded_valid = (
        (padded_pos[None, :] >= first_step[:, None]) & (padded_pos[None, :] >= 0)
    ).astype(jnp.float32)[:, None, :]
    normed = (
        (padded * padded_valid - channel_mean[..., None]) * padded_valid * inv_std
    ).astype(jnp.bfloat16)
    kernel = patch_weight.reshape(channels, 2 * STRIDE, patch_weight.shape[1])
    chunk_tok = 32 if tok_count % 32 == 0 else tok_count
    chunk_count = tok_count // chunk_tok
    chunks = jnp.stack(
        [
            normed[:, :, q * chunk_tok * STRIDE : (q + 1) * chunk_tok * STRIDE + STRIDE]
            for q in range(chunk_count)
        ],
        1,
    ).reshape(seq_count * chunk_count, channels, chunk_tok * STRIDE + STRIDE)
    tokens = lax.conv_general_dilated(
        chunks,
        kernel,
        window_strides=(STRIDE,),
        padding="VALID",
        dimension_numbers=("NCW", "IWO", "NWC"),
        preferred_element_type=jnp.float32,
    ).astype(jnp.bfloat16)
    tokens = tokens.reshape(seq_count, tok_count, tokens.shape[2])
    column_count = patch_weight.shape[1]
    hidden0 = lax.all_gather(tokens, feat_axes, axis=2, tiled=True)
    feature_count = hidden0.shape[2]
    head_cols = feature_count // mp_n
    sizes = (tm_n, sec_n, tm_at, total_tokens)

    partial0, key0, value0 = attend_layer(
        hidden0, lengths, norm_gain[0], query_weight[0], key_weight[0], value_weight[0],
        out_weight[0], sizes, 0,
    )
    per_section = seq_count // sec_n
    is_first = sec_at == 0
    partial0 = partial0.astype(jnp.bfloat16)
    key_parts, value_parts, partial_parts, hidden_parts = [], [], [], []
    for seq in range(seq_count):
        head_sum = None
        for by in range(mp_n):
            pairs = [(m * sec_n, ((m + by) % mp_n) * sec_n + 1) for m in range(mp_n)]
            term = lax.ppermute(partial0[seq : seq + 1], feat_axes, pairs).astype(jnp.float32)
            head_sum = term if head_sum is None else head_sum + term
        hidden_seq = (hidden0[seq : seq + 1].astype(jnp.float32) + head_sum).astype(jnp.bfloat16)
        partial_seq, key_seq, value_seq = attend_layer(
            hidden_seq, lengths[seq : seq + 1], norm_gain[0], query_weight[0], key_weight[0],
            value_weight[0], out_weight[0], sizes, 1,
        )
        key_parts.append(key_seq)
        value_parts.append(value_seq)
        partial_parts.append(partial_seq.astype(jnp.bfloat16))
        hidden_parts.append(hidden_seq)
    key1 = jnp.concatenate(key_parts, 0)
    value1 = jnp.concatenate(value_parts, 0)
    key_store = jnp.where(is_first, key0, key1)[None]
    value_store = jnp.where(is_first, value0, value1)[None]

    low_rows = jnp.concatenate(partial_parts[:per_section], 0)
    high_rows = jnp.concatenate(partial_parts[per_section:], 0)
    low_hidden = jnp.concatenate(hidden_parts[:per_section], 0)
    high_hidden = jnp.concatenate(hidden_parts[per_section:], 0)
    to_low = []
    to_high = []
    for by in range(mp_n):
        target_mp = (mp_at + by) % mp_n
        cols = lax.dynamic_slice_in_dim(low_rows, target_mp * head_cols, head_cols, 2)
        if by == 0:
            cols = jnp.stack(
                [lax.dynamic_slice_in_dim(low_hidden, target_mp * head_cols, head_cols, 2), cols], 0
            )
        pairs = [(m * sec_n + 1, ((m + by) % mp_n) * sec_n) for m in range(mp_n)]
        to_low.append(lax.ppermute(cols, feat_axes, pairs))
        if by > 0:
            cols_high = lax.dynamic_slice_in_dim(high_rows, target_mp * head_cols, head_cols, 2)
            pairs = [(m * sec_n + 1, ((m + by) % mp_n) * sec_n + 1) for m in range(mp_n)]
            to_high.append(lax.ppermute(cols_high, feat_axes, pairs))
    low_total = to_low[0][0].astype(jnp.float32) + (
        to_low[0][1].astype(jnp.float32)
        + sum(piece.astype(jnp.float32) for piece in to_low[1:])
    )
    own_high = lax.dynamic_slice_in_dim(high_rows, mp_at * head_cols, head_cols, 2)
    own_hidden = lax.dynamic_slice_in_dim(high_hidden, mp_at * head_cols, head_cols, 2)
    high_total = own_hidden.astype(jnp.float32) + (
        own_high.astype(jnp.float32) + sum(piece.astype(jnp.float32) for piece in to_high)
    )
    final_cols = jnp.where(is_first, low_total, high_total).astype(jnp.bfloat16)
    return (key_store, value_store, final_cols)


def solution(mesh):
    sizes = dict(tm_n=mesh.shape["tm"], mp_n=mesh.shape["mp"], sec_n=mesh.shape["section"])
    in_specs = (
        P("groups", None, "tm"),
        P("groups"),
        P(None, ("mp", "section")),
        P("section", None),
        P("section", None, "mp"),
        P("section", None, "mp"),
        P("section", None, "mp"),
        P("section", "mp", None),
    )
    out_specs = (
        P("section", "groups", "mp", None, "tm"),
        P("section", "groups", "mp", None, "tm"),
        P(("groups", "section"), "tm", "mp"),
    )

    def body(*args):
        return per_device(*args, **sizes)

    return jax.shard_map(body, mesh=mesh, in_specs=in_specs, out_specs=out_specs, check_vma=False)
```

```python
import jax
import jax.numpy as jnp
from jax import lax
from jax.sharding import PartitionSpec as P

STRIDE = 32
HD = 80
SMALL_GROUP = 4


def shift_from(value, axis, size, by, cyclic):
    pairs = [(i, (i + by) % size) for i in range(size) if cyclic or i + by < size]
    return lax.ppermute(value, axis, pairs)


def gather_ordered(value, axis, size, me):
    if size > SMALL_GROUP:
        return lax.all_gather(value, axis, axis=0)
    received = [value] + [shift_from(value, axis, size, by, True) for by in range(1, size)]
    stack = jnp.stack(received, 0)
    order = (me - jnp.arange(size, dtype=jnp.int32)) % size
    return jnp.take(stack, order, axis=0)


def gather_causal(value, tm_n, sec_n, tm_at, phase, width):
    if tm_n > SMALL_GROUP:
        gathered = lax.all_gather(value, "tm", axis=value.ndim - 1, tiled=True)
        return gathered, jnp.arange(tm_n * width, dtype=jnp.int32)
    pieces = []
    positions = []
    local = jnp.arange(width, dtype=jnp.int32)
    for by in range(tm_n - 1, 0, -1):
        pairs = [(t * sec_n + phase, (t + by) * sec_n + phase) for t in range(tm_n - by)]
        pieces.append(lax.ppermute(value, ("tm", "section"), pairs))
        positions.append((tm_at - by) * width + local)
    pieces.append(value)
    positions.append(tm_at * width + local)
    return jnp.concatenate(pieces, -1), jnp.concatenate(positions, 0)


def absorb_block(running, key_block, value_block, key_pos, query_rows, query_pos, first_valid):
    run_max, run_sum, accumulated = running
    allowed = (key_pos[None, None, :] <= query_pos[None, :, None]) & (
        (key_pos[None, None, :] >= first_valid[:, None, None])
        | (key_pos[None, None, :] == query_pos[None, :, None])
    )
    scores = jnp.einsum(
        "btkgh,bkhn->bkgtn", query_rows, key_block, preferred_element_type=jnp.float32
    )
    scores = jnp.where(allowed[:, None, None], scores, -jnp.inf)
    new_max = jnp.maximum(run_max, jnp.max(scores, -1))
    rescale = jnp.exp(run_max - new_max)
    exp_scores = jnp.exp(scores - new_max[..., None])
    new_sum = run_sum * rescale + jnp.sum(exp_scores, -1)
    contribution = jnp.einsum(
        "bkgtn,bkhn->bkgth",
        exp_scores.astype(jnp.bfloat16),
        value_block,
        preferred_element_type=jnp.float32,
    )
    return (new_max, new_sum, accumulated * rescale[..., None] + contribution)


def attend_layer(hidden_in, seq_lens, gain, query_w, key_w, value_w, out_w, sizes, phase):
    tm_n, sec_n, tm_at, total_tokens = sizes
    batch_count, tok_count, feature_count = hidden_in.shape
    hidden32 = hidden_in.astype(jnp.float32)
    gain32 = gain.astype(jnp.float32)
    scaled = hidden32 * lax.rsqrt(jnp.mean(hidden32 * hidden32, -1, keepdims=True) + 1e-06)
    layer_input = (scaled * gain32).astype(jnp.bfloat16)
    queries = (
        jnp.einsum("btd,de->bte", layer_input, query_w, preferred_element_type=jnp.float32)
        * HD ** (-0.5)
    ).astype(jnp.bfloat16)
    key_t = jnp.einsum(
        "btd,de->bet", layer_input, key_w, preferred_element_type=jnp.float32
    ).astype(jnp.bfloat16)
    value_t = jnp.einsum(
        "btd,de->bet", layer_input, value_w, preferred_element_type=jnp.float32
    ).astype(jnp.bfloat16)
    kv_local = key_w.shape[1] // HD
    group_size = query_w.shape[1] // key_w.shape[1]
    key_t = key_t.reshape(batch_count, kv_local, HD, tok_count)
    value_t = value_t.reshape(batch_count, kv_local, HD, tok_count)
    query_rows = queries.reshape(batch_count, tok_count, kv_local, group_size, HD)
    query_pos = tm_at * tok_count + jnp.arange(tok_count, dtype=jnp.int32)
    first_valid = total_tokens - seq_lens // STRIDE
    both, key_pos = gather_causal(
        jnp.stack([key_t, value_t], 0), tm_n, sec_n, tm_at, phase, tok_count
    )
    key_count = both.shape[-1]
    block_width = 1024 if key_count % 1024 == 0 else key_count
    rounds = key_count // block_width
    blocks = jnp.moveaxis(
        both.reshape(2, batch_count, kv_local, HD, rounds, block_width), 4, 0
    )
    pos_blocks = key_pos.reshape(rounds, block_width)
    start_state = (
        jnp.full((batch_count, kv_local, group_size, tok_count), -1e30, jnp.float32),
        jnp.zeros((batch_count, kv_local, group_size, tok_count), jnp.float32),
        jnp.zeros((batch_count, kv_local, group_size, tok_count, HD), jnp.float32),
    )
    if rounds == 1:
        result = absorb_block(
            start_state, blocks[0, 0], blocks[0, 1], pos_blocks[0], query_rows, query_pos,
            first_valid,
        )
    else:

        def scan_step(state, block_item):
            kv_block, pos_block = block_item
            return (
                absorb_block(
                    state, kv_block[0], kv_block[1], pos_block, query_rows, query_pos,
                    first_valid,
                ),
                None,
            )

        result, _ = lax.scan(scan_step, start_state, (blocks, pos_blocks))
    run_max, run_sum, accumulated = result
    attended = (accumulated / run_sum[..., None]).astype(jnp.bfloat16)
    attended = attended.transpose(0, 3, 1, 2, 4).reshape(
        batch_count, tok_count, kv_local * group_size * HD
    )
    if out_w is None:
        return attended, key_t, value_t
    partial_value = jnp.einsum("bte,ed->btd", attended, out_w, preferred_element_type=jnp.float32)
    return partial_value, key_t, value_t


def per_device(
    series, lengths, patch_weight, norm_gain, query_weight, key_weight, value_weight, out_weight,
    *, tm_n, mp_n, sec_n
):
    seq_count, channels, steps_dev = series.shape
    tok_count = steps_dev // STRIDE
    tm_at = lax.axis_index("tm")
    mp_at = lax.axis_index("mp")
    sec_at = lax.axis_index("section")
    feat_axes = ("mp", "section")
    feat_n = mp_n * sec_n
    total_steps = steps_dev * tm_n
    total_tokens = tok_count * tm_n

    first_step = total_steps - lengths
    step_pos = tm_at * steps_dev + jnp.arange(steps_dev, dtype=jnp.int32)
    valid = (step_pos[None, :] >= first_step[:, None]).astype(jnp.float32)
    values = series.astype(jnp.float32)
    masked = values * valid[:, None, :]
    local_sum = jnp.sum(masked, -1)
    shard_lo = jnp.arange(tm_n, dtype=jnp.int32) * steps_dev
    counts = jnp.clip(
        shard_lo[None, :] + steps_dev - jnp.maximum(shard_lo[None, :], first_step[:, None]),
        0,
        steps_dev,
    ).astype(jnp.float32)
    my_count = jnp.sum(valid, -1)
    local_mean = local_sum / jnp.maximum(my_count, 1.0)[:, None]
    local_dev = (values - local_mean[..., None]) * valid[:, None, :]
    local_m2 = jnp.sum(local_dev * local_dev, -1)
    tail = series[:, :, steps_dev - STRIDE :]
    if tm_n > SMALL_GROUP:
        stats = lax.all_gather(jnp.stack([local_sum, local_m2], -1), "tm", axis=0)
        prior_raw = shift_from(tail, "tm", tm_n, 1, False).astype(jnp.float32)
    else:
        payload = jnp.concatenate(
            [jnp.stack([local_sum, local_m2], -1), tail.astype(jnp.float32)], -1
        )
        received = [payload] + [shift_from(payload, "tm", tm_n, by, True) for by in range(1, tm_n)]
        prior_raw = received[1][..., 2:] if tm_n > 1 else jnp.zeros_like(payload[..., 2:])
        order = (tm_at - jnp.arange(tm_n, dtype=jnp.int32)) % tm_n
        stats = jnp.take(jnp.stack([piece[..., :2] for piece in received], 0), order, axis=0)
    history = lengths.astype(jnp.float32)[:, None]
    shard_sums = stats[..., 0]
    shard_m2 = stats[..., 1]
    channel_mean = jnp.sum(shard_sums, 0) / history
    shard_counts = jnp.moveaxis(counts, 1, 0)[:, :, None]
    shard_means = shard_sums / jnp.maximum(shard_counts, 1.0)
    gap = shard_means - channel_mean[None]
    spread_total = jnp.sum(shard_m2 + shard_counts * gap * gap, 0)
    variance = spread_total / history
    inv_std = lax.rsqrt(variance + 1e-05)[..., None]

    padded = jnp.concatenate([prior_raw, series.astype(jnp.float32)], -1)
    padded_pos = tm_at * steps_dev - STRIDE + jnp.arange(steps_dev + STRIDE, dtype=jnp.int32)
    padded_valid = (
        (padded_pos[None, :] >= first_step[:, None]) & (padded_pos[None, :] >= 0)
    ).astype(jnp.float32)[:, None, :]
    normed = (
        (padded * padded_valid - channel_mean[..., None]) * padded_valid * inv_std
    ).astype(jnp.bfloat16)
    kernel = patch_weight.reshape(channels, 2 * STRIDE, patch_weight.shape[1])
    chunk_tok = 32 if tok_count % 32 == 0 else tok_count
    chunk_count = tok_count // chunk_tok
    chunks = jnp.stack(
        [
            normed[:, :, q * chunk_tok * STRIDE : (q + 1) * chunk_tok * STRIDE + STRIDE]
            for q in range(chunk_count)
        ],
        1,
    ).reshape(seq_count * chunk_count, channels, chunk_tok * STRIDE + STRIDE)
    tokens = lax.conv_general_dilated(
        chunks,
        kernel,
        window_strides=(STRIDE,),
        padding="VALID",
        dimension_numbers=("NCW", "IWO", "NWC"),
        preferred_element_type=jnp.float32,
    ).astype(jnp.bfloat16)
    tokens = tokens.reshape(seq_count, tok_count, tokens.shape[2])
    column_count = patch_weight.shape[1]
    hidden0 = lax.all_gather(tokens, feat_axes, axis=2, tiled=True)
    feature_count = hidden0.shape[2]
    head_cols = feature_count // mp_n
    sizes = (tm_n, sec_n, tm_at, total_tokens)

    partial0, key0, value0 = attend_layer(
        hidden0, lengths, norm_gain[0], query_weight[0], key_weight[0], value_weight[0],
        out_weight[0], sizes, 0,
    )
    head_sum = None
    for by in range(mp_n):
        pairs = [(m * sec_n, ((m + by) % mp_n) * sec_n + 1) for m in range(mp_n)]
        term = lax.ppermute(partial0.astype(jnp.bfloat16), feat_axes, pairs).astype(jnp.float32)
        head_sum = term if head_sum is None else head_sum + term
    hidden1 = (hidden0.astype(jnp.float32) + head_sum).astype(jnp.bfloat16)

    partial1, key1, value1 = attend_layer(
        hidden1, lengths, norm_gain[0], query_weight[0], key_weight[0], value_weight[0],
        out_weight[0], sizes, 1,
    )
    is_first = sec_at == 0
    key_store = jnp.where(is_first, key0, key1)[None]
    value_store = jnp.where(is_first, value0, value1)[None]

    per_section = seq_count // sec_n
    low_rows = partial1[:per_section]
    high_rows = partial1[per_section:]
    low_hidden = hidden1[:per_section]
    to_low = []
    to_high = []
    for by in range(mp_n):
        target_mp = (mp_at + by) % mp_n
        cols = lax.dynamic_slice_in_dim(low_rows, target_mp * head_cols, head_cols, 2)
        if by == 0:
            residual = lax.dynamic_slice_in_dim(low_hidden, target_mp * head_cols, head_cols, 2)
            cols = residual.astype(jnp.float32) + cols
        pairs = [(m * sec_n + 1, ((m + by) % mp_n) * sec_n) for m in range(mp_n)]
        to_low.append(lax.ppermute(cols.astype(jnp.bfloat16), feat_axes, pairs))
        if by > 0:
            cols_high = lax.dynamic_slice_in_dim(high_rows, target_mp * head_cols, head_cols, 2)
            pairs = [(m * sec_n + 1, ((m + by) % mp_n) * sec_n + 1) for m in range(mp_n)]
            to_high.append(lax.ppermute(cols_high.astype(jnp.bfloat16), feat_axes, pairs))
    low_total = to_low[0].astype(jnp.float32) + sum(
        piece.astype(jnp.float32) for piece in to_low[1:]
    )
    own_high = lax.dynamic_slice_in_dim(high_rows, mp_at * head_cols, head_cols, 2)
    own_hidden = lax.dynamic_slice_in_dim(hidden1[per_section:], mp_at * head_cols, head_cols, 2)
    high_total = own_hidden.astype(jnp.float32) + own_high + sum(
        piece.astype(jnp.float32) for piece in to_high
    )
    final_cols = jnp.where(is_first, low_total, high_total).astype(jnp.bfloat16)
    return (key_store, value_store, final_cols)


def solution(mesh):
    sizes = dict(tm_n=mesh.shape["tm"], mp_n=mesh.shape["mp"], sec_n=mesh.shape["section"])
    in_specs = (
        P("groups", None, "tm"),
        P("groups"),
        P(None, ("mp", "section")),
        P("section", None),
        P("section", None, "mp"),
        P("section", None, "mp"),
        P("section", None, "mp"),
        P("section", "mp", None),
    )
    out_specs = (
        P("section", "groups", "mp", None, "tm"),
        P("section", "groups", "mp", None, "tm"),
        P(("groups", "section"), "tm", "mp"),
    )

    def body(*args):
        return per_device(*args, **sizes)

    return jax.shard_map(body, mesh=mesh, in_specs=in_specs, out_specs=out_specs, check_vma=False)
```

```python
import jax
import jax.numpy as jnp
from jax import lax
from jax.sharding import PartitionSpec as P

STRIDE = 32
HD = 80
SMALL_GROUP = 4


def shift_from(value, axis, size, by, cyclic):
    pairs = [(i, (i + by) % size) for i in range(size) if cyclic or i + by < size]
    return lax.ppermute(value, axis, pairs)


def gather_ordered(value, axis, size, me):
    if size > SMALL_GROUP:
        return lax.all_gather(value, axis, axis=0)
    received = [value] + [shift_from(value, axis, size, by, True) for by in range(1, size)]
    stack = jnp.stack(received, 0)
    order = (me - jnp.arange(size, dtype=jnp.int32)) % size
    return jnp.take(stack, order, axis=0)


def gather_causal(value, tm_n, sec_n, tm_at, phase, width):
    if tm_n > SMALL_GROUP:
        gathered = lax.all_gather(value, "tm", axis=value.ndim - 1, tiled=True)
        return gathered, jnp.arange(tm_n * width, dtype=jnp.int32)
    pieces = []
    positions = []
    local = jnp.arange(width, dtype=jnp.int32)
    for by in range(tm_n - 1, 0, -1):
        pairs = [(t * sec_n + phase, (t + by) * sec_n + phase) for t in range(tm_n - by)]
        pieces.append(lax.ppermute(value, ("tm", "section"), pairs))
        positions.append((tm_at - by) * width + local)
    pieces.append(value)
    positions.append(tm_at * width + local)
    return jnp.concatenate(pieces, -1), jnp.concatenate(positions, 0)


def absorb_block(running, key_block, value_block, key_pos, query_rows, query_pos, first_valid):
    run_max, run_sum, accumulated = running
    allowed = (key_pos[None, None, :] <= query_pos[None, :, None]) & (
        (key_pos[None, None, :] >= first_valid[:, None, None])
        | (key_pos[None, None, :] == query_pos[None, :, None])
    )
    scores = jnp.einsum(
        "btkgh,bkhn->bkgtn", query_rows, key_block, preferred_element_type=jnp.float32
    )
    scores = jnp.where(allowed[:, None, None], scores, -jnp.inf)
    new_max = jnp.maximum(run_max, jnp.max(scores, -1))
    rescale = jnp.exp(run_max - new_max)
    exp_scores = jnp.exp(scores - new_max[..., None])
    new_sum = run_sum * rescale + jnp.sum(exp_scores, -1)
    contribution = jnp.einsum(
        "bkgtn,bkhn->bkgth",
        exp_scores.astype(jnp.bfloat16),
        value_block,
        preferred_element_type=jnp.float32,
    )
    return (new_max, new_sum, accumulated * rescale[..., None] + contribution)


def attend_layer(hidden_in, seq_lens, gain, query_w, key_w, value_w, out_w, sizes, phase):
    tm_n, sec_n, tm_at, total_tokens = sizes
    batch_count, tok_count, feature_count = hidden_in.shape
    hidden32 = hidden_in.astype(jnp.float32)
    gain32 = gain.astype(jnp.float32)
    scaled = hidden32 * lax.rsqrt(jnp.mean(hidden32 * hidden32, -1, keepdims=True) + 1e-06)
    layer_input = (scaled * gain32).astype(jnp.bfloat16)
    queries = (
        jnp.einsum("btd,de->bte", layer_input, query_w, preferred_element_type=jnp.float32)
        * HD ** (-0.5)
    ).astype(jnp.bfloat16)
    key_t = jnp.einsum(
        "btd,de->bet", layer_input, key_w, preferred_element_type=jnp.float32
    ).astype(jnp.bfloat16)
    value_t = jnp.einsum(
        "btd,de->bet", layer_input, value_w, preferred_element_type=jnp.float32
    ).astype(jnp.bfloat16)
    kv_local = key_w.shape[1] // HD
    group_size = query_w.shape[1] // key_w.shape[1]
    key_t = key_t.reshape(batch_count, kv_local, HD, tok_count)
    value_t = value_t.reshape(batch_count, kv_local, HD, tok_count)
    query_rows = queries.reshape(batch_count, tok_count, kv_local, group_size, HD)
    query_pos = tm_at * tok_count + jnp.arange(tok_count, dtype=jnp.int32)
    first_valid = total_tokens - seq_lens // STRIDE
    both, key_pos = gather_causal(
        jnp.stack([key_t, value_t], 0), tm_n, sec_n, tm_at, phase, tok_count
    )
    key_count = both.shape[-1]
    block_width = 1024 if key_count % 1024 == 0 else key_count
    rounds = key_count // block_width
    blocks = jnp.moveaxis(
        both.reshape(2, batch_count, kv_local, HD, rounds, block_width), 4, 0
    )
    pos_blocks = key_pos.reshape(rounds, block_width)
    start_state = (
        jnp.full((batch_count, kv_local, group_size, tok_count), -1e30, jnp.float32),
        jnp.zeros((batch_count, kv_local, group_size, tok_count), jnp.float32),
        jnp.zeros((batch_count, kv_local, group_size, tok_count, HD), jnp.float32),
    )
    if rounds == 1:
        result = absorb_block(
            start_state, blocks[0, 0], blocks[0, 1], pos_blocks[0], query_rows, query_pos,
            first_valid,
        )
    else:

        def scan_step(state, block_item):
            kv_block, pos_block = block_item
            return (
                absorb_block(
                    state, kv_block[0], kv_block[1], pos_block, query_rows, query_pos,
                    first_valid,
                ),
                None,
            )

        result, _ = lax.scan(scan_step, start_state, (blocks, pos_blocks))
    run_max, run_sum, accumulated = result
    attended = (accumulated / run_sum[..., None]).astype(jnp.bfloat16)
    attended = attended.transpose(0, 3, 1, 2, 4).reshape(
        batch_count, tok_count, kv_local * group_size * HD
    )
    if out_w is None:
        return attended, key_t, value_t
    partial_value = jnp.einsum("bte,ed->btd", attended, out_w, preferred_element_type=jnp.float32)
    return partial_value, key_t, value_t, attended


def per_device(
    series, lengths, patch_weight, norm_gain, query_weight, key_weight, value_weight, out_weight,
    *, tm_n, mp_n, sec_n
):
    seq_count, channels, steps_dev = series.shape
    tok_count = steps_dev // STRIDE
    tm_at = lax.axis_index("tm")
    mp_at = lax.axis_index("mp")
    sec_at = lax.axis_index("section")
    feat_axes = ("mp", "section")
    feat_n = mp_n * sec_n
    total_steps = steps_dev * tm_n
    total_tokens = tok_count * tm_n

    first_step = total_steps - lengths
    step_pos = tm_at * steps_dev + jnp.arange(steps_dev, dtype=jnp.int32)
    valid = (step_pos[None, :] >= first_step[:, None]).astype(jnp.float32)
    values = series.astype(jnp.float32)
    masked = values * valid[:, None, :]
    local_sum = jnp.sum(masked, -1)
    shard_lo = jnp.arange(tm_n, dtype=jnp.int32) * steps_dev
    counts = jnp.clip(
        shard_lo[None, :] + steps_dev - jnp.maximum(shard_lo[None, :], first_step[:, None]),
        0,
        steps_dev,
    ).astype(jnp.float32)
    my_count = jnp.sum(valid, -1)
    local_mean = local_sum / jnp.maximum(my_count, 1.0)[:, None]
    local_dev = (values - local_mean[..., None]) * valid[:, None, :]
    local_m2 = jnp.sum(local_dev * local_dev, -1)
    tail = series[:, :, steps_dev - STRIDE :]
    if tm_n > SMALL_GROUP:
        stats = lax.all_gather(jnp.stack([local_sum, local_m2], -1), "tm", axis=0)
        prior_raw = shift_from(tail, "tm", tm_n, 1, False).astype(jnp.float32)
    else:
        payload = jnp.concatenate(
            [jnp.stack([local_sum, local_m2], -1), tail.astype(jnp.float32)], -1
        )
        received = [payload] + [shift_from(payload, "tm", tm_n, by, True) for by in range(1, tm_n)]
        prior_raw = received[1][..., 2:] if tm_n > 1 else jnp.zeros_like(payload[..., 2:])
        order = (tm_at - jnp.arange(tm_n, dtype=jnp.int32)) % tm_n
        stats = jnp.take(jnp.stack([piece[..., :2] for piece in received], 0), order, axis=0)
    history = lengths.astype(jnp.float32)[:, None]
    shard_sums = stats[..., 0]
    shard_m2 = stats[..., 1]
    channel_mean = jnp.sum(shard_sums, 0) / history
    shard_counts = jnp.moveaxis(counts, 1, 0)[:, :, None]
    shard_means = shard_sums / jnp.maximum(shard_counts, 1.0)
    gap = shard_means - channel_mean[None]
    spread_total = jnp.sum(shard_m2 + shard_counts * gap * gap, 0)
    variance = spread_total / history
    inv_std = lax.rsqrt(variance + 1e-05)[..., None]

    padded = jnp.concatenate([prior_raw, series.astype(jnp.float32)], -1)
    padded_pos = tm_at * steps_dev - STRIDE + jnp.arange(steps_dev + STRIDE, dtype=jnp.int32)
    padded_valid = (
        (padded_pos[None, :] >= first_step[:, None]) & (padded_pos[None, :] >= 0)
    ).astype(jnp.float32)[:, None, :]
    normed = (
        (padded * padded_valid - channel_mean[..., None]) * padded_valid * inv_std
    ).astype(jnp.bfloat16)
    kernel = patch_weight.reshape(channels, 2 * STRIDE, patch_weight.shape[1])
    chunk_tok = 32 if tok_count % 32 == 0 else tok_count
    chunk_count = tok_count // chunk_tok
    chunks = jnp.stack(
        [
            normed[:, :, q * chunk_tok * STRIDE : (q + 1) * chunk_tok * STRIDE + STRIDE]
            for q in range(chunk_count)
        ],
        1,
    ).reshape(seq_count * chunk_count, channels, chunk_tok * STRIDE + STRIDE)
    tokens = lax.conv_general_dilated(
        chunks,
        kernel,
        window_strides=(STRIDE,),
        padding="VALID",
        dimension_numbers=("NCW", "IWO", "NWC"),
        preferred_element_type=jnp.float32,
    ).astype(jnp.bfloat16)
    tokens = tokens.reshape(seq_count, tok_count, tokens.shape[2])
    column_count = patch_weight.shape[1]
    rows_out, tokens = lax.optimization_barrier((out_weight[0], tokens))
    on_chip = [(m * sec_n, m * sec_n + 1) for m in range(mp_n)]
    partner_rows = lax.ppermute(rows_out, feat_axes, on_chip)
    hidden0 = lax.all_gather(tokens, feat_axes, axis=2, tiled=True)
    feature_count = hidden0.shape[2]
    head_cols = feature_count // mp_n
    sizes = (tm_n, sec_n, tm_at, total_tokens)

    partial0, key0, value0, attended0 = attend_layer(
        hidden0, lengths, norm_gain[0], query_weight[0], key_weight[0], value_weight[0],
        out_weight[0], sizes, 0,
    )
    arrived = lax.ppermute(attended0, feat_axes, on_chip)
    head_sum = jnp.einsum("bte,ed->btd", arrived, partner_rows, preferred_element_type=jnp.float32)
    for by in range(1, mp_n):
        pairs = [(m * sec_n, ((m + by) % mp_n) * sec_n + 1) for m in range(mp_n)]
        term = lax.ppermute(partial0.astype(jnp.bfloat16), feat_axes, pairs).astype(jnp.float32)
        head_sum = head_sum + term
    hidden1 = (hidden0.astype(jnp.float32) + head_sum).astype(jnp.bfloat16)

    partial1, key1, value1, _ = attend_layer(
        hidden1, lengths, norm_gain[0], query_weight[0], key_weight[0], value_weight[0],
        out_weight[0], sizes, 1,
    )
    is_first = sec_at == 0
    key_store = jnp.where(is_first, key0, key1)[None]
    value_store = jnp.where(is_first, value0, value1)[None]

    per_section = seq_count // sec_n
    low_rows = partial1[:per_section]
    high_rows = partial1[per_section:]
    low_hidden = hidden1[:per_section]
    to_low = []
    to_high = []
    for by in range(mp_n):
        target_mp = (mp_at + by) % mp_n
        cols = lax.dynamic_slice_in_dim(low_rows, target_mp * head_cols, head_cols, 2)
        if by == 0:
            residual = lax.dynamic_slice_in_dim(low_hidden, target_mp * head_cols, head_cols, 2)
            cols = residual.astype(jnp.float32) + cols
        pairs = [(m * sec_n + 1, ((m + by) % mp_n) * sec_n) for m in range(mp_n)]
        to_low.append(lax.ppermute(cols.astype(jnp.bfloat16), feat_axes, pairs))
        if by > 0:
            cols_high = lax.dynamic_slice_in_dim(high_rows, target_mp * head_cols, head_cols, 2)
            pairs = [(m * sec_n + 1, ((m + by) % mp_n) * sec_n + 1) for m in range(mp_n)]
            to_high.append(lax.ppermute(cols_high.astype(jnp.bfloat16), feat_axes, pairs))
    low_total = to_low[0].astype(jnp.float32) + sum(
        piece.astype(jnp.float32) for piece in to_low[1:]
    )
    own_high = lax.dynamic_slice_in_dim(high_rows, mp_at * head_cols, head_cols, 2)
    own_hidden = lax.dynamic_slice_in_dim(hidden1[per_section:], mp_at * head_cols, head_cols, 2)
    high_total = own_hidden.astype(jnp.float32) + own_high + sum(
        piece.astype(jnp.float32) for piece in to_high
    )
    final_cols = jnp.where(is_first, low_total, high_total).astype(jnp.bfloat16)
    return (key_store, value_store, final_cols)


def solution(mesh):
    sizes = dict(tm_n=mesh.shape["tm"], mp_n=mesh.shape["mp"], sec_n=mesh.shape["section"])
    in_specs = (
        P("groups", None, "tm"),
        P("groups"),
        P(None, ("mp", "section")),
        P("section", None),
        P("section", None, "mp"),
        P("section", None, "mp"),
        P("section", None, "mp"),
        P("section", "mp", None),
    )
    out_specs = (
        P("section", "groups", "mp", None, "tm"),
        P("section", "groups", "mp", None, "tm"),
        P(("groups", "section"), "tm", "mp"),
    )

    def body(*args):
        return per_device(*args, **sizes)

    return jax.shard_map(body, mesh=mesh, in_specs=in_specs, out_specs=out_specs, check_vma=False)
```

```python
import jax
import jax.numpy as jnp
from jax import lax
from jax.sharding import PartitionSpec as P

STRIDE = 32
HD = 80
SMALL_GROUP = 4


def shift_from(value, axis, size, by, cyclic):
    pairs = [(i, (i + by) % size) for i in range(size) if cyclic or i + by < size]
    return lax.ppermute(value, axis, pairs)


def gather_ordered(value, axis, size, me):
    if size > SMALL_GROUP:
        return lax.all_gather(value, axis, axis=0)
    received = [value] + [shift_from(value, axis, size, by, True) for by in range(1, size)]
    stack = jnp.stack(received, 0)
    order = (me - jnp.arange(size, dtype=jnp.int32)) % size
    return jnp.take(stack, order, axis=0)


def gather_causal(value, tm_n, sec_n, tm_at, phase, width):
    if tm_n > SMALL_GROUP:
        gathered = lax.all_gather(value, "tm", axis=value.ndim - 1, tiled=True)
        return gathered, jnp.arange(tm_n * width, dtype=jnp.int32)
    pieces = []
    positions = []
    local = jnp.arange(width, dtype=jnp.int32)
    for by in range(tm_n - 1, 0, -1):
        pairs = [(t * sec_n + phase, (t + by) * sec_n + phase) for t in range(tm_n - by)]
        pieces.append(lax.ppermute(value, ("tm", "section"), pairs))
        positions.append((tm_at - by) * width + local)
    pieces.append(value)
    positions.append(tm_at * width + local)
    return jnp.concatenate(pieces, -1), jnp.concatenate(positions, 0)


def absorb_block(running, key_block, value_block, key_pos, query_rows, query_pos, first_valid):
    run_max, run_sum, accumulated = running
    allowed = (key_pos[None, None, :] <= query_pos[None, :, None]) & (
        (key_pos[None, None, :] >= first_valid[:, None, None])
        | (key_pos[None, None, :] == query_pos[None, :, None])
    )
    scores = jnp.einsum(
        "btkgh,bkhn->bkgtn", query_rows, key_block, preferred_element_type=jnp.float32
    )
    scores = jnp.where(allowed[:, None, None], scores, -jnp.inf)
    new_max = jnp.maximum(run_max, jnp.max(scores, -1))
    rescale = jnp.exp(run_max - new_max)
    exp_scores = jnp.exp(scores - new_max[..., None])
    new_sum = run_sum * rescale + jnp.sum(exp_scores, -1)
    contribution = jnp.einsum(
        "bkgtn,bkhn->bkgth",
        exp_scores.astype(jnp.bfloat16),
        value_block,
        preferred_element_type=jnp.float32,
    )
    return (new_max, new_sum, accumulated * rescale[..., None] + contribution)


def attend_layer(hidden_in, seq_lens, gain, query_w, key_w, value_w, out_w, sizes, phase):
    tm_n, sec_n, tm_at, total_tokens = sizes
    batch_count, tok_count, feature_count = hidden_in.shape
    hidden32 = hidden_in.astype(jnp.float32)
    gain32 = gain.astype(jnp.float32)
    scaled = hidden32 * lax.rsqrt(jnp.mean(hidden32 * hidden32, -1, keepdims=True) + 1e-06)
    layer_input = (scaled * gain32).astype(jnp.bfloat16)
    queries = (
        jnp.einsum("btd,de->bte", layer_input, query_w, preferred_element_type=jnp.float32)
        * HD ** (-0.5)
    ).astype(jnp.bfloat16)
    kv_local = key_w.shape[1] // HD
    group_size = query_w.shape[1] // key_w.shape[1]
    kv_t = jnp.einsum(
        "btd,de->bet", layer_input, jnp.concatenate([key_w, value_w], 1),
        preferred_element_type=jnp.float32,
    ).astype(jnp.bfloat16)
    kv_t = kv_t.reshape(batch_count, 2, kv_local, HD, tok_count)
    key_t = kv_t[:, 0]
    value_t = kv_t[:, 1]
    query_rows = queries.reshape(batch_count, tok_count, kv_local, group_size, HD)
    query_pos = tm_at * tok_count + jnp.arange(tok_count, dtype=jnp.int32)
    first_valid = total_tokens - seq_lens // STRIDE
    both, key_pos = gather_causal(kv_t, tm_n, sec_n, tm_at, phase, tok_count)
    key_count = both.shape[-1]
    block_width = 1024 if key_count % 1024 == 0 else key_count
    rounds = key_count // block_width
    blocks = jnp.moveaxis(
        both.reshape(batch_count, 2, kv_local, HD, rounds, block_width), 4, 0
    )
    pos_blocks = key_pos.reshape(rounds, block_width)
    start_state = (
        jnp.full((batch_count, kv_local, group_size, tok_count), -1e30, jnp.float32),
        jnp.zeros((batch_count, kv_local, group_size, tok_count), jnp.float32),
        jnp.zeros((batch_count, kv_local, group_size, tok_count, HD), jnp.float32),
    )
    if rounds == 1:
        result = absorb_block(
            start_state, blocks[0][:, 0], blocks[0][:, 1], pos_blocks[0], query_rows, query_pos,
            first_valid,
        )
    else:

        def scan_step(state, block_item):
            kv_block, pos_block = block_item
            return (
                absorb_block(
                    state, kv_block[:, 0], kv_block[:, 1], pos_block, query_rows, query_pos,
                    first_valid,
                ),
                None,
            )

        result, _ = lax.scan(scan_step, start_state, (blocks, pos_blocks))
    run_max, run_sum, accumulated = result
    attended = (accumulated / run_sum[..., None]).astype(jnp.bfloat16)
    attended = attended.transpose(0, 3, 1, 2, 4).reshape(
        batch_count, tok_count, kv_local * group_size * HD
    )
    if out_w is None:
        return attended, key_t, value_t
    partial_value = jnp.einsum("bte,ed->btd", attended, out_w, preferred_element_type=jnp.float32)
    return partial_value, key_t, value_t


def per_device(
    series, lengths, patch_weight, norm_gain, query_weight, key_weight, value_weight, out_weight,
    *, tm_n, mp_n, sec_n
):
    seq_count, channels, steps_dev = series.shape
    tok_count = steps_dev // STRIDE
    tm_at = lax.axis_index("tm")
    mp_at = lax.axis_index("mp")
    sec_at = lax.axis_index("section")
    feat_axes = ("mp", "section")
    feat_n = mp_n * sec_n
    total_steps = steps_dev * tm_n
    total_tokens = tok_count * tm_n

    first_step = total_steps - lengths
    step_pos = tm_at * steps_dev + jnp.arange(steps_dev, dtype=jnp.int32)
    valid = (step_pos[None, :] >= first_step[:, None]).astype(jnp.float32)
    values = series.astype(jnp.float32)
    masked = values * valid[:, None, :]
    local_sum = jnp.sum(masked, -1)
    shard_lo = jnp.arange(tm_n, dtype=jnp.int32) * steps_dev
    counts = jnp.clip(
        shard_lo[None, :] + steps_dev - jnp.maximum(shard_lo[None, :], first_step[:, None]),
        0,
        steps_dev,
    ).astype(jnp.float32)
    my_count = jnp.sum(valid, -1)
    local_mean = local_sum / jnp.maximum(my_count, 1.0)[:, None]
    local_dev = (values - local_mean[..., None]) * valid[:, None, :]
    local_m2 = jnp.sum(local_dev * local_dev, -1)
    tail = series[:, :, steps_dev - STRIDE :]
    if tm_n > SMALL_GROUP:
        stats = lax.all_gather(jnp.stack([local_sum, local_m2], -1), "tm", axis=0)
        prior_raw = shift_from(tail, "tm", tm_n, 1, False).astype(jnp.float32)
    else:
        payload = jnp.concatenate(
            [jnp.stack([local_sum, local_m2], -1), tail.astype(jnp.float32)], -1
        )
        received = [payload] + [shift_from(payload, "tm", tm_n, by, True) for by in range(1, tm_n)]
        prior_raw = received[1][..., 2:] if tm_n > 1 else jnp.zeros_like(payload[..., 2:])
        order = (tm_at - jnp.arange(tm_n, dtype=jnp.int32)) % tm_n
        stats = jnp.take(jnp.stack([piece[..., :2] for piece in received], 0), order, axis=0)
    history = lengths.astype(jnp.float32)[:, None]
    shard_sums = stats[..., 0]
    shard_m2 = stats[..., 1]
    channel_mean = jnp.sum(shard_sums, 0) / history
    shard_counts = jnp.moveaxis(counts, 1, 0)[:, :, None]
    shard_means = shard_sums / jnp.maximum(shard_counts, 1.0)
    gap = shard_means - channel_mean[None]
    spread_total = jnp.sum(shard_m2 + shard_counts * gap * gap, 0)
    variance = spread_total / history
    inv_std = lax.rsqrt(variance + 1e-05)[..., None]

    padded = jnp.concatenate([prior_raw, series.astype(jnp.float32)], -1)
    padded_pos = tm_at * steps_dev - STRIDE + jnp.arange(steps_dev + STRIDE, dtype=jnp.int32)
    padded_valid = (
        (padded_pos[None, :] >= first_step[:, None]) & (padded_pos[None, :] >= 0)
    ).astype(jnp.float32)[:, None, :]
    normed = (
        (padded * padded_valid - channel_mean[..., None]) * padded_valid * inv_std
    ).astype(jnp.bfloat16)
    kernel = patch_weight.reshape(channels, 2 * STRIDE, patch_weight.shape[1])
    chunk_tok = 32 if tok_count % 32 == 0 else tok_count
    chunk_count = tok_count // chunk_tok
    chunks = jnp.stack(
        [
            normed[:, :, q * chunk_tok * STRIDE : (q + 1) * chunk_tok * STRIDE + STRIDE]
            for q in range(chunk_count)
        ],
        1,
    ).reshape(seq_count * chunk_count, channels, chunk_tok * STRIDE + STRIDE)
    tokens = lax.conv_general_dilated(
        chunks,
        kernel,
        window_strides=(STRIDE,),
        padding="VALID",
        dimension_numbers=("NCW", "IWO", "NWC"),
        preferred_element_type=jnp.float32,
    ).astype(jnp.bfloat16)
    tokens = tokens.reshape(seq_count, tok_count, tokens.shape[2])
    column_count = patch_weight.shape[1]
    hidden0 = lax.all_gather(tokens, feat_axes, axis=2, tiled=True)
    feature_count = hidden0.shape[2]
    head_cols = feature_count // mp_n
    sizes = (tm_n, sec_n, tm_at, total_tokens)

    partial0, key0, value0 = attend_layer(
        hidden0, lengths, norm_gain[0], query_weight[0], key_weight[0], value_weight[0],
        out_weight[0], sizes, 0,
    )
    head_sum = None
    for by in range(mp_n):
        pairs = [(m * sec_n, ((m + by) % mp_n) * sec_n + 1) for m in range(mp_n)]
        term = lax.ppermute(partial0.astype(jnp.bfloat16), feat_axes, pairs).astype(jnp.float32)
        head_sum = term if head_sum is None else head_sum + term
    hidden1 = (hidden0.astype(jnp.float32) + head_sum).astype(jnp.bfloat16)

    partial1, key1, value1 = attend_layer(
        hidden1, lengths, norm_gain[0], query_weight[0], key_weight[0], value_weight[0],
        out_weight[0], sizes, 1,
    )
    is_first = sec_at == 0
    key_store = jnp.where(is_first, key0, key1)[None]
    value_store = jnp.where(is_first, value0, value1)[None]

    per_section = seq_count // sec_n
    low_rows = partial1[:per_section]
    high_rows = partial1[per_section:]
    low_hidden = hidden1[:per_section]
    to_low = []
    to_high = []
    for by in range(mp_n):
        target_mp = (mp_at + by) % mp_n
        cols = lax.dynamic_slice_in_dim(low_rows, target_mp * head_cols, head_cols, 2)
        if by == 0:
            residual = lax.dynamic_slice_in_dim(low_hidden, target_mp * head_cols, head_cols, 2)
            cols = residual.astype(jnp.float32) + cols
        pairs = [(m * sec_n + 1, ((m + by) % mp_n) * sec_n) for m in range(mp_n)]
        to_low.append(lax.ppermute(cols.astype(jnp.bfloat16), feat_axes, pairs))
        if by > 0:
            cols_high = lax.dynamic_slice_in_dim(high_rows, target_mp * head_cols, head_cols, 2)
            pairs = [(m * sec_n + 1, ((m + by) % mp_n) * sec_n + 1) for m in range(mp_n)]
            to_high.append(lax.ppermute(cols_high.astype(jnp.bfloat16), feat_axes, pairs))
    low_total = to_low[0].astype(jnp.float32) + sum(
        piece.astype(jnp.float32) for piece in to_low[1:]
    )
    own_high = lax.dynamic_slice_in_dim(high_rows, mp_at * head_cols, head_cols, 2)
    own_hidden = lax.dynamic_slice_in_dim(hidden1[per_section:], mp_at * head_cols, head_cols, 2)
    high_total = own_hidden.astype(jnp.float32) + own_high + sum(
        piece.astype(jnp.float32) for piece in to_high
    )
    final_cols = jnp.where(is_first, low_total, high_total).astype(jnp.bfloat16)
    return (key_store, value_store, final_cols)


def solution(mesh):
    sizes = dict(tm_n=mesh.shape["tm"], mp_n=mesh.shape["mp"], sec_n=mesh.shape["section"])
    in_specs = (
        P("groups", None, "tm"),
        P("groups"),
        P(None, ("mp", "section")),
        P("section", None),
        P("section", None, "mp"),
        P("section", None, "mp"),
        P("section", None, "mp"),
        P("section", "mp", None),
    )
    out_specs = (
        P("section", "groups", "mp", None, "tm"),
        P("section", "groups", "mp", None, "tm"),
        P(("groups", "section"), "tm", "mp"),
    )

    def body(*args):
        return per_device(*args, **sizes)

    return jax.shard_map(body, mesh=mesh, in_specs=in_specs, out_specs=out_specs, check_vma=False)
```

```python
import jax
import jax.numpy as jnp
from jax import lax
from jax.sharding import PartitionSpec as P

STRIDE = 32
HD = 80
SMALL_GROUP = 4


def shift_from(value, axis, size, by, cyclic):
    pairs = [(i, (i + by) % size) for i in range(size) if cyclic or i + by < size]
    return lax.ppermute(value, axis, pairs)


def gather_ordered(value, axis, size, me):
    if size > SMALL_GROUP:
        return lax.all_gather(value, axis, axis=0)
    received = [value] + [shift_from(value, axis, size, by, True) for by in range(1, size)]
    stack = jnp.stack(received, 0)
    order = (me - jnp.arange(size, dtype=jnp.int32)) % size
    return jnp.take(stack, order, axis=0)


def gather_causal(value, tm_n, sec_n, tm_at, phase, width):
    if tm_n > SMALL_GROUP:
        gathered = lax.all_gather(value, "tm", axis=value.ndim - 1, tiled=True)
        return gathered, jnp.arange(tm_n * width, dtype=jnp.int32)
    pieces = []
    positions = []
    local = jnp.arange(width, dtype=jnp.int32)
    for by in range(tm_n - 1, 0, -1):
        pairs = [(t * sec_n + phase, (t + by) * sec_n + phase) for t in range(tm_n - by)]
        pieces.append(lax.ppermute(value, ("tm", "section"), pairs))
        positions.append((tm_at - by) * width + local)
    pieces.append(value)
    positions.append(tm_at * width + local)
    return jnp.concatenate(pieces, -1), jnp.concatenate(positions, 0)


def absorb_block(running, key_block, value_block, key_pos, query_rows, query_pos, first_valid):
    run_max, run_sum, accumulated = running
    allowed = (key_pos[None, None, :] <= query_pos[None, :, None]) & (
        (key_pos[None, None, :] >= first_valid[:, None, None])
        | (key_pos[None, None, :] == query_pos[None, :, None])
    )
    scores = jnp.einsum(
        "btkgh,bkhn->bkgtn", query_rows, key_block, preferred_element_type=jnp.float32
    )
    scores = jnp.where(allowed[:, None, None], scores, -jnp.inf)
    new_max = jnp.maximum(run_max, jnp.max(scores, -1))
    rescale = jnp.exp(run_max - new_max)
    exp_scores = jnp.exp(scores - new_max[..., None])
    new_sum = run_sum * rescale + jnp.sum(exp_scores, -1)
    contribution = jnp.einsum(
        "bkgtn,bkhn->bkgth",
        exp_scores.astype(jnp.bfloat16),
        value_block,
        preferred_element_type=jnp.float32,
    )
    return (new_max, new_sum, accumulated * rescale[..., None] + contribution)


def attend_layer(hidden_in, seq_lens, gain, query_w, key_w, value_w, out_w, sizes, phase):
    tm_n, sec_n, tm_at, total_tokens = sizes
    batch_count, tok_count, feature_count = hidden_in.shape
    hidden32 = hidden_in.astype(jnp.float32)
    gain32 = gain.astype(jnp.float32)
    scaled = hidden32 * lax.rsqrt(jnp.mean(hidden32 * hidden32, -1, keepdims=True) + 1e-06)
    layer_input = (scaled * gain32).astype(jnp.bfloat16)
    queries = (
        jnp.einsum("btd,de->bte", layer_input, query_w, preferred_element_type=jnp.float32)
        * HD ** (-0.5)
    ).astype(jnp.bfloat16)
    kv_local = key_w.shape[1] // HD
    group_size = query_w.shape[1] // key_w.shape[1]
    kv_t = jnp.einsum(
        "btd,de->ebt", layer_input, jnp.concatenate([key_w, value_w], 1),
        preferred_element_type=jnp.float32,
    ).astype(jnp.bfloat16)
    kv_t = kv_t.reshape(2, kv_local, HD, batch_count, tok_count).transpose(0, 3, 1, 2, 4)
    key_t = kv_t[0]
    value_t = kv_t[1]
    query_rows = queries.reshape(batch_count, tok_count, kv_local, group_size, HD)
    query_pos = tm_at * tok_count + jnp.arange(tok_count, dtype=jnp.int32)
    first_valid = total_tokens - seq_lens // STRIDE
    both, key_pos = gather_causal(kv_t, tm_n, sec_n, tm_at, phase, tok_count)
    key_count = both.shape[-1]
    block_width = 1024 if key_count % 1024 == 0 else key_count
    rounds = key_count // block_width
    blocks = jnp.moveaxis(
        both.reshape(2, batch_count, kv_local, HD, rounds, block_width), 4, 0
    )
    pos_blocks = key_pos.reshape(rounds, block_width)
    start_state = (
        jnp.full((batch_count, kv_local, group_size, tok_count), -1e30, jnp.float32),
        jnp.zeros((batch_count, kv_local, group_size, tok_count), jnp.float32),
        jnp.zeros((batch_count, kv_local, group_size, tok_count, HD), jnp.float32),
    )
    if rounds == 1:
        result = absorb_block(
            start_state, blocks[0, 0], blocks[0, 1], pos_blocks[0], query_rows, query_pos,
            first_valid,
        )
    else:

        def scan_step(state, block_item):
            kv_block, pos_block = block_item
            return (
                absorb_block(
                    state, kv_block[0], kv_block[1], pos_block, query_rows, query_pos,
                    first_valid,
                ),
                None,
            )

        result, _ = lax.scan(scan_step, start_state, (blocks, pos_blocks))
    run_max, run_sum, accumulated = result
    attended = (accumulated / run_sum[..., None]).astype(jnp.bfloat16)
    attended = attended.transpose(0, 3, 1, 2, 4).reshape(
        batch_count, tok_count, kv_local * group_size * HD
    )
    if out_w is None:
        return attended, key_t, value_t
    partial_value = jnp.einsum("bte,ed->btd", attended, out_w, preferred_element_type=jnp.float32)
    return partial_value, key_t, value_t


def per_device(
    series, lengths, patch_weight, norm_gain, query_weight, key_weight, value_weight, out_weight,
    *, tm_n, mp_n, sec_n
):
    seq_count, channels, steps_dev = series.shape
    tok_count = steps_dev // STRIDE
    tm_at = lax.axis_index("tm")
    mp_at = lax.axis_index("mp")
    sec_at = lax.axis_index("section")
    feat_axes = ("mp", "section")
    feat_n = mp_n * sec_n
    total_steps = steps_dev * tm_n
    total_tokens = tok_count * tm_n

    first_step = total_steps - lengths
    step_pos = tm_at * steps_dev + jnp.arange(steps_dev, dtype=jnp.int32)
    valid = (step_pos[None, :] >= first_step[:, None]).astype(jnp.float32)
    values = series.astype(jnp.float32)
    masked = values * valid[:, None, :]
    local_sum = jnp.sum(masked, -1)
    shard_lo = jnp.arange(tm_n, dtype=jnp.int32) * steps_dev
    counts = jnp.clip(
        shard_lo[None, :] + steps_dev - jnp.maximum(shard_lo[None, :], first_step[:, None]),
        0,
        steps_dev,
    ).astype(jnp.float32)
    my_count = jnp.sum(valid, -1)
    local_mean = local_sum / jnp.maximum(my_count, 1.0)[:, None]
    local_dev = (values - local_mean[..., None]) * valid[:, None, :]
    local_m2 = jnp.sum(local_dev * local_dev, -1)
    tail = series[:, :, steps_dev - STRIDE :]
    if tm_n > SMALL_GROUP:
        stats = lax.all_gather(jnp.stack([local_sum, local_m2], -1), "tm", axis=0)
        prior_raw = shift_from(tail, "tm", tm_n, 1, False).astype(jnp.float32)
    else:
        payload = jnp.concatenate(
            [jnp.stack([local_sum, local_m2], -1), tail.astype(jnp.float32)], -1
        )
        received = [payload] + [shift_from(payload, "tm", tm_n, by, True) for by in range(1, tm_n)]
        prior_raw = received[1][..., 2:] if tm_n > 1 else jnp.zeros_like(payload[..., 2:])
        order = (tm_at - jnp.arange(tm_n, dtype=jnp.int32)) % tm_n
        stats = jnp.take(jnp.stack([piece[..., :2] for piece in received], 0), order, axis=0)
    history = lengths.astype(jnp.float32)[:, None]
    shard_sums = stats[..., 0]
    shard_m2 = stats[..., 1]
    channel_mean = jnp.sum(shard_sums, 0) / history
    shard_counts = jnp.moveaxis(counts, 1, 0)[:, :, None]
    shard_means = shard_sums / jnp.maximum(shard_counts, 1.0)
    gap = shard_means - channel_mean[None]
    spread_total = jnp.sum(shard_m2 + shard_counts * gap * gap, 0)
    variance = spread_total / history
    inv_std = lax.rsqrt(variance + 1e-05)[..., None]

    padded = jnp.concatenate([prior_raw, series.astype(jnp.float32)], -1)
    padded_pos = tm_at * steps_dev - STRIDE + jnp.arange(steps_dev + STRIDE, dtype=jnp.int32)
    padded_valid = (
        (padded_pos[None, :] >= first_step[:, None]) & (padded_pos[None, :] >= 0)
    ).astype(jnp.float32)[:, None, :]
    normed = (
        (padded * padded_valid - channel_mean[..., None]) * padded_valid * inv_std
    ).astype(jnp.bfloat16)
    kernel = patch_weight.reshape(channels, 2 * STRIDE, patch_weight.shape[1])
    chunk_tok = 32 if tok_count % 32 == 0 else tok_count
    chunk_count = tok_count // chunk_tok
    chunks = jnp.stack(
        [
            normed[:, :, q * chunk_tok * STRIDE : (q + 1) * chunk_tok * STRIDE + STRIDE]
            for q in range(chunk_count)
        ],
        1,
    ).reshape(seq_count * chunk_count, channels, chunk_tok * STRIDE + STRIDE)
    tokens = lax.conv_general_dilated(
        chunks,
        kernel,
        window_strides=(STRIDE,),
        padding="VALID",
        dimension_numbers=("NCW", "IWO", "NWC"),
        preferred_element_type=jnp.float32,
    ).astype(jnp.bfloat16)
    tokens = tokens.reshape(seq_count, tok_count, tokens.shape[2])
    column_count = patch_weight.shape[1]
    hidden0 = lax.all_gather(tokens, feat_axes, axis=2, tiled=True)
    feature_count = hidden0.shape[2]
    head_cols = feature_count // mp_n
    sizes = (tm_n, sec_n, tm_at, total_tokens)

    partial0, key0, value0 = attend_layer(
        hidden0, lengths, norm_gain[0], query_weight[0], key_weight[0], value_weight[0],
        out_weight[0], sizes, 0,
    )
    head_sum = None
    for by in range(mp_n):
        pairs = [(m * sec_n, ((m + by) % mp_n) * sec_n + 1) for m in range(mp_n)]
        term = lax.ppermute(partial0.astype(jnp.bfloat16), feat_axes, pairs).astype(jnp.float32)
        head_sum = term if head_sum is None else head_sum + term
    hidden1 = (hidden0.astype(jnp.float32) + head_sum).astype(jnp.bfloat16)

    partial1, key1, value1 = attend_layer(
        hidden1, lengths, norm_gain[0], query_weight[0], key_weight[0], value_weight[0],
        out_weight[0], sizes, 1,
    )
    is_first = sec_at == 0
    key_store = jnp.where(is_first, key0, key1)[None]
    value_store = jnp.where(is_first, value0, value1)[None]

    per_section = seq_count // sec_n
    low_rows = partial1[:per_section]
    high_rows = partial1[per_section:]
    low_hidden = hidden1[:per_section]
    to_low = []
    to_high = []
    for by in range(mp_n):
        target_mp = (mp_at + by) % mp_n
        cols = lax.dynamic_slice_in_dim(low_rows, target_mp * head_cols, head_cols, 2)
        if by == 0:
            residual = lax.dynamic_slice_in_dim(low_hidden, target_mp * head_cols, head_cols, 2)
            cols = residual.astype(jnp.float32) + cols
        pairs = [(m * sec_n + 1, ((m + by) % mp_n) * sec_n) for m in range(mp_n)]
        to_low.append(lax.ppermute(cols.astype(jnp.bfloat16), feat_axes, pairs))
        if by > 0:
            cols_high = lax.dynamic_slice_in_dim(high_rows, target_mp * head_cols, head_cols, 2)
            pairs = [(m * sec_n + 1, ((m + by) % mp_n) * sec_n + 1) for m in range(mp_n)]
            to_high.append(lax.ppermute(cols_high.astype(jnp.bfloat16), feat_axes, pairs))
    low_total = to_low[0].astype(jnp.float32) + sum(
        piece.astype(jnp.float32) for piece in to_low[1:]
    )
    own_high = lax.dynamic_slice_in_dim(high_rows, mp_at * head_cols, head_cols, 2)
    own_hidden = lax.dynamic_slice_in_dim(hidden1[per_section:], mp_at * head_cols, head_cols, 2)
    high_total = own_hidden.astype(jnp.float32) + own_high + sum(
        piece.astype(jnp.float32) for piece in to_high
    )
    final_cols = jnp.where(is_first, low_total, high_total).astype(jnp.bfloat16)
    return (key_store, value_store, final_cols)


def solution(mesh):
    sizes = dict(tm_n=mesh.shape["tm"], mp_n=mesh.shape["mp"], sec_n=mesh.shape["section"])
    in_specs = (
        P("groups", None, "tm"),
        P("groups"),
        P(None, ("mp", "section")),
        P("section", None),
        P("section", None, "mp"),
        P("section", None, "mp"),
        P("section", None, "mp"),
        P("section", "mp", None),
    )
    out_specs = (
        P("section", "groups", "mp", None, "tm"),
        P("section", "groups", "mp", None, "tm"),
        P(("groups", "section"), "tm", "mp"),
    )

    def body(*args):
        return per_device(*args, **sizes)

    return jax.shard_map(body, mesh=mesh, in_specs=in_specs, out_specs=out_specs, check_vma=False)
```

```python
import jax
import jax.numpy as jnp
from jax import lax
from jax.sharding import PartitionSpec as P

STRIDE = 32
HD = 80
SMALL_GROUP = 4


def shift_from(value, axis, size, by, cyclic):
    pairs = [(i, (i + by) % size) for i in range(size) if cyclic or i + by < size]
    return lax.ppermute(value, axis, pairs)


def gather_ordered(value, axis, size, me):
    if size > SMALL_GROUP:
        return lax.all_gather(value, axis, axis=0)
    received = [value] + [shift_from(value, axis, size, by, True) for by in range(1, size)]
    stack = jnp.stack(received, 0)
    order = (me - jnp.arange(size, dtype=jnp.int32)) % size
    return jnp.take(stack, order, axis=0)


def gather_causal(value, tm_n, sec_n, tm_at, phase, width):
    if tm_n > SMALL_GROUP:
        gathered = lax.all_gather(value, "tm", axis=value.ndim - 1, tiled=True)
        return gathered, jnp.arange(tm_n * width, dtype=jnp.int32)
    pieces = []
    positions = []
    local = jnp.arange(width, dtype=jnp.int32)
    for by in range(tm_n - 1, 0, -1):
        pairs = [(t * sec_n + phase, (t + by) * sec_n + phase) for t in range(tm_n - by)]
        pieces.append(lax.ppermute(value, ("tm", "section"), pairs))
        positions.append((tm_at - by) * width + local)
    pieces.append(value)
    positions.append(tm_at * width + local)
    return jnp.concatenate(pieces, -1), jnp.concatenate(positions, 0)


def absorb_block(running, key_block, value_block, key_pos, query_rows, query_pos, first_valid):
    run_max, run_sum, accumulated = running
    allowed = (key_pos[None, None, :] <= query_pos[None, :, None]) & (
        (key_pos[None, None, :] >= first_valid[:, None, None])
        | (key_pos[None, None, :] == query_pos[None, :, None])
    )
    scores = jnp.einsum(
        "btkgh,bkhn->bkgtn", query_rows, key_block, preferred_element_type=jnp.float32
    )
    scores = jnp.where(allowed[:, None, None], scores, -jnp.inf)
    new_max = jnp.maximum(run_max, jnp.max(scores, -1))
    rescale = jnp.exp(run_max - new_max)
    exp_scores = jnp.exp(scores - new_max[..., None])
    new_sum = run_sum * rescale + jnp.sum(exp_scores, -1)
    contribution = jnp.einsum(
        "bkgtn,bkhn->bkgth",
        exp_scores.astype(jnp.bfloat16),
        value_block,
        preferred_element_type=jnp.float32,
    )
    return (new_max, new_sum, accumulated * rescale[..., None] + contribution)


def attend_layer(hidden_in, seq_lens, gain, query_w, key_w, value_w, out_w, sizes, phase):
    tm_n, sec_n, tm_at, total_tokens = sizes
    batch_count, tok_count, feature_count = hidden_in.shape
    hidden32 = hidden_in.astype(jnp.float32)
    gain32 = gain.astype(jnp.float32)
    scaled = hidden32 * lax.rsqrt(jnp.mean(hidden32 * hidden32, -1, keepdims=True) + 1e-06)
    layer_input = (scaled * gain32).astype(jnp.bfloat16)
    queries = (
        jnp.einsum("btd,de->bte", layer_input, query_w, preferred_element_type=jnp.float32)
        * HD ** (-0.5)
    ).astype(jnp.bfloat16)
    kv_local = key_w.shape[1] // HD
    group_size = query_w.shape[1] // key_w.shape[1]
    kv_t = jnp.einsum(
        "btd,de->ebt", layer_input, jnp.concatenate([key_w, value_w], 1),
        preferred_element_type=jnp.float32,
    ).astype(jnp.bfloat16)
    kv_t = kv_t.reshape(2, kv_local, HD, batch_count, tok_count).transpose(0, 3, 1, 2, 4)
    key_t = kv_t[0]
    value_t = kv_t[1]
    query_rows = queries.reshape(batch_count, tok_count, kv_local, group_size, HD)
    query_pos = tm_at * tok_count + jnp.arange(tok_count, dtype=jnp.int32)
    first_valid = total_tokens - seq_lens // STRIDE
    both, key_pos = gather_causal(kv_t, tm_n, sec_n, tm_at, phase, tok_count)
    key_count = both.shape[-1]
    block_width = 1024 if key_count % 1024 == 0 else key_count
    rounds = key_count // block_width
    blocks = jnp.moveaxis(
        both.reshape(2, batch_count, kv_local, HD, rounds, block_width), 4, 0
    )
    pos_blocks = key_pos.reshape(rounds, block_width)
    start_state = (
        jnp.full((batch_count, kv_local, group_size, tok_count), -1e30, jnp.float32),
        jnp.zeros((batch_count, kv_local, group_size, tok_count), jnp.float32),
        jnp.zeros((batch_count, kv_local, group_size, tok_count, HD), jnp.float32),
    )
    if rounds == 1:
        key_pos1 = pos_blocks[0]
        allowed = (key_pos1[None, None, :] <= query_pos[None, :, None]) & (
            (key_pos1[None, None, :] >= first_valid[:, None, None])
            | (key_pos1[None, None, :] == query_pos[None, :, None])
        )
        scores = jnp.einsum(
            "btkgh,bkhn->bkgtn", query_rows, blocks[0, 0], preferred_element_type=jnp.float32
        )
        scores = jnp.where(allowed[:, None, None], scores, -jnp.inf)
        exp_scores = jnp.exp(scores - jnp.max(scores, -1, keepdims=True))
        result = (
            None,
            jnp.sum(exp_scores, -1),
            jnp.einsum(
                "bkgtn,bkhn->bkgth",
                exp_scores.astype(jnp.bfloat16),
                blocks[0, 1],
                preferred_element_type=jnp.float32,
            ),
        )
    else:

        def scan_step(state, block_item):
            kv_block, pos_block = block_item
            return (
                absorb_block(
                    state, kv_block[0], kv_block[1], pos_block, query_rows, query_pos,
                    first_valid,
                ),
                None,
            )

        result, _ = lax.scan(scan_step, start_state, (blocks, pos_blocks))
    run_max, run_sum, accumulated = result
    attended = (accumulated / run_sum[..., None]).astype(jnp.bfloat16)
    attended = attended.transpose(0, 3, 1, 2, 4).reshape(
        batch_count, tok_count, kv_local * group_size * HD
    )
    if out_w is None:
        return attended, key_t, value_t
    partial_value = jnp.einsum("bte,ed->btd", attended, out_w, preferred_element_type=jnp.float32)
    return partial_value, key_t, value_t


def per_device(
    series, lengths, patch_weight, norm_gain, query_weight, key_weight, value_weight, out_weight,
    *, tm_n, mp_n, sec_n
):
    seq_count, channels, steps_dev = series.shape
    tok_count = steps_dev // STRIDE
    tm_at = lax.axis_index("tm")
    mp_at = lax.axis_index("mp")
    sec_at = lax.axis_index("section")
    feat_axes = ("mp", "section")
    feat_n = mp_n * sec_n
    total_steps = steps_dev * tm_n
    total_tokens = tok_count * tm_n

    first_step = total_steps - lengths
    step_pos = tm_at * steps_dev + jnp.arange(steps_dev, dtype=jnp.int32)
    valid = (step_pos[None, :] >= first_step[:, None]).astype(jnp.float32)
    values = series.astype(jnp.float32)
    masked = values * valid[:, None, :]
    local_sum = jnp.sum(masked, -1)
    shard_lo = jnp.arange(tm_n, dtype=jnp.int32) * steps_dev
    counts = jnp.clip(
        shard_lo[None, :] + steps_dev - jnp.maximum(shard_lo[None, :], first_step[:, None]),
        0,
        steps_dev,
    ).astype(jnp.float32)
    my_count = jnp.sum(valid, -1)
    local_mean = local_sum / jnp.maximum(my_count, 1.0)[:, None]
    local_dev = (values - local_mean[..., None]) * valid[:, None, :]
    local_m2 = jnp.sum(local_dev * local_dev, -1)
    tail = series[:, :, steps_dev - STRIDE :]
    if tm_n > SMALL_GROUP:
        stats = lax.all_gather(jnp.stack([local_sum, local_m2], -1), "tm", axis=0)
        prior_raw = shift_from(tail, "tm", tm_n, 1, False).astype(jnp.float32)
    else:
        payload = jnp.concatenate(
            [jnp.stack([local_sum, local_m2], -1), tail.astype(jnp.float32)], -1
        )
        received = [payload] + [shift_from(payload, "tm", tm_n, by, True) for by in range(1, tm_n)]
        prior_raw = received[1][..., 2:] if tm_n > 1 else jnp.zeros_like(payload[..., 2:])
        order = (tm_at - jnp.arange(tm_n, dtype=jnp.int32)) % tm_n
        stats = jnp.take(jnp.stack([piece[..., :2] for piece in received], 0), order, axis=0)
    history = lengths.astype(jnp.float32)[:, None]
    shard_sums = stats[..., 0]
    shard_m2 = stats[..., 1]
    channel_mean = jnp.sum(shard_sums, 0) / history
    shard_counts = jnp.moveaxis(counts, 1, 0)[:, :, None]
    shard_means = shard_sums / jnp.maximum(shard_counts, 1.0)
    gap = shard_means - channel_mean[None]
    spread_total = jnp.sum(shard_m2 + shard_counts * gap * gap, 0)
    variance = spread_total / history
    inv_std = lax.rsqrt(variance + 1e-05)[..., None]

    padded = jnp.concatenate([prior_raw, series.astype(jnp.float32)], -1)
    padded_pos = tm_at * steps_dev - STRIDE + jnp.arange(steps_dev + STRIDE, dtype=jnp.int32)
    padded_valid = (
        (padded_pos[None, :] >= first_step[:, None]) & (padded_pos[None, :] >= 0)
    ).astype(jnp.float32)[:, None, :]
    normed = (
        (padded * padded_valid - channel_mean[..., None]) * padded_valid * inv_std
    ).astype(jnp.bfloat16)
    kernel = patch_weight.reshape(channels, 2 * STRIDE, patch_weight.shape[1])
    chunk_tok = 32 if tok_count % 32 == 0 else tok_count
    chunk_count = tok_count // chunk_tok
    chunks = jnp.stack(
        [
            normed[:, :, q * chunk_tok * STRIDE : (q + 1) * chunk_tok * STRIDE + STRIDE]
            for q in range(chunk_count)
        ],
        1,
    ).reshape(seq_count * chunk_count, channels, chunk_tok * STRIDE + STRIDE)
    tokens = lax.conv_general_dilated(
        chunks,
        kernel,
        window_strides=(STRIDE,),
        padding="VALID",
        dimension_numbers=("NCW", "IWO", "NWC"),
        preferred_element_type=jnp.float32,
    ).astype(jnp.bfloat16)
    tokens = tokens.reshape(seq_count, tok_count, tokens.shape[2])
    column_count = patch_weight.shape[1]
    hidden0 = lax.all_gather(tokens, feat_axes, axis=2, tiled=True)
    feature_count = hidden0.shape[2]
    head_cols = feature_count // mp_n
    sizes = (tm_n, sec_n, tm_at, total_tokens)

    partial0, key0, value0 = attend_layer(
        hidden0, lengths, norm_gain[0], query_weight[0], key_weight[0], value_weight[0],
        out_weight[0], sizes, 0,
    )
    head_sum = None
    for by in range(mp_n):
        pairs = [(m * sec_n, ((m + by) % mp_n) * sec_n + 1) for m in range(mp_n)]
        term = lax.ppermute(partial0.astype(jnp.bfloat16), feat_axes, pairs).astype(jnp.float32)
        head_sum = term if head_sum is None else head_sum + term
    hidden1 = (hidden0.astype(jnp.float32) + head_sum).astype(jnp.bfloat16)

    partial1, key1, value1 = attend_layer(
        hidden1, lengths, norm_gain[0], query_weight[0], key_weight[0], value_weight[0],
        out_weight[0], sizes, 1,
    )
    is_first = sec_at == 0
    key_store = jnp.where(is_first, key0, key1)[None]
    value_store = jnp.where(is_first, value0, value1)[None]

    per_section = seq_count // sec_n
    low_rows = partial1[:per_section]
    high_rows = partial1[per_section:]
    low_hidden = hidden1[:per_section]
    to_low = []
    to_high = []
    for by in range(mp_n):
        target_mp = (mp_at + by) % mp_n
        cols = lax.dynamic_slice_in_dim(low_rows, target_mp * head_cols, head_cols, 2)
        if by == 0:
            residual = lax.dynamic_slice_in_dim(low_hidden, target_mp * head_cols, head_cols, 2)
            cols = residual.astype(jnp.float32) + cols
        pairs = [(m * sec_n + 1, ((m + by) % mp_n) * sec_n) for m in range(mp_n)]
        to_low.append(lax.ppermute(cols.astype(jnp.bfloat16), feat_axes, pairs))
        if by > 0:
            cols_high = lax.dynamic_slice_in_dim(high_rows, target_mp * head_cols, head_cols, 2)
            pairs = [(m * sec_n + 1, ((m + by) % mp_n) * sec_n + 1) for m in range(mp_n)]
            to_high.append(lax.ppermute(cols_high.astype(jnp.bfloat16), feat_axes, pairs))
    low_total = to_low[0].astype(jnp.float32) + sum(
        piece.astype(jnp.float32) for piece in to_low[1:]
    )
    own_high = lax.dynamic_slice_in_dim(high_rows, mp_at * head_cols, head_cols, 2)
    own_hidden = lax.dynamic_slice_in_dim(hidden1[per_section:], mp_at * head_cols, head_cols, 2)
    high_total = own_hidden.astype(jnp.float32) + own_high + sum(
        piece.astype(jnp.float32) for piece in to_high
    )
    final_cols = jnp.where(is_first, low_total, high_total).astype(jnp.bfloat16)
    return (key_store, value_store, final_cols)


def solution(mesh):
    sizes = dict(tm_n=mesh.shape["tm"], mp_n=mesh.shape["mp"], sec_n=mesh.shape["section"])
    in_specs = (
        P("groups", None, "tm"),
        P("groups"),
        P(None, ("mp", "section")),
        P("section", None),
        P("section", None, "mp"),
        P("section", None, "mp"),
        P("section", None, "mp"),
        P("section", "mp", None),
    )
    out_specs = (
        P("section", "groups", "mp", None, "tm"),
        P("section", "groups", "mp", None, "tm"),
        P(("groups", "section"), "tm", "mp"),
    )

    def body(*args):
        return per_device(*args, **sizes)

    return jax.shard_map(body, mesh=mesh, in_specs=in_specs, out_specs=out_specs, check_vma=False)
```

```python
import jax
import jax.numpy as jnp
from jax import lax
from jax.sharding import PartitionSpec as P

STRIDE = 32
HD = 80
SMALL_GROUP = 4


def shift_from(value, axis, size, by, cyclic):
    pairs = [(i, (i + by) % size) for i in range(size) if cyclic or i + by < size]
    return lax.ppermute(value, axis, pairs)


def gather_ordered(value, axis, size, me):
    if size > SMALL_GROUP:
        return lax.all_gather(value, axis, axis=0)
    received = [value] + [shift_from(value, axis, size, by, True) for by in range(1, size)]
    stack = jnp.stack(received, 0)
    order = (me - jnp.arange(size, dtype=jnp.int32)) % size
    return jnp.take(stack, order, axis=0)


def gather_causal(value, tm_n, sec_n, tm_at, phase, width):
    if tm_n > SMALL_GROUP:
        gathered = lax.all_gather(value, "tm", axis=value.ndim - 1, tiled=True)
        return gathered, jnp.arange(tm_n * width, dtype=jnp.int32)
    pieces = []
    positions = []
    local = jnp.arange(width, dtype=jnp.int32)
    for by in range(tm_n - 1, 0, -1):
        pairs = [(t * sec_n + phase, (t + by) * sec_n + phase) for t in range(tm_n - by)]
        pieces.append(lax.ppermute(value, ("tm", "section"), pairs))
        positions.append((tm_at - by) * width + local)
    pieces.append(value)
    positions.append(tm_at * width + local)
    return jnp.concatenate(pieces, -1), jnp.concatenate(positions, 0)


def absorb_block(running, key_block, value_block, key_pos, query_rows, query_pos, first_valid):
    run_max, run_sum, accumulated = running
    allowed = (key_pos[None, None, :] <= query_pos[None, :, None]) & (
        (key_pos[None, None, :] >= first_valid[:, None, None])
        | (key_pos[None, None, :] == query_pos[None, :, None])
    )
    scores = jnp.einsum(
        "btkgh,bkhn->bkgtn", query_rows, key_block, preferred_element_type=jnp.float32
    )
    scores = jnp.where(allowed[:, None, None], scores, -jnp.inf)
    new_max = jnp.maximum(run_max, jnp.max(scores, -1))
    rescale = jnp.exp(run_max - new_max)
    exp_scores = jnp.exp(scores - new_max[..., None])
    new_sum = run_sum * rescale + jnp.sum(exp_scores, -1)
    contribution = jnp.einsum(
        "bkgtn,bkhn->bkgth",
        exp_scores.astype(jnp.bfloat16),
        value_block,
        preferred_element_type=jnp.float32,
    )
    return (new_max, new_sum, accumulated * rescale[..., None] + contribution)


def attend_layer(hidden_in, seq_lens, gain, query_w, key_w, value_w, out_w, sizes, phase):
    tm_n, sec_n, tm_at, total_tokens = sizes
    batch_count, tok_count, feature_count = hidden_in.shape
    hidden32 = hidden_in.astype(jnp.float32)
    gain32 = gain.astype(jnp.float32)
    scaled = hidden32 * lax.rsqrt(jnp.mean(hidden32 * hidden32, -1, keepdims=True) + 1e-06)
    layer_input = (scaled * gain32).astype(jnp.bfloat16)
    kv_local = key_w.shape[1] // HD
    group_size = query_w.shape[1] // key_w.shape[1]
    q_width = query_w.shape[1]
    projected = jnp.einsum(
        "btd,de->ebt", layer_input, jnp.concatenate([query_w, key_w, value_w], 1),
        preferred_element_type=jnp.float32,
    )
    queries = (projected[:q_width] * HD ** (-0.5)).astype(jnp.bfloat16)
    queries = queries.reshape(kv_local, group_size, HD, batch_count, tok_count)
    kv_t = projected[q_width:].astype(jnp.bfloat16)
    kv_t = kv_t.reshape(2, kv_local, HD, batch_count, tok_count).transpose(0, 3, 1, 2, 4)
    key_t = kv_t[0]
    value_t = kv_t[1]
    query_rows = queries.transpose(3, 4, 0, 1, 2)
    query_pos = tm_at * tok_count + jnp.arange(tok_count, dtype=jnp.int32)
    first_valid = total_tokens - seq_lens // STRIDE
    both, key_pos = gather_causal(kv_t, tm_n, sec_n, tm_at, phase, tok_count)
    key_count = both.shape[-1]
    block_width = 1024 if key_count % 1024 == 0 else key_count
    rounds = key_count // block_width
    blocks = jnp.moveaxis(
        both.reshape(2, batch_count, kv_local, HD, rounds, block_width), 4, 0
    )
    pos_blocks = key_pos.reshape(rounds, block_width)
    start_state = (
        jnp.full((batch_count, kv_local, group_size, tok_count), -1e30, jnp.float32),
        jnp.zeros((batch_count, kv_local, group_size, tok_count), jnp.float32),
        jnp.zeros((batch_count, kv_local, group_size, tok_count, HD), jnp.float32),
    )
    if rounds == 1:
        key_pos1 = pos_blocks[0]
        allowed = (key_pos1[None, None, :] <= query_pos[None, :, None]) & (
            (key_pos1[None, None, :] >= first_valid[:, None, None])
            | (key_pos1[None, None, :] == query_pos[None, :, None])
        )
        scores = jnp.einsum(
            "btkgh,bkhn->bkgtn", query_rows, blocks[0, 0], preferred_element_type=jnp.float32
        )
        scores = jnp.where(allowed[:, None, None], scores, -jnp.inf)
        exp_scores = jnp.exp(scores - jnp.max(scores, -1, keepdims=True))
        result = (
            None,
            jnp.sum(exp_scores, -1),
            jnp.einsum(
                "bkgtn,bkhn->bkgth",
                exp_scores.astype(jnp.bfloat16),
                blocks[0, 1],
                preferred_element_type=jnp.float32,
            ),
        )
    else:

        def scan_step(state, block_item):
            kv_block, pos_block = block_item
            return (
                absorb_block(
                    state, kv_block[0], kv_block[1], pos_block, query_rows, query_pos,
                    first_valid,
                ),
                None,
            )

        result, _ = lax.scan(scan_step, start_state, (blocks, pos_blocks))
    run_max, run_sum, accumulated = result
    attended = (accumulated / run_sum[..., None]).astype(jnp.bfloat16)
    attended = attended.transpose(0, 3, 1, 2, 4).reshape(
        batch_count, tok_count, kv_local * group_size * HD
    )
    if out_w is None:
        return attended, key_t, value_t
    partial_value = jnp.einsum("bte,ed->btd", attended, out_w, preferred_element_type=jnp.float32)
    return partial_value, key_t, value_t


def per_device(
    series, lengths, patch_weight, norm_gain, query_weight, key_weight, value_weight, out_weight,
    *, tm_n, mp_n, sec_n
):
    seq_count, channels, steps_dev = series.shape
    tok_count = steps_dev // STRIDE
    tm_at = lax.axis_index("tm")
    mp_at = lax.axis_index("mp")
    sec_at = lax.axis_index("section")
    feat_axes = ("mp", "section")
    feat_n = mp_n * sec_n
    total_steps = steps_dev * tm_n
    total_tokens = tok_count * tm_n

    first_step = total_steps - lengths
    step_pos = tm_at * steps_dev + jnp.arange(steps_dev, dtype=jnp.int32)
    valid = (step_pos[None, :] >= first_step[:, None]).astype(jnp.float32)
    values = series.astype(jnp.float32)
    masked = values * valid[:, None, :]
    local_sum = jnp.sum(masked, -1)
    shard_lo = jnp.arange(tm_n, dtype=jnp.int32) * steps_dev
    counts = jnp.clip(
        shard_lo[None, :] + steps_dev - jnp.maximum(shard_lo[None, :], first_step[:, None]),
        0,
        steps_dev,
    ).astype(jnp.float32)
    my_count = jnp.sum(valid, -1)
    local_mean = local_sum / jnp.maximum(my_count, 1.0)[:, None]
    local_dev = (values - local_mean[..., None]) * valid[:, None, :]
    local_m2 = jnp.sum(local_dev * local_dev, -1)
    tail = series[:, :, steps_dev - STRIDE :]
    if tm_n > SMALL_GROUP:
        stats = lax.all_gather(jnp.stack([local_sum, local_m2], -1), "tm", axis=0)
        prior_raw = shift_from(tail, "tm", tm_n, 1, False).astype(jnp.float32)
    else:
        payload = jnp.concatenate(
            [jnp.stack([local_sum, local_m2], -1), tail.astype(jnp.float32)], -1
        )
        received = [payload] + [shift_from(payload, "tm", tm_n, by, True) for by in range(1, tm_n)]
        prior_raw = received[1][..., 2:] if tm_n > 1 else jnp.zeros_like(payload[..., 2:])
        order = (tm_at - jnp.arange(tm_n, dtype=jnp.int32)) % tm_n
        stats = jnp.take(jnp.stack([piece[..., :2] for piece in received], 0), order, axis=0)
    history = lengths.astype(jnp.float32)[:, None]
    shard_sums = stats[..., 0]
    shard_m2 = stats[..., 1]
    channel_mean = jnp.sum(shard_sums, 0) / history
    shard_counts = jnp.moveaxis(counts, 1, 0)[:, :, None]
    shard_means = shard_sums / jnp.maximum(shard_counts, 1.0)
    gap = shard_means - channel_mean[None]
    spread_total = jnp.sum(shard_m2 + shard_counts * gap * gap, 0)
    variance = spread_total / history
    inv_std = lax.rsqrt(variance + 1e-05)[..., None]

    padded = jnp.concatenate([prior_raw, series.astype(jnp.float32)], -1)
    padded_pos = tm_at * steps_dev - STRIDE + jnp.arange(steps_dev + STRIDE, dtype=jnp.int32)
    padded_valid = (
        (padded_pos[None, :] >= first_step[:, None]) & (padded_pos[None, :] >= 0)
    ).astype(jnp.float32)[:, None, :]
    normed = (
        (padded * padded_valid - channel_mean[..., None]) * padded_valid * inv_std
    ).astype(jnp.bfloat16)
    kernel = patch_weight.reshape(channels, 2 * STRIDE, patch_weight.shape[1])
    chunk_tok = 32 if tok_count % 32 == 0 else tok_count
    chunk_count = tok_count // chunk_tok
    chunks = jnp.stack(
        [
            normed[:, :, q * chunk_tok * STRIDE : (q + 1) * chunk_tok * STRIDE + STRIDE]
            for q in range(chunk_count)
        ],
        1,
    ).reshape(seq_count * chunk_count, channels, chunk_tok * STRIDE + STRIDE)
    tokens = lax.conv_general_dilated(
        chunks,
        kernel,
        window_strides=(STRIDE,),
        padding="VALID",
        dimension_numbers=("NCW", "IWO", "NWC"),
        preferred_element_type=jnp.float32,
    ).astype(jnp.bfloat16)
    tokens = tokens.reshape(seq_count, tok_count, tokens.shape[2])
    column_count = patch_weight.shape[1]
    hidden0 = lax.all_gather(tokens, feat_axes, axis=2, tiled=True)
    feature_count = hidden0.shape[2]
    head_cols = feature_count // mp_n
    sizes = (tm_n, sec_n, tm_at, total_tokens)

    partial0, key0, value0 = attend_layer(
        hidden0, lengths, norm_gain[0], query_weight[0], key_weight[0], value_weight[0],
        out_weight[0], sizes, 0,
    )
    head_sum = None
    for by in range(mp_n):
        pairs = [(m * sec_n, ((m + by) % mp_n) * sec_n + 1) for m in range(mp_n)]
        term = lax.ppermute(partial0.astype(jnp.bfloat16), feat_axes, pairs).astype(jnp.float32)
        head_sum = term if head_sum is None else head_sum + term
    hidden1 = (hidden0.astype(jnp.float32) + head_sum).astype(jnp.bfloat16)

    partial1, key1, value1 = attend_layer(
        hidden1, lengths, norm_gain[0], query_weight[0], key_weight[0], value_weight[0],
        out_weight[0], sizes, 1,
    )
    is_first = sec_at == 0
    key_store = jnp.where(is_first, key0, key1)[None]
    value_store = jnp.where(is_first, value0, value1)[None]

    per_section = seq_count // sec_n
    low_rows = partial1[:per_section]
    high_rows = partial1[per_section:]
    low_hidden = hidden1[:per_section]
    to_low = []
    to_high = []
    for by in range(mp_n):
        target_mp = (mp_at + by) % mp_n
        cols = lax.dynamic_slice_in_dim(low_rows, target_mp * head_cols, head_cols, 2)
        if by == 0:
            residual = lax.dynamic_slice_in_dim(low_hidden, target_mp * head_cols, head_cols, 2)
            cols = residual.astype(jnp.float32) + cols
        pairs = [(m * sec_n + 1, ((m + by) % mp_n) * sec_n) for m in range(mp_n)]
        to_low.append(lax.ppermute(cols.astype(jnp.bfloat16), feat_axes, pairs))
        if by > 0:
            cols_high = lax.dynamic_slice_in_dim(high_rows, target_mp * head_cols, head_cols, 2)
            pairs = [(m * sec_n + 1, ((m + by) % mp_n) * sec_n + 1) for m in range(mp_n)]
            to_high.append(lax.ppermute(cols_high.astype(jnp.bfloat16), feat_axes, pairs))
    low_total = to_low[0].astype(jnp.float32) + sum(
        piece.astype(jnp.float32) for piece in to_low[1:]
    )
    own_high = lax.dynamic_slice_in_dim(high_rows, mp_at * head_cols, head_cols, 2)
    own_hidden = lax.dynamic_slice_in_dim(hidden1[per_section:], mp_at * head_cols, head_cols, 2)
    high_total = own_hidden.astype(jnp.float32) + own_high + sum(
        piece.astype(jnp.float32) for piece in to_high
    )
    final_cols = jnp.where(is_first, low_total, high_total).astype(jnp.bfloat16)
    return (key_store, value_store, final_cols)


def solution(mesh):
    sizes = dict(tm_n=mesh.shape["tm"], mp_n=mesh.shape["mp"], sec_n=mesh.shape["section"])
    in_specs = (
        P("groups", None, "tm"),
        P("groups"),
        P(None, ("mp", "section")),
        P("section", None),
        P("section", None, "mp"),
        P("section", None, "mp"),
        P("section", None, "mp"),
        P("section", "mp", None),
    )
    out_specs = (
        P("section", "groups", "mp", None, "tm"),
        P("section", "groups", "mp", None, "tm"),
        P(("groups", "section"), "tm", "mp"),
    )

    def body(*args):
        return per_device(*args, **sizes)

    return jax.shard_map(body, mesh=mesh, in_specs=in_specs, out_specs=out_specs, check_vma=False)
```

```python
import jax
import jax.numpy as jnp
from jax import lax
from jax.sharding import PartitionSpec as P

STRIDE = 32
HD = 80
SMALL_GROUP = 4


def shift_from(value, axis, size, by, cyclic):
    pairs = [(i, (i + by) % size) for i in range(size) if cyclic or i + by < size]
    return lax.ppermute(value, axis, pairs)


def gather_ordered(value, axis, size, me):
    if size > SMALL_GROUP:
        return lax.all_gather(value, axis, axis=0)
    received = [value] + [shift_from(value, axis, size, by, True) for by in range(1, size)]
    stack = jnp.stack(received, 0)
    order = (me - jnp.arange(size, dtype=jnp.int32)) % size
    return jnp.take(stack, order, axis=0)


def gather_causal(value, tm_n, sec_n, tm_at, phase, width):
    if tm_n > SMALL_GROUP:
        gathered = lax.all_gather(value, "tm", axis=value.ndim - 1, tiled=True)
        return gathered, jnp.arange(tm_n * width, dtype=jnp.int32)
    pieces = []
    positions = []
    local = jnp.arange(width, dtype=jnp.int32)
    for by in range(tm_n - 1, 0, -1):
        pairs = [(t * sec_n + phase, (t + by) * sec_n + phase) for t in range(tm_n - by)]
        pieces.append(lax.ppermute(value, ("tm", "section"), pairs))
        positions.append((tm_at - by) * width + local)
    pieces.append(value)
    positions.append(tm_at * width + local)
    return jnp.concatenate(pieces, -1), jnp.concatenate(positions, 0)


def absorb_block(running, key_block, value_block, key_pos, query_rows, query_pos, first_valid):
    run_max, run_sum, accumulated = running
    allowed = (key_pos[None, None, :] <= query_pos[None, :, None]) & (
        (key_pos[None, None, :] >= first_valid[:, None, None])
        | (key_pos[None, None, :] == query_pos[None, :, None])
    )
    scores = jnp.einsum(
        "bkght,bkhn->bkgtn", query_rows, key_block, preferred_element_type=jnp.float32
    )
    scores = jnp.where(allowed[:, None, None], scores, -jnp.inf)
    new_max = jnp.maximum(run_max, jnp.max(scores, -1))
    rescale = jnp.exp(run_max - new_max)
    exp_scores = jnp.exp(scores - new_max[..., None])
    new_sum = run_sum * rescale + jnp.sum(exp_scores, -1)
    contribution = jnp.einsum(
        "bkgtn,bkhn->bkgth",
        exp_scores.astype(jnp.bfloat16),
        value_block,
        preferred_element_type=jnp.float32,
    )
    return (new_max, new_sum, accumulated * rescale[..., None] + contribution)


def attend_layer(hidden_in, seq_lens, gain, query_w, key_w, value_w, out_w, sizes, phase):
    tm_n, sec_n, tm_at, total_tokens = sizes
    batch_count, tok_count, feature_count = hidden_in.shape
    hidden32 = hidden_in.astype(jnp.float32)
    gain32 = gain.astype(jnp.float32)
    scaled = hidden32 * lax.rsqrt(jnp.mean(hidden32 * hidden32, -1, keepdims=True) + 1e-06)
    layer_input = (scaled * gain32).astype(jnp.bfloat16)
    queries = (
        jnp.einsum("btd,de->bet", layer_input, query_w, preferred_element_type=jnp.float32)
        * HD ** (-0.5)
    ).astype(jnp.bfloat16)
    kv_local = key_w.shape[1] // HD
    group_size = query_w.shape[1] // key_w.shape[1]
    kv_t = jnp.einsum(
        "btd,de->ebt", layer_input, jnp.concatenate([key_w, value_w], 1),
        preferred_element_type=jnp.float32,
    ).astype(jnp.bfloat16)
    kv_t = kv_t.reshape(2, kv_local, HD, batch_count, tok_count).transpose(0, 3, 1, 2, 4)
    key_t = kv_t[0]
    value_t = kv_t[1]
    query_rows = queries.reshape(batch_count, kv_local, group_size, HD, tok_count)
    query_pos = tm_at * tok_count + jnp.arange(tok_count, dtype=jnp.int32)
    first_valid = total_tokens - seq_lens // STRIDE
    both, key_pos = gather_causal(kv_t, tm_n, sec_n, tm_at, phase, tok_count)
    key_count = both.shape[-1]
    block_width = 1024 if key_count % 1024 == 0 else key_count
    rounds = key_count // block_width
    blocks = jnp.moveaxis(
        both.reshape(2, batch_count, kv_local, HD, rounds, block_width), 4, 0
    )
    pos_blocks = key_pos.reshape(rounds, block_width)
    start_state = (
        jnp.full((batch_count, kv_local, group_size, tok_count), -1e30, jnp.float32),
        jnp.zeros((batch_count, kv_local, group_size, tok_count), jnp.float32),
        jnp.zeros((batch_count, kv_local, group_size, tok_count, HD), jnp.float32),
    )
    if rounds == 1:
        result = absorb_block(
            start_state, blocks[0, 0], blocks[0, 1], pos_blocks[0], query_rows, query_pos,
            first_valid,
        )
    else:

        def scan_step(state, block_item):
            kv_block, pos_block = block_item
            return (
                absorb_block(
                    state, kv_block[0], kv_block[1], pos_block, query_rows, query_pos,
                    first_valid,
                ),
                None,
            )

        result, _ = lax.scan(scan_step, start_state, (blocks, pos_blocks))
    run_max, run_sum, accumulated = result
    attended = (accumulated / run_sum[..., None]).astype(jnp.bfloat16)
    attended = attended.transpose(0, 3, 1, 2, 4).reshape(
        batch_count, tok_count, kv_local * group_size * HD
    )
    if out_w is None:
        return attended, key_t, value_t
    partial_value = jnp.einsum("bte,ed->btd", attended, out_w, preferred_element_type=jnp.float32)
    return partial_value, key_t, value_t


def per_device(
    series, lengths, patch_weight, norm_gain, query_weight, key_weight, value_weight, out_weight,
    *, tm_n, mp_n, sec_n
):
    seq_count, channels, steps_dev = series.shape
    tok_count = steps_dev // STRIDE
    tm_at = lax.axis_index("tm")
    mp_at = lax.axis_index("mp")
    sec_at = lax.axis_index("section")
    feat_axes = ("mp", "section")
    feat_n = mp_n * sec_n
    total_steps = steps_dev * tm_n
    total_tokens = tok_count * tm_n

    first_step = total_steps - lengths
    step_pos = tm_at * steps_dev + jnp.arange(steps_dev, dtype=jnp.int32)
    valid = (step_pos[None, :] >= first_step[:, None]).astype(jnp.float32)
    values = series.astype(jnp.float32)
    masked = values * valid[:, None, :]
    local_sum = jnp.sum(masked, -1)
    shard_lo = jnp.arange(tm_n, dtype=jnp.int32) * steps_dev
    counts = jnp.clip(
        shard_lo[None, :] + steps_dev - jnp.maximum(shard_lo[None, :], first_step[:, None]),
        0,
        steps_dev,
    ).astype(jnp.float32)
    my_count = jnp.sum(valid, -1)
    local_mean = local_sum / jnp.maximum(my_count, 1.0)[:, None]
    local_dev = (values - local_mean[..., None]) * valid[:, None, :]
    local_m2 = jnp.sum(local_dev * local_dev, -1)
    tail = series[:, :, steps_dev - STRIDE :]
    if tm_n > SMALL_GROUP:
        stats = lax.all_gather(jnp.stack([local_sum, local_m2], -1), "tm", axis=0)
        prior_raw = shift_from(tail, "tm", tm_n, 1, False).astype(jnp.float32)
    else:
        payload = jnp.concatenate(
            [jnp.stack([local_sum, local_m2], -1), tail.astype(jnp.float32)], -1
        )
        received = [payload] + [shift_from(payload, "tm", tm_n, by, True) for by in range(1, tm_n)]
        prior_raw = received[1][..., 2:] if tm_n > 1 else jnp.zeros_like(payload[..., 2:])
        order = (tm_at - jnp.arange(tm_n, dtype=jnp.int32)) % tm_n
        stats = jnp.take(jnp.stack([piece[..., :2] for piece in received], 0), order, axis=0)
    history = lengths.astype(jnp.float32)[:, None]
    shard_sums = stats[..., 0]
    shard_m2 = stats[..., 1]
    channel_mean = jnp.sum(shard_sums, 0) / history
    shard_counts = jnp.moveaxis(counts, 1, 0)[:, :, None]
    shard_means = shard_sums / jnp.maximum(shard_counts, 1.0)
    gap = shard_means - channel_mean[None]
    spread_total = jnp.sum(shard_m2 + shard_counts * gap * gap, 0)
    variance = spread_total / history
    inv_std = lax.rsqrt(variance + 1e-05)[..., None]

    padded = jnp.concatenate([prior_raw, series.astype(jnp.float32)], -1)
    padded_pos = tm_at * steps_dev - STRIDE + jnp.arange(steps_dev + STRIDE, dtype=jnp.int32)
    padded_valid = (
        (padded_pos[None, :] >= first_step[:, None]) & (padded_pos[None, :] >= 0)
    ).astype(jnp.float32)[:, None, :]
    normed = (
        (padded * padded_valid - channel_mean[..., None]) * padded_valid * inv_std
    ).astype(jnp.bfloat16)
    kernel = patch_weight.reshape(channels, 2 * STRIDE, patch_weight.shape[1])
    chunk_tok = 32 if tok_count % 32 == 0 else tok_count
    chunk_count = tok_count // chunk_tok
    chunks = jnp.stack(
        [
            normed[:, :, q * chunk_tok * STRIDE : (q + 1) * chunk_tok * STRIDE + STRIDE]
            for q in range(chunk_count)
        ],
        1,
    ).reshape(seq_count * chunk_count, channels, chunk_tok * STRIDE + STRIDE)
    tokens = lax.conv_general_dilated(
        chunks,
        kernel,
        window_strides=(STRIDE,),
        padding="VALID",
        dimension_numbers=("NCW", "IWO", "NWC"),
        preferred_element_type=jnp.float32,
    ).astype(jnp.bfloat16)
    tokens = tokens.reshape(seq_count, tok_count, tokens.shape[2])
    column_count = patch_weight.shape[1]
    hidden0 = lax.all_gather(tokens, feat_axes, axis=2, tiled=True)
    feature_count = hidden0.shape[2]
    head_cols = feature_count // mp_n
    sizes = (tm_n, sec_n, tm_at, total_tokens)

    partial0, key0, value0 = attend_layer(
        hidden0, lengths, norm_gain[0], query_weight[0], key_weight[0], value_weight[0],
        out_weight[0], sizes, 0,
    )
    head_sum = None
    for by in range(mp_n):
        pairs = [(m * sec_n, ((m + by) % mp_n) * sec_n + 1) for m in range(mp_n)]
        term = lax.ppermute(partial0.astype(jnp.bfloat16), feat_axes, pairs).astype(jnp.float32)
        head_sum = term if head_sum is None else head_sum + term
    hidden1 = (hidden0.astype(jnp.float32) + head_sum).astype(jnp.bfloat16)

    partial1, key1, value1 = attend_layer(
        hidden1, lengths, norm_gain[0], query_weight[0], key_weight[0], value_weight[0],
        out_weight[0], sizes, 1,
    )
    is_first = sec_at == 0
    key_store = jnp.where(is_first, key0, key1)[None]
    value_store = jnp.where(is_first, value0, value1)[None]

    per_section = seq_count // sec_n
    low_rows = partial1[:per_section]
    high_rows = partial1[per_section:]
    low_hidden = hidden1[:per_section]
    to_low = []
    to_high = []
    for by in range(mp_n):
        target_mp = (mp_at + by) % mp_n
        cols = lax.dynamic_slice_in_dim(low_rows, target_mp * head_cols, head_cols, 2)
        if by == 0:
            residual = lax.dynamic_slice_in_dim(low_hidden, target_mp * head_cols, head_cols, 2)
            cols = residual.astype(jnp.float32) + cols
        pairs = [(m * sec_n + 1, ((m + by) % mp_n) * sec_n) for m in range(mp_n)]
        to_low.append(lax.ppermute(cols.astype(jnp.bfloat16), feat_axes, pairs))
        if by > 0:
            cols_high = lax.dynamic_slice_in_dim(high_rows, target_mp * head_cols, head_cols, 2)
            pairs = [(m * sec_n + 1, ((m + by) % mp_n) * sec_n + 1) for m in range(mp_n)]
            to_high.append(lax.ppermute(cols_high.astype(jnp.bfloat16), feat_axes, pairs))
    low_total = to_low[0].astype(jnp.float32) + sum(
        piece.astype(jnp.float32) for piece in to_low[1:]
    )
    own_high = lax.dynamic_slice_in_dim(high_rows, mp_at * head_cols, head_cols, 2)
    own_hidden = lax.dynamic_slice_in_dim(hidden1[per_section:], mp_at * head_cols, head_cols, 2)
    high_total = own_hidden.astype(jnp.float32) + own_high + sum(
        piece.astype(jnp.float32) for piece in to_high
    )
    final_cols = jnp.where(is_first, low_total, high_total).astype(jnp.bfloat16)
    return (key_store, value_store, final_cols)


def solution(mesh):
    sizes = dict(tm_n=mesh.shape["tm"], mp_n=mesh.shape["mp"], sec_n=mesh.shape["section"])
    in_specs = (
        P("groups", None, "tm"),
        P("groups"),
        P(None, ("mp", "section")),
        P("section", None),
        P("section", None, "mp"),
        P("section", None, "mp"),
        P("section", None, "mp"),
        P("section", "mp", None),
    )
    out_specs = (
        P("section", "groups", "mp", None, "tm"),
        P("section", "groups", "mp", None, "tm"),
        P(("groups", "section"), "tm", "mp"),
    )

    def body(*args):
        return per_device(*args, **sizes)

    return jax.shard_map(body, mesh=mesh, in_specs=in_specs, out_specs=out_specs, check_vma=False)
```

```python
import jax
import jax.numpy as jnp
from jax import lax
from jax.sharding import PartitionSpec as P

STRIDE = 32
HD = 80
SMALL_GROUP = 4


def shift_from(value, axis, size, by, cyclic):
    pairs = [(i, (i + by) % size) for i in range(size) if cyclic or i + by < size]
    return lax.ppermute(value, axis, pairs)


def gather_ordered(value, axis, size, me):
    if size > SMALL_GROUP:
        return lax.all_gather(value, axis, axis=0)
    received = [value] + [shift_from(value, axis, size, by, True) for by in range(1, size)]
    stack = jnp.stack(received, 0)
    order = (me - jnp.arange(size, dtype=jnp.int32)) % size
    return jnp.take(stack, order, axis=0)


def gather_causal(value, tm_n, sec_n, tm_at, phase, width):
    if tm_n > SMALL_GROUP:
        gathered = lax.all_gather(value, "tm", axis=value.ndim - 1, tiled=True)
        return gathered, jnp.arange(tm_n * width, dtype=jnp.int32)
    pieces = []
    positions = []
    local = jnp.arange(width, dtype=jnp.int32)
    for by in range(tm_n - 1, 0, -1):
        pairs = [(t * sec_n + phase, (t + by) * sec_n + phase) for t in range(tm_n - by)]
        pieces.append(lax.ppermute(value, ("tm", "section"), pairs))
        positions.append((tm_at - by) * width + local)
    pieces.append(value)
    positions.append(tm_at * width + local)
    return jnp.concatenate(pieces, -1), jnp.concatenate(positions, 0)


def absorb_block(running, key_block, value_block, key_pos, query_rows, query_pos, first_valid):
    run_max, run_sum, accumulated = running
    allowed = (key_pos[None, None, :] <= query_pos[None, :, None]) & (
        (key_pos[None, None, :] >= first_valid[:, None, None])
        | (key_pos[None, None, :] == query_pos[None, :, None])
    )
    scores = jnp.einsum(
        "btkgh,bkhn->bkgtn", query_rows, key_block, preferred_element_type=jnp.float32
    )
    scores = jnp.where(allowed[:, None, None], scores, -jnp.inf)
    new_max = jnp.maximum(run_max, jnp.max(scores, -1))
    rescale = jnp.exp(run_max - new_max)
    exp_scores = jnp.exp(scores - new_max[..., None])
    new_sum = run_sum * rescale + jnp.sum(exp_scores, -1)
    contribution = jnp.einsum(
        "bkgtn,bkhn->bkgth",
        exp_scores.astype(jnp.bfloat16),
        value_block,
        preferred_element_type=jnp.float32,
    )
    return (new_max, new_sum, accumulated * rescale[..., None] + contribution)


def attend_layer(hidden_in, seq_lens, gain, query_w, key_w, value_w, out_w, sizes, phase):
    tm_n, sec_n, tm_at, total_tokens = sizes
    batch_count, tok_count, feature_count = hidden_in.shape
    hidden32 = hidden_in.astype(jnp.float32)
    gain32 = gain.astype(jnp.float32)
    scaled = hidden32 * lax.rsqrt(jnp.mean(hidden32 * hidden32, -1, keepdims=True) + 1e-06)
    layer_input = (scaled * gain32).astype(jnp.bfloat16)
    queries = (
        jnp.einsum("btd,de->bte", layer_input, query_w, preferred_element_type=jnp.float32)
        * HD ** (-0.5)
    ).astype(jnp.bfloat16)
    kv_local = key_w.shape[1] // HD
    group_size = query_w.shape[1] // key_w.shape[1]
    kv_t = jnp.einsum(
        "btd,de->ebt", layer_input, jnp.concatenate([key_w, value_w], 1),
        preferred_element_type=jnp.float32,
    ).astype(jnp.bfloat16)
    kv_t = kv_t.reshape(2, kv_local, HD, batch_count, tok_count).transpose(0, 3, 1, 2, 4)
    key_t = kv_t[0]
    value_t = kv_t[1]
    query_rows = queries.reshape(batch_count, tok_count, kv_local, group_size, HD)
    query_pos = tm_at * tok_count + jnp.arange(tok_count, dtype=jnp.int32)
    first_valid = total_tokens - seq_lens // STRIDE
    both, key_pos = gather_causal(kv_t, tm_n, sec_n, tm_at, phase, tok_count)
    key_count = both.shape[-1]
    block_width = 1024 if key_count % 1024 == 0 else key_count
    rounds = key_count // block_width
    blocks = jnp.moveaxis(
        both.reshape(2, batch_count, kv_local, HD, rounds, block_width), 4, 0
    )
    pos_blocks = key_pos.reshape(rounds, block_width)
    start_state = (
        jnp.full((batch_count, kv_local, group_size, tok_count), -1e30, jnp.float32),
        jnp.zeros((batch_count, kv_local, group_size, tok_count), jnp.float32),
        jnp.zeros((batch_count, kv_local, group_size, tok_count, HD), jnp.float32),
    )
    if rounds == 1:
        result = absorb_block(
            start_state, blocks[0, 0], blocks[0, 1], pos_blocks[0], query_rows, query_pos,
            first_valid,
        )
    else:

        def scan_step(state, block_item):
            kv_block, pos_block = block_item
            return (
                absorb_block(
                    state, kv_block[0], kv_block[1], pos_block, query_rows, query_pos,
                    first_valid,
                ),
                None,
            )

        result, _ = lax.scan(scan_step, start_state, (blocks, pos_blocks))
    run_max, run_sum, accumulated = result
    attended = (accumulated / run_sum[..., None]).astype(jnp.bfloat16)
    attended = attended.transpose(0, 3, 1, 2, 4).reshape(
        batch_count, tok_count, kv_local * group_size * HD
    )
    if out_w is None:
        return attended, key_t, value_t
    partial_value = jnp.einsum("bte,ed->btd", attended, out_w, preferred_element_type=jnp.float32)
    return partial_value, key_t, value_t


def per_device(
    series, lengths, patch_weight, norm_gain, query_weight, key_weight, value_weight, out_weight,
    *, tm_n, mp_n, sec_n
):
    seq_count, channels, steps_dev = series.shape
    tok_count = steps_dev // STRIDE
    tm_at = lax.axis_index("tm")
    mp_at = lax.axis_index("mp")
    sec_at = lax.axis_index("section")
    feat_axes = ("mp", "section")
    feat_n = mp_n * sec_n
    total_steps = steps_dev * tm_n
    total_tokens = tok_count * tm_n

    first_step = total_steps - lengths
    step_pos = tm_at * steps_dev + jnp.arange(steps_dev, dtype=jnp.int32)
    valid = (step_pos[None, :] >= first_step[:, None]).astype(jnp.float32)
    values = series.astype(jnp.float32)
    masked = values * valid[:, None, :]
    local_sum = jnp.sum(masked, -1)
    shard_lo = jnp.arange(tm_n, dtype=jnp.int32) * steps_dev
    counts = jnp.clip(
        shard_lo[None, :] + steps_dev - jnp.maximum(shard_lo[None, :], first_step[:, None]),
        0,
        steps_dev,
    ).astype(jnp.float32)
    my_count = jnp.sum(valid, -1)
    local_mean = local_sum / jnp.maximum(my_count, 1.0)[:, None]
    local_dev = (values - local_mean[..., None]) * valid[:, None, :]
    local_m2 = jnp.sum(local_dev * local_dev, -1)
    tail = series[:, :, steps_dev - STRIDE :]
    if tm_n > SMALL_GROUP:
        stats = lax.all_gather(jnp.stack([local_sum, local_m2], -1), "tm", axis=0)
        prior_raw = shift_from(tail, "tm", tm_n, 1, False).astype(jnp.float32)
    else:
        payload = jnp.concatenate(
            [jnp.stack([local_sum, local_m2], -1), tail.astype(jnp.float32)], -1
        )
        received = [payload] + [shift_from(payload, "tm", tm_n, by, True) for by in range(1, tm_n)]
        prior_raw = received[1][..., 2:] if tm_n > 1 else jnp.zeros_like(payload[..., 2:])
        order = (tm_at - jnp.arange(tm_n, dtype=jnp.int32)) % tm_n
        stats = jnp.take(jnp.stack([piece[..., :2] for piece in received], 0), order, axis=0)
    history = lengths.astype(jnp.float32)[:, None]
    shard_sums = stats[..., 0]
    shard_m2 = stats[..., 1]
    channel_mean = jnp.sum(shard_sums, 0) / history
    shard_counts = jnp.moveaxis(counts, 1, 0)[:, :, None]
    shard_means = shard_sums / jnp.maximum(shard_counts, 1.0)
    gap = shard_means - channel_mean[None]
    spread_total = jnp.sum(shard_m2 + shard_counts * gap * gap, 0)
    variance = spread_total / history
    inv_std = lax.rsqrt(variance + 1e-05)[..., None]

    padded = jnp.concatenate([prior_raw.astype(jnp.bfloat16), series], -1).astype(jnp.float32)
    padded_pos = tm_at * steps_dev - STRIDE + jnp.arange(steps_dev + STRIDE, dtype=jnp.int32)
    padded_valid = (
        (padded_pos[None, :] >= first_step[:, None]) & (padded_pos[None, :] >= 0)
    ).astype(jnp.float32)[:, None, :]
    normed = (
        (padded * padded_valid - channel_mean[..., None]) * padded_valid * inv_std
    ).astype(jnp.bfloat16)
    kernel = patch_weight.reshape(channels, 2 * STRIDE, patch_weight.shape[1])
    chunk_tok = 32 if tok_count % 32 == 0 else tok_count
    chunk_count = tok_count // chunk_tok
    chunks = jnp.stack(
        [
            normed[:, :, q * chunk_tok * STRIDE : (q + 1) * chunk_tok * STRIDE + STRIDE]
            for q in range(chunk_count)
        ],
        1,
    ).reshape(seq_count * chunk_count, channels, chunk_tok * STRIDE + STRIDE)
    tokens = lax.conv_general_dilated(
        chunks,
        kernel,
        window_strides=(STRIDE,),
        padding="VALID",
        dimension_numbers=("NCW", "IWO", "NWC"),
        preferred_element_type=jnp.float32,
    ).astype(jnp.bfloat16)
    tokens = tokens.reshape(seq_count, tok_count, tokens.shape[2])
    column_count = patch_weight.shape[1]
    hidden0 = lax.all_gather(tokens, feat_axes, axis=2, tiled=True)
    feature_count = hidden0.shape[2]
    head_cols = feature_count // mp_n
    sizes = (tm_n, sec_n, tm_at, total_tokens)

    partial0, key0, value0 = attend_layer(
        hidden0, lengths, norm_gain[0], query_weight[0], key_weight[0], value_weight[0],
        out_weight[0], sizes, 0,
    )
    head_sum = None
    for by in range(mp_n):
        pairs = [(m * sec_n, ((m + by) % mp_n) * sec_n + 1) for m in range(mp_n)]
        term = lax.ppermute(partial0.astype(jnp.bfloat16), feat_axes, pairs).astype(jnp.float32)
        head_sum = term if head_sum is None else head_sum + term
    hidden1 = (hidden0.astype(jnp.float32) + head_sum).astype(jnp.bfloat16)

    partial1, key1, value1 = attend_layer(
        hidden1, lengths, norm_gain[0], query_weight[0], key_weight[0], value_weight[0],
        out_weight[0], sizes, 1,
    )
    is_first = sec_at == 0
    key_store = jnp.where(is_first, key0, key1)[None]
    value_store = jnp.where(is_first, value0, value1)[None]

    per_section = seq_count // sec_n
    low_rows = partial1[:per_section]
    high_rows = partial1[per_section:]
    low_hidden = hidden1[:per_section]
    to_low = []
    to_high = []
    for by in range(mp_n):
        target_mp = (mp_at + by) % mp_n
        cols = lax.dynamic_slice_in_dim(low_rows, target_mp * head_cols, head_cols, 2)
        if by == 0:
            residual = lax.dynamic_slice_in_dim(low_hidden, target_mp * head_cols, head_cols, 2)
            cols = residual.astype(jnp.float32) + cols
        pairs = [(m * sec_n + 1, ((m + by) % mp_n) * sec_n) for m in range(mp_n)]
        to_low.append(lax.ppermute(cols.astype(jnp.bfloat16), feat_axes, pairs))
        if by > 0:
            cols_high = lax.dynamic_slice_in_dim(high_rows, target_mp * head_cols, head_cols, 2)
            pairs = [(m * sec_n + 1, ((m + by) % mp_n) * sec_n + 1) for m in range(mp_n)]
            to_high.append(lax.ppermute(cols_high.astype(jnp.bfloat16), feat_axes, pairs))
    low_total = to_low[0].astype(jnp.float32) + sum(
        piece.astype(jnp.float32) for piece in to_low[1:]
    )
    own_high = lax.dynamic_slice_in_dim(high_rows, mp_at * head_cols, head_cols, 2)
    own_hidden = lax.dynamic_slice_in_dim(hidden1[per_section:], mp_at * head_cols, head_cols, 2)
    high_total = own_hidden.astype(jnp.float32) + own_high + sum(
        piece.astype(jnp.float32) for piece in to_high
    )
    final_cols = jnp.where(is_first, low_total, high_total).astype(jnp.bfloat16)
    return (key_store, value_store, final_cols)


def solution(mesh):
    sizes = dict(tm_n=mesh.shape["tm"], mp_n=mesh.shape["mp"], sec_n=mesh.shape["section"])
    in_specs = (
        P("groups", None, "tm"),
        P("groups"),
        P(None, ("mp", "section")),
        P("section", None),
        P("section", None, "mp"),
        P("section", None, "mp"),
        P("section", None, "mp"),
        P("section", "mp", None),
    )
    out_specs = (
        P("section", "groups", "mp", None, "tm"),
        P("section", "groups", "mp", None, "tm"),
        P(("groups", "section"), "tm", "mp"),
    )

    def body(*args):
        return per_device(*args, **sizes)

    return jax.shard_map(body, mesh=mesh, in_specs=in_specs, out_specs=out_specs, check_vma=False)
```
